32 devices in a mesh: grp: 2 (over x), stretch: 8 (over z, y), req: 2 (over core).
Axes of the slice: x: 2, y: 2, z: 4, core: 2. Of those that a mesh axis runs over, the one named last changes fastest.
Arguments:
- queries: bfloat16 [16, 256, 4096], P(('grp', 'stretch'), None, 'req'), parts along dimension 0, may hold values from -32 to 32
- fresh_keys: bfloat16 [16, 256, 512], P(('grp', 'stretch'), None, 'req'), parts along dimension 0, may hold values from -32 to 32
- fresh_values: bfloat16 [16, 256, 512], P(('grp', 'stretch'), None, 'req'), parts along dimension 0, may hold values from -6 to 6
- stored_stretch_keys: bfloat16 [256, 128, 512], P(('grp', 'stretch'), None, 'req'), parts along dimension 0, may hold values from -6 to 6
- stored_stretch_values: bfloat16 [256, 128, 512], P(('grp', 'stretch'), None, 'req'), parts along dimension 0, may hold values from -6 to 6
- scales: bfloat16 [256, 2, 4], P(('grp', 'stretch'), None, 'req'), parts along dimension 0, may hold values from 0.29 to 3.02
- stretch_ids: int32 [16, 32], P(('grp', 'stretch')), parts along dimension 0, may hold values from 0 to 127, as said below
- counts: int32 [16], P(('grp', 'stretch')), parts along dimension 0, may hold values from 24 to 32
- stretch_pos: int32 [16, 32], P(('grp', 'stretch')), parts along dimension 0, may hold values from 0 to 4095
Outputs:
- attended: bfloat16 [16, 256, 4096], P(('grp', 'stretch'), None, 'req'), parts along dimension 0
The draws below stay inside these ranges and needn't reach their ends.
There are 2 independent parts, one for each index of `grp`. The reference program is written for one: setup_inputs(seed, part) draws one part's arguments, and reference() takes and returns one part's arrays. A program takes and returns all parts, laid end to end along the dimension named above; each array names one. Nothing has to cross between parts.
Inputs may be any that keep to these rules, and one draw needn't show every extreme that they name: `stretch_ids`: the 32 stretch ids of a request are distinct; at most 8 of them lie on one owner (owner = id // 16); the first 8 of every request lie on one owner, the same for all requests of a group.
All inputs are finite; a program needn't handle non-finite values.
Results may differ from the reference program's by a relative error of at most 0.012.
Values may be sent and summed in bfloat16 or wider, within the bound.
No kernel may reach another device: no remote copies, remote signals or barrier semaphores. Data moves between devices by JAX's collectives and lax.ppermute only.
A program may use at most 64 MiB of HBM per device.

```python
import jax
import jax.numpy as jnp
from jax import lax

HEAD_SIZE = 128
QUERY_HEADS = 32
KEY_VALUE_HEADS = 4
STRETCH_TOKENS = 128
STRETCH_SLOTS = 32
NEW_TOKENS = 256
CH_DEV = 16
GROUP_REQUESTS = 8
STORE_STRETCHES = 128
CAP = 8


def slow_lanes():
    lane = jnp.arange(HEAD_SIZE, dtype=jnp.int32) % (HEAD_SIZE // 2)
    return (lane >= 7 * HEAD_SIZE // 16).astype(jnp.float32)


def slow_signs(key):
    flips = jax.random.bernoulli(jax.random.fold_in(key, 31), 0.5, (HEAD_SIZE,))
    return jnp.where(flips, 1.0, -1.0).astype(jnp.float32) * slow_lanes()


def stretch_scales(key):
    spread = jax.random.uniform(jax.random.fold_in(key, 23), (STORE_STRETCHES, 2, KEY_VALUE_HEADS), jnp.float32, jnp.log(0.3), jnp.log(3.0))
    return jnp.exp(spread).astype(jnp.bfloat16)


def aligned_pair(key):
    base = jax.random.fold_in(key, 11)
    key_query, random_key_for_keys = jax.random.split(base, 2)
    steps = jnp.arange(NEW_TOKENS, dtype=jnp.int32)
    sampled_queries = jnp.clip(jax.random.normal(key_query, (GROUP_REQUESTS, NEW_TOKENS, QUERY_HEADS, HEAD_SIZE), jnp.float32), -6.0, 6.0)
    sampled_keys = jnp.clip(jax.random.normal(random_key_for_keys, (GROUP_REQUESTS, NEW_TOKENS, KEY_VALUE_HEADS, HEAD_SIZE), jnp.float32), -6.0, 6.0)
    seeker = steps % 16 == 7
    slow = slow_lanes()
    signs = slow_signs(key)
    sought = seeker[None, :, None, None] & (slow[None, None, None, :] > 0.0)
    sampled_queries = jnp.where(sought, 16.0 * signs[None, None, None, :], sampled_queries)
    return (sampled_queries.reshape(GROUP_REQUESTS, NEW_TOKENS, QUERY_HEADS * HEAD_SIZE), sampled_keys.reshape(GROUP_REQUESTS, NEW_TOKENS, KEY_VALUE_HEADS * HEAD_SIZE))


def draw_queries(key, part):
    return aligned_pair(key)[0].astype(jnp.bfloat16)


def draw_fresh_keys(key, part):
    return aligned_pair(key)[1].astype(jnp.bfloat16)


def draw_scales(key, part):
    return stretch_scales(key)


def draw_stored_stretch_keys(key, part):
    base = jax.random.fold_in(key, 41)
    key_noise, key_pick = jax.random.split(base, 2)
    shape = (STORE_STRETCHES, STRETCH_TOKENS, KEY_VALUE_HEADS, HEAD_SIZE)
    noise = jnp.clip(jax.random.normal(key_noise, shape, jnp.float32), -6.0, 6.0)
    slow = slow_lanes()
    signs = slow_signs(key)
    noise = noise * (1.0 - 0.75 * slow)
    key_scale = stretch_scales(key)[:, 0, :].astype(jnp.float32)
    inverse = 1.0 / key_scale
    planted = jnp.where(slow > 0.0, 1.8 * signs, 0.5 * noise) * inverse[:, None, :, None]
    planted = jnp.clip(planted, -6.0, 6.0)
    pick = jax.random.randint(key_pick, (STORE_STRETCHES, KEY_VALUE_HEADS), 0, STRETCH_TOKENS)
    planted_row = jnp.arange(STRETCH_TOKENS, dtype=jnp.int32)[None, :, None] == pick[:, None, :]
    result = jnp.where(planted_row[..., None], planted, noise)
    return result.reshape(STORE_STRETCHES, STRETCH_TOKENS, KEY_VALUE_HEADS * HEAD_SIZE).astype(jnp.bfloat16)


def draw_stretch_ids(key, part):
    base = jax.random.fold_in(key, 5)
    key_hot, key_tilt, key_noise, key_local, key_order = jax.random.split(base, 5)
    owners = STORE_STRETCHES // CH_DEV
    used = STRETCH_SLOTS // CAP
    hottest = jax.random.randint(key_hot, (), 0, owners)
    tilt = jax.random.randint(key_tilt, (owners,), 0, owners)
    noise = jax.random.randint(key_noise, (GROUP_REQUESTS, owners), 0, 2 * owners)
    member = jnp.arange(owners, dtype=jnp.int32)
    score = (noise + tilt[None, :]) * owners + member[None, :]
    score = jnp.where(member[None, :] == hottest, score + 8 * owners * owners, score)
    picked = lax.top_k(score, used)[1].astype(jnp.int32)
    local_keys = jax.random.split(key_local, GROUP_REQUESTS * used)
    local_ids = jax.vmap(lambda single: jax.random.permutation(single, CH_DEV)[:CAP])(local_keys)
    local_ids = local_ids.reshape(GROUP_REQUESTS, STRETCH_SLOTS).astype(jnp.int32)
    slot_stretch_ids = jnp.repeat(picked, CAP, axis=1) * CH_DEV + local_ids
    order_keys = jax.random.split(key_order, GROUP_REQUESTS)
    tails = jax.vmap(lambda single: jax.random.permutation(single, STRETCH_SLOTS - CAP))(order_keys).astype(jnp.int32) + CAP
    heads = jnp.broadcast_to(jnp.arange(CAP, dtype=jnp.int32)[None, :], (GROUP_REQUESTS, CAP))
    order = jnp.concatenate([heads, tails], axis=1)
    return jnp.take_along_axis(slot_stretch_ids, order, axis=1).astype(jnp.int32)


def set_ends(entries, key, least, top_value):
    index_at = [jax.random.randint(jax.random.fold_in(key, axis), (), 0, length) for axis, length in enumerate(entries.shape)]
    main_axis = entries.shape.index(max(entries.shape))
    next_to = index_at[:main_axis] + [(index_at[main_axis] + 1) % entries.shape[main_axis]] + index_at[main_axis + 1:]
    return entries.at[tuple(index_at)].set(least).at[tuple(next_to)].set(top_value)


def level_of(key, shape, shards, least, top_value):
    def one(axis_at, shards_of):
        draws = jax.random.uniform(jax.random.fold_in(jax.random.fold_in(key, 6), axis_at), (shards_of,), jnp.float32, least / len(shards), top_value / len(shards))
        return jnp.repeat(jnp.exp(draws), shape[axis_at] // shards_of).reshape((-1,) + (1,) * (len(shape) - axis_at - 1))

    loudness = one(*shards[0])
    for cut in shards[1:]:
        loudness = loudness * one(*cut)
    return loudness


def normal_values(key, shape, deviation, most, shards=(), held_as=jnp.bfloat16):
    values = deviation * jax.random.normal(key, shape, jnp.float32)
    if shards:
        values = values * level_of(key, shape, shards, -0.22, 0.18)
    return jnp.clip(values, -most, most).astype(held_as)


def setup_inputs(seed: int = 0, part: int = 0) -> dict:
    seeds = jax.random.split(jax.random.key(seed), 10)
    own_keys = jax.random.split(jax.random.fold_in(seeds[9], part), 10)
    return {
        "queries": draw_queries(jax.random.fold_in(jax.random.fold_in(seeds[9], part), 71), part),
        "fresh_keys": draw_fresh_keys(jax.random.fold_in(jax.random.fold_in(seeds[9], part), 71), part),
        "fresh_values": normal_values(own_keys[2], (GROUP_REQUESTS, NEW_TOKENS, KEY_VALUE_HEADS * HEAD_SIZE), 1.0, 6.0, ((0, 8), (2, 2))),
        "stored_stretch_keys": draw_stored_stretch_keys(jax.random.fold_in(jax.random.fold_in(seeds[9], part), 71), part),
        "stored_stretch_values": normal_values(own_keys[4], (STORE_STRETCHES, STRETCH_TOKENS, KEY_VALUE_HEADS * HEAD_SIZE), 1.0, 6.0, ((0, 8), (2, 2))),
        "scales": draw_scales(jax.random.fold_in(jax.random.fold_in(seeds[9], part), 71), part),
        "stretch_ids": draw_stretch_ids(jax.random.fold_in(jax.random.fold_in(seeds[9], part), 71), part),
        "counts": set_ends(jax.random.randint(own_keys[7], (GROUP_REQUESTS,), 3 * STRETCH_SLOTS // 4, STRETCH_SLOTS + 1), jax.random.fold_in(own_keys[7], 1), 3 * STRETCH_SLOTS // 4, STRETCH_SLOTS).astype(jnp.int32),
        "stretch_pos": set_ends(jax.random.randint(own_keys[8], (GROUP_REQUESTS, STRETCH_SLOTS), 0, STRETCH_SLOTS * STRETCH_TOKENS), jax.random.fold_in(own_keys[8], 1), 0, (STRETCH_SLOTS * STRETCH_TOKENS) - 1).astype(jnp.int32),
    }


rope_base = 500000.0


def apply_rotary(x, pos):
    half = x.shape[-1] // 2
    inv = rope_base ** (-(jnp.arange(half, dtype=jnp.float32) * 2.0 / x.shape[-1]))
    angle = pos.astype(jnp.float32)[..., None] * inv
    cosine = jnp.cos(angle)
    sine = jnp.sin(angle)
    first = x[..., :half]
    second = x[..., half:]
    return jnp.concatenate([first * cosine - second * sine, second * cosine + first * sine], axis=-1)


def reference(queries, fresh_keys, fresh_values, stored_stretch_keys, stored_stretch_values, scales, stretch_ids, counts, stretch_pos):
    request_group = QUERY_HEADS // KEY_VALUE_HEADS
    cache_length = STRETCH_SLOTS * STRETCH_TOKENS

    def single(request_index):
        slot_stretch_ids = stretch_ids[request_index]
        scale_factor = scales[slot_stretch_ids].astype(jnp.float32)
        random_key_stored = stored_stretch_keys[slot_stretch_ids].reshape(STRETCH_SLOTS, STRETCH_TOKENS, KEY_VALUE_HEADS, HEAD_SIZE).astype(jnp.float32) * scale_factor[:, 0][:, None, :, None]
        random_key_values = stored_stretch_values[slot_stretch_ids].reshape(STRETCH_SLOTS, STRETCH_TOKENS, KEY_VALUE_HEADS, HEAD_SIZE).astype(jnp.float32) * scale_factor[:, 1][:, None, :, None]
        stretch_placement = (stretch_pos[request_index][:, None] + jnp.arange(STRETCH_TOKENS, dtype=jnp.int32)[None, :])[:, :, None]
        key_cache_rows = apply_rotary(random_key_stored, stretch_placement).astype(jnp.bfloat16).reshape(cache_length, KEY_VALUE_HEADS, HEAD_SIZE)
        value_cache_rows = random_key_values.astype(jnp.bfloat16).reshape(cache_length, KEY_VALUE_HEADS, HEAD_SIZE)
        token_positions = (cache_length + jnp.arange(NEW_TOKENS, dtype=jnp.int32))[:, None]
        random_key_new = apply_rotary(fresh_keys[request_index].reshape(NEW_TOKENS, KEY_VALUE_HEADS, HEAD_SIZE).astype(jnp.float32), token_positions).astype(jnp.bfloat16)
        random_key_queries = (apply_rotary(queries[request_index].reshape(NEW_TOKENS, QUERY_HEADS, HEAD_SIZE).astype(jnp.float32), token_positions) * HEAD_SIZE ** -0.5).astype(jnp.bfloat16)
        key_cache_rows, value_cache_rows, random_key_new, random_key_queries = lax.optimization_barrier((key_cache_rows, value_cache_rows, random_key_new, random_key_queries))
        keys_all = jnp.concatenate([key_cache_rows, random_key_new], axis=0).astype(jnp.float32)
        combined_values = jnp.concatenate([value_cache_rows, fresh_values[request_index].reshape(NEW_TOKENS, KEY_VALUE_HEADS, HEAD_SIZE)], axis=0).astype(jnp.float32)
        grouped_queries = random_key_queries.reshape(NEW_TOKENS, KEY_VALUE_HEADS, request_group, HEAD_SIZE).astype(jnp.float32)
        scores = jnp.einsum('tkgd,lkd->ktgl', grouped_queries, keys_all)
        cache_ok = jnp.arange(cache_length, dtype=jnp.int32) // STRETCH_TOKENS < counts[request_index]
        own_ok = jnp.arange(NEW_TOKENS, dtype=jnp.int32)[None, :] <= jnp.arange(NEW_TOKENS, dtype=jnp.int32)[:, None]
        visible = jnp.concatenate([jnp.broadcast_to(cache_ok[None, :], (NEW_TOKENS, cache_length)), own_ok], axis=1)
        visible = visible[None, :, None, :]
        top = jnp.max(jnp.where(visible, scores, -1e30), axis=-1, keepdims=True)
        prob = jnp.where(visible, jnp.exp(scores - top), 0.0)
        total = jnp.sum(prob, axis=-1)
        rounded = lax.optimization_barrier(prob.astype(jnp.bfloat16))
        mixed = jnp.einsum('ktgl,lkd->tkgd', rounded.astype(jnp.float32), combined_values)
        result = mixed / jnp.transpose(total, (1, 0, 2))[..., None]
        return result.reshape(NEW_TOKENS, QUERY_HEADS * HEAD_SIZE).astype(jnp.bfloat16)

    return lax.map(single, jnp.arange(GROUP_REQUESTS, dtype=jnp.int32))
```

```python
import functools

import jax
import jax.numpy as jnp
from jax import lax
from jax.experimental import pallas as pl
from jax.experimental.pallas import tpu as pltpu
from jax.sharding import PartitionSpec as P

rope_base = 500000.0


def apply_rotary(x, pos):
    half = x.shape[-1] // 2
    inv = rope_base ** (-(jnp.arange(half, dtype=jnp.float32) * 2.0 / x.shape[-1]))
    angle = pos.astype(jnp.float32)[..., None] * inv
    cosine = jnp.cos(angle)
    sine = jnp.sin(angle)
    first = x[..., :half]
    second = x[..., half:]
    return jnp.concatenate(
        [first * cosine - second * sine, second * cosine + first * sine], axis=-1
    )


def slot_tables(slot_stretch_ids, counts, positions, owners, capacity, per_owner):
    rows, slots = slot_stretch_ids.shape
    owner = slot_stretch_ids // per_owner
    local = slot_stretch_ids % per_owner
    slot_iota = jnp.arange(slots, dtype=jnp.int32)
    live = slot_iota[None, :] < counts[:, None]
    same = owner[:, :, None] == owner[:, None, :]
    earlier = slot_iota[:, None] < slot_iota[None, :]
    rank = jnp.sum((same & earlier[None, :, :] & live[:, :, None]).astype(jnp.int32), axis=1)
    target = owner * capacity + rank
    hits = (
        target[:, :, None] == jnp.arange(owners * capacity, dtype=jnp.int32)[None, None, :]
    ) & live[:, :, None]
    hits = hits.astype(jnp.int32)
    local_table = jnp.sum(hits * (local + 1)[:, :, None], axis=1) - 1
    place_table = jnp.sum(hits * positions[:, :, None], axis=1)
    return (
        local_table.reshape(rows, owners, capacity),
        place_table.reshape(rows, owners, capacity),
        owner,
        rank,
        live,
    )


def shards(
    queries,
    fresh_keys,
    fresh_values,
    stored_stretch_keys,
    stored_stretch_values,
    scales,
    stretch_ids,
    counts,
    stretch_pos,
):
    owners = lax.axis_size("stretch")
    rows, slots = stretch_ids.shape
    per_owner, span, width = stored_stretch_keys.shape
    kv_heads = scales.shape[2]
    head_dim = width // kv_heads
    q_heads = queries.shape[2] // head_dim
    request_group = q_heads // kv_heads
    tokens = queries.shape[1]
    capacity = 2 * slots // owners
    mine = slot_tables(stretch_ids, counts, stretch_pos, owners, capacity, per_owner)
    owner, rank, live = (mine[2], mine[3], mine[4])
    wanted, starts = (
        lax.all_to_all(
            jnp.transpose(mine[0], (1, 0, 2)), "stretch", split_axis=0, concat_axis=0, tiled=True
        ),
        lax.all_to_all(
            jnp.transpose(mine[1], (1, 0, 2)), "stretch", split_axis=0, concat_axis=0, tiled=True
        ),
    )
    chosen = jnp.maximum(wanted, 0)
    raw_keys = stored_stretch_keys[chosen]
    raw_values = stored_stretch_values[chosen]
    flat = owners * rows * capacity
    index = (owner * rows + jnp.arange(rows, dtype=jnp.int32)[:, None]) * capacity + rank
    index = jnp.where(live, index, 0)
    stretch_iota = jnp.arange(span, dtype=jnp.int32)
    got_keys, got_vals, got_scales = (
        lax.all_to_all(raw_keys, "stretch", split_axis=0, concat_axis=0, tiled=True),
        lax.all_to_all(raw_values, "stretch", split_axis=0, concat_axis=0, tiled=True),
        lax.all_to_all(scales[chosen], "stretch", split_axis=0, concat_axis=0, tiled=True),
    )
    scale_factor = got_scales.reshape(flat, 2, kv_heads)[index].astype(jnp.float32)
    keys_wide = (
        got_keys.reshape(flat, span, width)[index]
        .reshape(rows, slots, span, kv_heads, head_dim)
        .astype(jnp.float32)
    )
    keys_wide = keys_wide * scale_factor[:, :, 0][:, :, None, :, None]
    stretch_placement = (stretch_pos[:, :, None] + stretch_iota)[..., None]
    cached_keys = (
        apply_rotary(keys_wide, stretch_placement)
        .astype(jnp.bfloat16)
        .reshape(rows, slots, span, width)
    )
    vals_wide = (
        got_vals.reshape(flat, span, width)[index]
        .reshape(rows, slots, span, kv_heads, head_dim)
        .astype(jnp.float32)
    )
    cached_vals = (
        (vals_wide * scale_factor[:, :, 1][:, :, None, :, None])
        .astype(jnp.bfloat16)
        .reshape(rows, slots, span, width)
    )
    cache_length = slots * span
    token_iota = jnp.arange(tokens, dtype=jnp.int32)
    token_positions = (cache_length + token_iota)[:, None]
    new_keys = apply_rotary(
        fresh_keys.reshape(rows, tokens, kv_heads, head_dim).astype(jnp.float32),
        token_positions,
    ).astype(jnp.bfloat16)
    keys_all = jnp.concatenate(
        [cached_keys.reshape(rows, cache_length, width), new_keys.reshape(rows, tokens, width)],
        axis=1,
    )
    values_all = jnp.concatenate(
        [cached_vals.reshape(rows, cache_length, width), fresh_values], axis=1
    )
    query_rot = (
        apply_rotary(
            queries.reshape(rows, tokens, q_heads, head_dim).astype(jnp.float32), token_positions
        )
        * head_dim ** (-0.5)
    ).astype(jnp.bfloat16)
    query_rot = query_rot.reshape(rows, tokens, q_heads * head_dim)
    return flash(query_rot, keys_all, values_all, counts * span, request_group, cache_length)


def flash_kernel(live_ref, q_ref, k_ref, v_ref, o_ref, m_sc, l_sc, acc_sc, *, cache_length, chunk):
    tokens = q_ref.shape[0]
    live = live_ref[pl.program_id(0)]
    q = q_ref[...]
    m_sc[...] = jnp.full(m_sc.shape, -1e30, jnp.float32)
    l_sc[...] = jnp.zeros(l_sc.shape, jnp.float32)
    acc_sc[...] = jnp.zeros(acc_sc.shape, jnp.float32)

    def step(first, size, causal):
        k = k_ref[pl.ds(first, size), :]
        v = v_ref[pl.ds(first, size), :]
        s = lax.dot_general(q, k, (((1,), (1,)), ((), ())), preferred_element_type=jnp.float32)
        col = lax.broadcasted_iota(jnp.int32, s.shape, 1)
        if causal:
            visible = col <= lax.broadcasted_iota(jnp.int32, s.shape, 0)
        else:
            visible = first + col < live
        s = jnp.where(visible, s, -1e30)
        m_old = m_sc[...]
        m_new = jnp.maximum(m_old, jnp.max(s, axis=1, keepdims=True))
        alpha = jnp.exp(m_old - m_new)
        p = jnp.where(visible, jnp.exp(s - m_new), 0.0)
        l_sc[...] = alpha * l_sc[...] + jnp.sum(p, axis=1, keepdims=True)
        acc_sc[...] = alpha * acc_sc[...] + lax.dot_general(
            p.astype(jnp.bfloat16), v, (((1,), (0,)), ((), ())), preferred_element_type=jnp.float32
        )
        m_sc[...] = m_new

    for index in range(cache_length // chunk):

        @pl.when(index * chunk < live)
        def _():
            step(index * chunk, chunk, False)

    step(cache_length, tokens, True)
    o_ref[...] = (acc_sc[...] / l_sc[...]).astype(o_ref.dtype)


def flash(query_rot, keys_all, values_all, live, request_group, cache_length):
    rows, tokens, q_width = query_rot.shape
    length, width = keys_all.shape[1:]
    head_dim = 128
    q_heads = q_width // head_dim
    kv_heads = width // head_dim
    chunk = 512 if cache_length % 512 == 0 else 128
    kernel = functools.partial(flash_kernel, cache_length=cache_length, chunk=chunk)
    return pl.pallas_call(
        kernel,
        grid_spec=pltpu.PrefetchScalarGridSpec(
            num_scalar_prefetch=1,
            grid=(rows, kv_heads, request_group),
            in_specs=[
                pl.BlockSpec((None, tokens, head_dim), lambda r, h, g, lv: (r, 0, h * request_group + g)),
                pl.BlockSpec((None, length, head_dim), lambda r, h, g, lv: (r, 0, h)),
                pl.BlockSpec((None, length, head_dim), lambda r, h, g, lv: (r, 0, h)),
            ],
            out_specs=pl.BlockSpec(
                (None, tokens, head_dim), lambda r, h, g, lv: (r, 0, h * request_group + g)
            ),
            scratch_shapes=[
                pltpu.VMEM((tokens, 1), jnp.float32),
                pltpu.VMEM((tokens, 1), jnp.float32),
                pltpu.VMEM((tokens, head_dim), jnp.float32),
            ],
        ),
        out_shape=jax.ShapeDtypeStruct((rows, tokens, q_width), jnp.bfloat16),
    )(live, query_rot, keys_all, values_all)


def solution(mesh):
    return jax.shard_map(
        shards,
        mesh=mesh,
        in_specs=(
            P(("grp", "stretch"), None, "req"),
            P(("grp", "stretch"), None, "req"),
            P(("grp", "stretch"), None, "req"),
            P(("grp", "stretch"), None, "req"),
            P(("grp", "stretch"), None, "req"),
            P(("grp", "stretch"), None, "req"),
            P(("grp", "stretch"), None),
            P(("grp", "stretch")),
            P(("grp", "stretch"), None),
        ),
        out_specs=P(("grp", "stretch"), None, "req"),
        check_vma=False,
    )
```

```python
import functools

import jax
import jax.numpy as jnp
from jax import lax
from jax.experimental import pallas as pl
from jax.experimental.pallas import tpu as pltpu
from jax.sharding import PartitionSpec as P

rope_base = 500000.0


def apply_rotary(x, pos):
    half = x.shape[-1] // 2
    inv = rope_base ** (-(jnp.arange(half, dtype=jnp.float32) * 2.0 / x.shape[-1]))
    angle = pos.astype(jnp.float32)[..., None] * inv
    cosine = jnp.cos(angle)
    sine = jnp.sin(angle)
    first = x[..., :half]
    second = x[..., half:]
    return jnp.concatenate(
        [first * cosine - second * sine, second * cosine + first * sine], axis=-1
    )


def slot_tables(slot_stretch_ids, counts, positions, owners, capacity, per_owner):
    rows, slots = slot_stretch_ids.shape
    owner = slot_stretch_ids // per_owner
    local = slot_stretch_ids % per_owner
    slot_iota = jnp.arange(slots, dtype=jnp.int32)
    live = slot_iota[None, :] < counts[:, None]
    same = owner[:, :, None] == owner[:, None, :]
    earlier = slot_iota[:, None] < slot_iota[None, :]
    rank = jnp.sum((same & earlier[None, :, :] & live[:, :, None]).astype(jnp.int32), axis=1)
    target = owner * capacity + rank
    hits = (
        target[:, :, None] == jnp.arange(owners * capacity, dtype=jnp.int32)[None, None, :]
    ) & live[:, :, None]
    hits = hits.astype(jnp.int32)
    local_table = jnp.sum(hits * (local + 1)[:, :, None], axis=1) - 1
    place_table = jnp.sum(hits * positions[:, :, None], axis=1)
    return (
        local_table.reshape(rows, owners, capacity),
        place_table.reshape(rows, owners, capacity),
        owner,
        rank,
        live,
    )


def shards(
    queries,
    fresh_keys,
    fresh_values,
    stored_stretch_keys,
    stored_stretch_values,
    scales,
    stretch_ids,
    counts,
    stretch_pos,
):
    owners = lax.axis_size("stretch")
    rows, slots = stretch_ids.shape
    per_owner, span, width = stored_stretch_keys.shape
    kv_heads = scales.shape[2]
    head_dim = width // kv_heads
    q_heads = queries.shape[2] // head_dim
    request_group = q_heads // kv_heads
    tokens = queries.shape[1]
    capacity = 2 * slots // owners
    mine = slot_tables(stretch_ids, counts, stretch_pos, owners, capacity, per_owner)
    owner, rank, live = (mine[2], mine[3], mine[4])
    wanted, starts = (
        lax.all_to_all(
            jnp.transpose(mine[0], (1, 0, 2)), "stretch", split_axis=0, concat_axis=0, tiled=True
        ),
        lax.all_to_all(
            jnp.transpose(mine[1], (1, 0, 2)), "stretch", split_axis=0, concat_axis=0, tiled=True
        ),
    )
    chosen = jnp.maximum(wanted, 0)
    raw_keys = stored_stretch_keys[chosen]
    raw_values = stored_stretch_values[chosen]
    flat = owners * rows * capacity
    index = (owner * rows + jnp.arange(rows, dtype=jnp.int32)[:, None]) * capacity + rank
    index = jnp.where(live, index, 0)
    stretch_iota = jnp.arange(span, dtype=jnp.int32)
    got_keys, got_vals, got_scales = (
        lax.all_to_all(raw_keys, "stretch", split_axis=0, concat_axis=0, tiled=True),
        lax.all_to_all(raw_values, "stretch", split_axis=0, concat_axis=0, tiled=True),
        lax.all_to_all(scales[chosen], "stretch", split_axis=0, concat_axis=0, tiled=True),
    )
    scale_factor = got_scales.reshape(flat, 2, kv_heads)[index].astype(jnp.float32)
    keys_wide = (
        got_keys.reshape(flat, span, width)[index]
        .reshape(rows, slots, span, kv_heads, head_dim)
        .astype(jnp.float32)
    )
    keys_wide = keys_wide * scale_factor[:, :, 0][:, :, None, :, None]
    stretch_placement = (stretch_pos[:, :, None] + stretch_iota)[..., None]
    cached_keys = (
        apply_rotary(keys_wide, stretch_placement)
        .astype(jnp.bfloat16)
        .reshape(rows, slots, span, width)
    )
    vals_wide = (
        got_vals.reshape(flat, span, width)[index]
        .reshape(rows, slots, span, kv_heads, head_dim)
        .astype(jnp.float32)
    )
    cached_vals = (
        (vals_wide * scale_factor[:, :, 1][:, :, None, :, None])
        .astype(jnp.bfloat16)
        .reshape(rows, slots, span, width)
    )
    cache_length = slots * span
    token_iota = jnp.arange(tokens, dtype=jnp.int32)
    token_positions = (cache_length + token_iota)[:, None]
    new_keys = apply_rotary(
        fresh_keys.reshape(rows, tokens, kv_heads, head_dim).astype(jnp.float32),
        token_positions,
    ).astype(jnp.bfloat16)
    keys_all = jnp.concatenate(
        [cached_keys.reshape(rows, cache_length, width), new_keys.reshape(rows, tokens, width)],
        axis=1,
    )
    values_all = jnp.concatenate(
        [cached_vals.reshape(rows, cache_length, width), fresh_values], axis=1
    )
    query_rot = (
        apply_rotary(
            queries.reshape(rows, tokens, q_heads, head_dim).astype(jnp.float32), token_positions
        )
        * head_dim ** (-0.5)
    ).astype(jnp.bfloat16)
    query_rot = query_rot.reshape(rows, tokens, q_heads * head_dim)
    return flash(query_rot, keys_all, values_all, counts * span, request_group, cache_length)


def flash_kernel(bias_ref, q_ref, k_ref, v_ref, o_ref, *, cache_length, chunk, heads):
    tokens = q_ref.shape[0]
    lanes = 128
    new_mask = lax.broadcasted_iota(jnp.int32, (tokens, tokens), 1) <= lax.broadcasted_iota(
        jnp.int32, (tokens, tokens), 0
    )

    def fold(acc, s, op):
        for b in range(s.shape[1] // lanes):
            acc = op(acc, s[:, b * lanes:(b + 1) * lanes])
        return acc

    for head in range(heads):
        q = q_ref[:, head * lanes:(head + 1) * lanes]

        def scores(first, size):
            return lax.dot_general(
                q, k_ref[:, first:first + size], (((1,), (0,)), ((), ())),
                preferred_element_type=jnp.float32,
            )

        def masked(first, size):
            return scores(first, size) + bias_ref[:, first:first + size]

        fresh = jnp.where(new_mask, scores(cache_length, tokens), -1e30)
        top = fold(jnp.full((tokens, lanes), -1e30, jnp.float32), fresh, jnp.maximum)
        for first in range(0, cache_length, chunk):
            top = fold(top, masked(first, chunk), jnp.maximum)
        top = jnp.max(top, axis=1, keepdims=True)

        def mix(s, first, size):
            p = jnp.exp(s - top)
            return p, lax.dot_general(
                p.astype(jnp.bfloat16), v_ref[first:first + size, :], (((1,), (0,)), ((), ())),
                preferred_element_type=jnp.float32,
            )

        p, acc = mix(fresh, cache_length, tokens)
        total = fold(jnp.zeros((tokens, lanes), jnp.float32), p, jnp.add)
        for first in range(0, cache_length, chunk):
            p, part = mix(masked(first, chunk), first, chunk)
            total = fold(total, p, jnp.add)
            acc = acc + part
        total = jnp.sum(total, axis=1, keepdims=True)
        o_ref[:, head * lanes:(head + 1) * lanes] = (acc / total).astype(o_ref.dtype)


CHUNK = 512
HEADS = 4


def flash(query_rot, keys_all, values_all, live, request_group, cache_length):
    rows, tokens, q_width = query_rot.shape
    length, width = keys_all.shape[1:]
    head_dim = 128
    kv_heads = width // head_dim
    chunk = CHUNK if cache_length % CHUNK == 0 else 128
    heads = HEADS
    keys_t = jnp.swapaxes(keys_all, 1, 2)
    bias = jnp.where(
        jnp.arange(cache_length, dtype=jnp.int32)[None, :] < live[:, None], 0.0, -1e30
    ).astype(jnp.float32)[:, None, :]
    kernel = functools.partial(flash_kernel, cache_length=cache_length, chunk=chunk, heads=heads)
    per = request_group // heads
    return pl.pallas_call(
        kernel,
        grid=(rows, kv_heads, per),
        in_specs=[
            pl.BlockSpec((None, 1, cache_length), lambda r, h, g: (r, 0, 0)),
            pl.BlockSpec((None, tokens, head_dim * heads), lambda r, h, g: (r, 0, h * per + g)),
            pl.BlockSpec((None, head_dim, length), lambda r, h, g: (r, h, 0)),
            pl.BlockSpec((None, length, head_dim), lambda r, h, g: (r, 0, h)),
        ],
        out_specs=pl.BlockSpec(
            (None, tokens, head_dim * heads), lambda r, h, g: (r, 0, h * per + g)
        ),
        out_shape=jax.ShapeDtypeStruct((rows, tokens, q_width), jnp.bfloat16),
    )(bias, query_rot, keys_t, values_all)


def solution(mesh):
    return jax.shard_map(
        shards,
        mesh=mesh,
        in_specs=(
            P(("grp", "stretch"), None, "req"),
            P(("grp", "stretch"), None, "req"),
            P(("grp", "stretch"), None, "req"),
            P(("grp", "stretch"), None, "req"),
            P(("grp", "stretch"), None, "req"),
            P(("grp", "stretch"), None, "req"),
            P(("grp", "stretch"), None),
            P(("grp", "stretch")),
            P(("grp", "stretch"), None),
        ),
        out_specs=P(("grp", "stretch"), None, "req"),
        check_vma=False,
    )
```

```python
import functools

import jax
import jax.numpy as jnp
from jax import lax
from jax.experimental import pallas as pl
from jax.experimental.pallas import tpu as pltpu
from jax.sharding import PartitionSpec as P

rope_base = 500000.0


def apply_rotary(x, pos):
    half = x.shape[-1] // 2
    inv = rope_base ** (-(jnp.arange(half, dtype=jnp.float32) * 2.0 / x.shape[-1]))
    angle = pos.astype(jnp.float32)[..., None] * inv
    cosine = jnp.cos(angle)
    sine = jnp.sin(angle)
    first = x[..., :half]
    second = x[..., half:]
    return jnp.concatenate(
        [first * cosine - second * sine, second * cosine + first * sine], axis=-1
    )


def slot_tables(slot_stretch_ids, counts, positions, owners, capacity, per_owner):
    rows, slots = slot_stretch_ids.shape
    owner = slot_stretch_ids // per_owner
    local = slot_stretch_ids % per_owner
    slot_iota = jnp.arange(slots, dtype=jnp.int32)
    live = slot_iota[None, :] < counts[:, None]
    same = owner[:, :, None] == owner[:, None, :]
    earlier = slot_iota[:, None] < slot_iota[None, :]
    rank = jnp.sum((same & earlier[None, :, :] & live[:, :, None]).astype(jnp.int32), axis=1)
    target = owner * capacity + rank
    hits = (
        target[:, :, None] == jnp.arange(owners * capacity, dtype=jnp.int32)[None, None, :]
    ) & live[:, :, None]
    hits = hits.astype(jnp.int32)
    local_table = jnp.sum(hits * (local + 1)[:, :, None], axis=1) - 1
    place_table = jnp.sum(hits * positions[:, :, None], axis=1)
    return (
        local_table.reshape(rows, owners, capacity),
        place_table.reshape(rows, owners, capacity),
        owner,
        rank,
        live,
    )


def shards(
    queries,
    fresh_keys,
    fresh_values,
    stored_stretch_keys,
    stored_stretch_values,
    scales,
    stretch_ids,
    counts,
    stretch_pos,
):
    owners = lax.axis_size("stretch")
    rows, slots = stretch_ids.shape
    per_owner, span, width = stored_stretch_keys.shape
    kv_heads = scales.shape[2]
    head_dim = width // kv_heads
    q_heads = queries.shape[2] // head_dim
    request_group = q_heads // kv_heads
    tokens = queries.shape[1]
    capacity = 2 * slots // owners
    cache_length = slots * span
    mine = slot_tables(stretch_ids, counts, stretch_pos, owners, capacity, per_owner)
    owner, rank, live = (mine[2], mine[3], mine[4])
    all_scales = lax.all_gather(scales, "stretch", axis=0, tiled=True)
    wanted = lax.all_to_all(
        jnp.transpose(mine[0], (1, 0, 2)), "stretch", split_axis=0, concat_axis=0, tiled=True
    )
    chosen = jnp.maximum(wanted, 0)
    raw_keys = stored_stretch_keys[chosen]
    raw_values = stored_stretch_values[chosen]
    flat = owners * rows * capacity
    index = (owner * rows + jnp.arange(rows, dtype=jnp.int32)[:, None]) * capacity + rank
    index = jnp.where(live, index, 0)
    slot_scale = all_scales[stretch_ids].astype(jnp.float32)
    placement = stretch_pos[:, :, None] + jnp.arange(span, dtype=jnp.int32)
    token_positions = cache_length + jnp.arange(tokens, dtype=jnp.int32)
    query_rot = (
        apply_rotary(
            queries.reshape(rows, tokens, q_heads, head_dim).astype(jnp.float32),
            token_positions[:, None],
        )
        * head_dim ** (-0.5)
    ).astype(jnp.bfloat16)
    query_rot = query_rot.reshape(rows, tokens, q_heads * head_dim)
    results = []
    for head in range(kv_heads):
        cols = slice(head * head_dim, (head + 1) * head_dim)
        sent = jnp.concatenate([raw_keys[..., cols], raw_values[..., cols]], axis=-1)
        got = lax.all_to_all(sent, "stretch", split_axis=0, concat_axis=0, tiled=True)
        if results:
            got, earlier = lax.optimization_barrier((got, results[-1]))
            results[-1] = earlier
        got = got.reshape(flat, span, 2 * head_dim)[index]
        keys = got[..., :head_dim].astype(jnp.float32) * slot_scale[:, :, 0, head][:, :, None, None]
        keys = apply_rotary(keys, placement).astype(jnp.bfloat16)
        vals = got[..., head_dim:].astype(jnp.float32) * slot_scale[:, :, 1, head][:, :, None, None]
        vals = vals.astype(jnp.bfloat16)
        new_keys = apply_rotary(
            fresh_keys[..., cols].astype(jnp.float32), token_positions
        ).astype(jnp.bfloat16)
        keys_all = jnp.concatenate(
            [keys.reshape(rows, cache_length, head_dim), new_keys], axis=1
        )
        values_all = jnp.concatenate(
            [vals.reshape(rows, cache_length, head_dim), fresh_values[..., cols]], axis=1
        )
        group_cols = slice(head * request_group * head_dim, (head + 1) * request_group * head_dim)
        results.append(
            flash(query_rot[..., group_cols], keys_all, values_all, counts * span, request_group, cache_length)
        )
    return jnp.concatenate(results, axis=-1)


def flash_kernel(bias_ref, q_ref, k_ref, v_ref, o_ref, *, cache_length, chunk, heads):
    tokens = q_ref.shape[0]
    lanes = 128
    new_mask = lax.broadcasted_iota(jnp.int32, (tokens, tokens), 1) <= lax.broadcasted_iota(
        jnp.int32, (tokens, tokens), 0
    )

    def fold(acc, s, op):
        for b in range(s.shape[1] // lanes):
            acc = op(acc, s[:, b * lanes:(b + 1) * lanes])
        return acc

    for head in range(heads):
        q = q_ref[:, head * lanes:(head + 1) * lanes]

        def scores(first, size):
            return lax.dot_general(
                q, k_ref[:, first:first + size], (((1,), (0,)), ((), ())),
                preferred_element_type=jnp.float32,
            )

        def masked(first, size):
            return scores(first, size) + bias_ref[:, first:first + size]

        fresh = jnp.where(new_mask, scores(cache_length, tokens), -1e30)
        top = fold(jnp.full((tokens, lanes), -1e30, jnp.float32), fresh, jnp.maximum)
        for first in range(0, cache_length, chunk):
            top = fold(top, masked(first, chunk), jnp.maximum)
        top = jnp.max(top, axis=1, keepdims=True)

        def mix(s, first, size):
            p = jnp.exp(s - top)
            return p, lax.dot_general(
                p.astype(jnp.bfloat16), v_ref[first:first + size, :], (((1,), (0,)), ((), ())),
                preferred_element_type=jnp.float32,
            )

        p, acc = mix(fresh, cache_length, tokens)
        total = fold(jnp.zeros((tokens, lanes), jnp.float32), p, jnp.add)
        for first in range(0, cache_length, chunk):
            p, part = mix(masked(first, chunk), first, chunk)
            total = fold(total, p, jnp.add)
            acc = acc + part
        total = jnp.sum(total, axis=1, keepdims=True)
        o_ref[:, head * lanes:(head + 1) * lanes] = (acc / total).astype(o_ref.dtype)


CHUNK = 512
HEADS = 4


def flash(query_rot, keys_all, values_all, live, request_group, cache_length):
    rows, tokens, q_width = query_rot.shape
    length, width = keys_all.shape[1:]
    head_dim = 128
    kv_heads = width // head_dim
    chunk = CHUNK if cache_length % CHUNK == 0 else 128
    heads = HEADS
    keys_t = jnp.swapaxes(keys_all, 1, 2)
    bias = jnp.where(
        jnp.arange(cache_length, dtype=jnp.int32)[None, :] < live[:, None], 0.0, -1e30
    ).astype(jnp.float32)[:, None, :]
    kernel = functools.partial(flash_kernel, cache_length=cache_length, chunk=chunk, heads=heads)
    per = request_group // heads
    return pl.pallas_call(
        kernel,
        grid=(rows, kv_heads, per),
        in_specs=[
            pl.BlockSpec((None, 1, cache_length), lambda r, h, g: (r, 0, 0)),
            pl.BlockSpec((None, tokens, head_dim * heads), lambda r, h, g: (r, 0, h * per + g)),
            pl.BlockSpec((None, head_dim, length), lambda r, h, g: (r, h, 0)),
            pl.BlockSpec((None, length, head_dim), lambda r, h, g: (r, 0, h)),
        ],
        out_specs=pl.BlockSpec(
            (None, tokens, head_dim * heads), lambda r, h, g: (r, 0, h * per + g)
        ),
        out_shape=jax.ShapeDtypeStruct((rows, tokens, q_width), jnp.bfloat16),
        cost_estimate=pl.CostEstimate(
            flops=6 * rows * tokens * q_width * length,
            transcendentals=rows * tokens * (q_width // head_dim) * length,
            bytes_accessed=2 * rows * (2 * tokens * q_width + 2 * length * width),
        ),
    )(bias, query_rot, keys_t, values_all)


def solution(mesh):
    return jax.shard_map(
        shards,
        mesh=mesh,
        in_specs=(
            P(("grp", "stretch"), None, "req"),
            P(("grp", "stretch"), None, "req"),
            P(("grp", "stretch"), None, "req"),
            P(("grp", "stretch"), None, "req"),
            P(("grp", "stretch"), None, "req"),
            P(("grp", "stretch"), None, "req"),
            P(("grp", "stretch"), None),
            P(("grp", "stretch")),
            P(("grp", "stretch"), None),
        ),
        out_specs=P(("grp", "stretch"), None, "req"),
        check_vma=False,
    )
```

```python
import functools

import jax
import jax.numpy as jnp
from jax import lax
from jax.experimental import pallas as pl
from jax.experimental.pallas import tpu as pltpu
from jax.sharding import PartitionSpec as P

rope_base = 500000.0


def apply_rotary(x, pos):
    half = x.shape[-1] // 2
    inv = rope_base ** (-(jnp.arange(half, dtype=jnp.float32) * 2.0 / x.shape[-1]))
    angle = pos.astype(jnp.float32)[..., None] * inv
    cosine = jnp.cos(angle)
    sine = jnp.sin(angle)
    first = x[..., :half]
    second = x[..., half:]
    return jnp.concatenate(
        [first * cosine - second * sine, second * cosine + first * sine], axis=-1
    )


def slot_tables(slot_stretch_ids, counts, positions, owners, capacity, per_owner):
    rows, slots = slot_stretch_ids.shape
    owner = slot_stretch_ids // per_owner
    local = slot_stretch_ids % per_owner
    slot_iota = jnp.arange(slots, dtype=jnp.int32)
    live = slot_iota[None, :] < counts[:, None]
    same = owner[:, :, None] == owner[:, None, :]
    earlier = slot_iota[:, None] < slot_iota[None, :]
    rank = jnp.sum((same & earlier[None, :, :] & live[:, :, None]).astype(jnp.int32), axis=1)
    target = owner * capacity + rank
    hits = (
        target[:, :, None] == jnp.arange(owners * capacity, dtype=jnp.int32)[None, None, :]
    ) & live[:, :, None]
    hits = hits.astype(jnp.int32)
    local_table = jnp.sum(hits * (local + 1)[:, :, None], axis=1) - 1
    place_table = jnp.sum(hits * positions[:, :, None], axis=1)
    return (
        local_table.reshape(rows, owners, capacity),
        place_table.reshape(rows, owners, capacity),
        owner,
        rank,
        live,
    )


def shards(
    queries,
    fresh_keys,
    fresh_values,
    stored_stretch_keys,
    stored_stretch_values,
    scales,
    stretch_ids,
    counts,
    stretch_pos,
):
    owners = lax.axis_size("stretch")
    rows, slots = stretch_ids.shape
    per_owner, span, width = stored_stretch_keys.shape
    kv_heads = scales.shape[2]
    head_dim = width // kv_heads
    q_heads = queries.shape[2] // head_dim
    request_group = q_heads // kv_heads
    tokens = queries.shape[1]
    capacity = 2 * slots // owners
    cache_length = slots * span
    mine = slot_tables(stretch_ids, counts, stretch_pos, owners, capacity, per_owner)
    owner, rank, live = (mine[2], mine[3], mine[4])
    all_scales = lax.all_gather(scales, "stretch", axis=0, tiled=True)
    all_scales, table = lax.optimization_barrier((all_scales, jnp.transpose(mine[0], (1, 0, 2))))
    wanted = lax.all_to_all(table, "stretch", split_axis=0, concat_axis=0, tiled=True)
    chosen = jnp.maximum(wanted, 0)
    raw_keys = stored_stretch_keys[chosen]
    raw_values = stored_stretch_values[chosen]
    flat = owners * rows * capacity
    index = (owner * rows + jnp.arange(rows, dtype=jnp.int32)[:, None]) * capacity + rank
    index = jnp.where(live, index, 0)
    slot_scale = all_scales[stretch_ids].astype(jnp.float32)
    placement = stretch_pos[:, :, None] + jnp.arange(span, dtype=jnp.int32)
    token_positions = cache_length + jnp.arange(tokens, dtype=jnp.int32)
    query_rot = (
        apply_rotary(
            queries.reshape(rows, tokens, q_heads, head_dim).astype(jnp.float32),
            token_positions[:, None],
        )
        * head_dim ** (-0.5)
    ).astype(jnp.bfloat16)
    query_rot = query_rot.reshape(rows, tokens, q_heads * head_dim)
    results = []
    for head in range(kv_heads):
        cols = slice(head * head_dim, (head + 1) * head_dim)
        sent = jnp.concatenate([raw_keys[..., cols], raw_values[..., cols]], axis=-1)
        got = lax.all_to_all(sent, "stretch", split_axis=0, concat_axis=0, tiled=True)
        if results:
            got, earlier = lax.optimization_barrier((got, results[-1]))
            results[-1] = earlier
        got = got.reshape(flat, span, 2 * head_dim)[index]
        keys = got[..., :head_dim].astype(jnp.float32) * slot_scale[:, :, 0, head][:, :, None, None]
        keys = apply_rotary(keys, placement).astype(jnp.bfloat16)
        vals = got[..., head_dim:].astype(jnp.float32) * slot_scale[:, :, 1, head][:, :, None, None]
        vals = vals.astype(jnp.bfloat16)
        new_keys = apply_rotary(
            fresh_keys[..., cols].astype(jnp.float32), token_positions
        ).astype(jnp.bfloat16)
        keys_all = jnp.concatenate(
            [keys.reshape(rows, cache_length, head_dim), new_keys], axis=1
        )
        values_all = jnp.concatenate(
            [vals.reshape(rows, cache_length, head_dim), fresh_values[..., cols]], axis=1
        )
        group_cols = slice(head * request_group * head_dim, (head + 1) * request_group * head_dim)
        results.append(
            flash(query_rot[..., group_cols], keys_all, values_all, counts * span, request_group, cache_length)
        )
    return jnp.concatenate(results, axis=-1)


def flash_kernel(bias_ref, q_ref, k_ref, v_ref, o_ref, *, cache_length, chunk, heads):
    tokens = q_ref.shape[0]
    lanes = 128
    new_mask = lax.broadcasted_iota(jnp.int32, (tokens, tokens), 1) <= lax.broadcasted_iota(
        jnp.int32, (tokens, tokens), 0
    )

    def fold(acc, s, op):
        for b in range(s.shape[1] // lanes):
            acc = op(acc, s[:, b * lanes:(b + 1) * lanes])
        return acc

    for head in range(heads):
        q = q_ref[:, head * lanes:(head + 1) * lanes]

        def scores(first, size):
            return lax.dot_general(
                q, k_ref[:, first:first + size], (((1,), (0,)), ((), ())),
                preferred_element_type=jnp.float32,
            )

        def masked(first, size):
            return scores(first, size) + bias_ref[:, first:first + size]

        fresh = jnp.where(new_mask, scores(cache_length, tokens), -1e30)
        top = fold(jnp.full((tokens, lanes), -1e30, jnp.float32), fresh, jnp.maximum)
        for first in range(0, cache_length, chunk):
            top = fold(top, masked(first, chunk), jnp.maximum)
        top = jnp.max(top, axis=1, keepdims=True)

        def mix(s, first, size):
            p = jnp.exp(s - top)
            return p, lax.dot_general(
                p.astype(jnp.bfloat16), v_ref[first:first + size, :], (((1,), (0,)), ((), ())),
                preferred_element_type=jnp.float32,
            )

        p, acc = mix(fresh, cache_length, tokens)
        total = fold(jnp.zeros((tokens, lanes), jnp.float32), p, jnp.add)
        for first in range(0, cache_length, chunk):
            p, part = mix(masked(first, chunk), first, chunk)
            total = fold(total, p, jnp.add)
            acc = acc + part
        total = jnp.sum(total, axis=1, keepdims=True)
        o_ref[:, head * lanes:(head + 1) * lanes] = (acc / total).astype(o_ref.dtype)


CHUNK = 512
HEADS = 4


def flash(query_rot, keys_all, values_all, live, request_group, cache_length):
    rows, tokens, q_width = query_rot.shape
    length, width = keys_all.shape[1:]
    head_dim = 128
    kv_heads = width // head_dim
    chunk = CHUNK if cache_length % CHUNK == 0 else 128
    heads = HEADS
    keys_t = jnp.swapaxes(keys_all, 1, 2)
    bias = jnp.where(
        jnp.arange(cache_length, dtype=jnp.int32)[None, :] < live[:, None], 0.0, -1e30
    ).astype(jnp.float32)[:, None, :]
    kernel = functools.partial(flash_kernel, cache_length=cache_length, chunk=chunk, heads=heads)
    per = request_group // heads
    return pl.pallas_call(
        kernel,
        grid=(rows, kv_heads, per),
        in_specs=[
            pl.BlockSpec((None, 1, cache_length), lambda r, h, g: (r, 0, 0)),
            pl.BlockSpec((None, tokens, head_dim * heads), lambda r, h, g: (r, 0, h * per + g)),
            pl.BlockSpec((None, head_dim, length), lambda r, h, g: (r, h, 0)),
            pl.BlockSpec((None, length, head_dim), lambda r, h, g: (r, 0, h)),
        ],
        out_specs=pl.BlockSpec(
            (None, tokens, head_dim * heads), lambda r, h, g: (r, 0, h * per + g)
        ),
        out_shape=jax.ShapeDtypeStruct((rows, tokens, q_width), jnp.bfloat16),
        cost_estimate=pl.CostEstimate(
            flops=6 * rows * tokens * q_width * length,
            transcendentals=rows * tokens * (q_width // head_dim) * length,
            bytes_accessed=2 * rows * (2 * tokens * q_width + 2 * length * width),
        ),
    )(bias, query_rot, keys_t, values_all)


def solution(mesh):
    return jax.shard_map(
        shards,
        mesh=mesh,
        in_specs=(
            P(("grp", "stretch"), None, "req"),
            P(("grp", "stretch"), None, "req"),
            P(("grp", "stretch"), None, "req"),
            P(("grp", "stretch"), None, "req"),
            P(("grp", "stretch"), None, "req"),
            P(("grp", "stretch"), None, "req"),
            P(("grp", "stretch"), None),
            P(("grp", "stretch")),
            P(("grp", "stretch"), None),
        ),
        out_specs=P(("grp", "stretch"), None, "req"),
        check_vma=False,
    )
```

```python
import functools

import jax
import jax.numpy as jnp
from jax import lax
from jax.experimental import pallas as pl
from jax.experimental.pallas import tpu as pltpu
from jax.sharding import PartitionSpec as P

rope_base = 500000.0


def apply_rotary(x, pos):
    half = x.shape[-1] // 2
    inv = rope_base ** (-(jnp.arange(half, dtype=jnp.float32) * 2.0 / x.shape[-1]))
    angle = pos.astype(jnp.float32)[..., None] * inv
    cosine = jnp.cos(angle)
    sine = jnp.sin(angle)
    first = x[..., :half]
    second = x[..., half:]
    return jnp.concatenate(
        [first * cosine - second * sine, second * cosine + first * sine], axis=-1
    )


def slot_tables(slot_stretch_ids, counts, positions, owners, capacity, per_owner):
    rows, slots = slot_stretch_ids.shape
    owner = slot_stretch_ids // per_owner
    local = slot_stretch_ids % per_owner
    slot_iota = jnp.arange(slots, dtype=jnp.int32)
    live = slot_iota[None, :] < counts[:, None]
    same = owner[:, :, None] == owner[:, None, :]
    earlier = slot_iota[:, None] < slot_iota[None, :]
    rank = jnp.sum((same & earlier[None, :, :] & live[:, :, None]).astype(jnp.int32), axis=1)
    target = owner * capacity + rank
    hits = (
        target[:, :, None] == jnp.arange(owners * capacity, dtype=jnp.int32)[None, None, :]
    ) & live[:, :, None]
    hits = hits.astype(jnp.int32)
    local_table = jnp.sum(hits * (local + 1)[:, :, None], axis=1) - 1
    place_table = jnp.sum(hits * positions[:, :, None], axis=1)
    return (
        local_table.reshape(rows, owners, capacity),
        place_table.reshape(rows, owners, capacity),
        owner,
        rank,
        live,
    )


def shards(
    queries,
    fresh_keys,
    fresh_values,
    stored_stretch_keys,
    stored_stretch_values,
    scales,
    stretch_ids,
    counts,
    stretch_pos,
):
    owners = lax.axis_size("stretch")
    rows, slots = stretch_ids.shape
    per_owner, span, width = stored_stretch_keys.shape
    kv_heads = scales.shape[2]
    head_dim = width // kv_heads
    q_heads = queries.shape[2] // head_dim
    request_group = q_heads // kv_heads
    tokens = queries.shape[1]
    capacity = 2 * slots // owners
    cache_length = slots * span
    mine = slot_tables(stretch_ids, counts, stretch_pos, owners, capacity, per_owner)
    owner, rank, live = (mine[2], mine[3], mine[4])
    scale_code = (scales.astype(jnp.float32) * 65536.0).astype(jnp.int32).reshape(1, 1, -1)
    requests = jnp.concatenate(
        [
            jnp.transpose(mine[0], (1, 0, 2)),
            jnp.broadcast_to(scale_code, (owners, rows, scale_code.shape[2])),
        ],
        axis=2,
    )
    answers = lax.all_to_all(requests, "stretch", split_axis=0, concat_axis=0, tiled=True)
    wanted = answers[:, :, :capacity]
    chosen = jnp.maximum(wanted, 0)
    all_scales = (answers[:, 0, capacity:].astype(jnp.float32) * (1.0 / 65536.0)).reshape(
        owners * per_owner, 2, scales.shape[2]
    )
    raw_keys = stored_stretch_keys[chosen]
    raw_values = stored_stretch_values[chosen]
    flat = owners * rows * capacity
    index = (owner * rows + jnp.arange(rows, dtype=jnp.int32)[:, None]) * capacity + rank
    index = jnp.where(live, index, 0)
    slot_scale = all_scales[stretch_ids]
    placement = stretch_pos[:, :, None] + jnp.arange(span, dtype=jnp.int32)
    token_positions = cache_length + jnp.arange(tokens, dtype=jnp.int32)
    query_rot = (
        apply_rotary(
            queries.reshape(rows, tokens, q_heads, head_dim).astype(jnp.float32),
            token_positions[:, None],
        )
        * head_dim ** (-0.5)
    ).astype(jnp.bfloat16)
    query_rot = query_rot.reshape(rows, tokens, q_heads * head_dim)
    results = []
    for head in range(kv_heads):
        cols = slice(head * head_dim, (head + 1) * head_dim)
        sent = jnp.concatenate([raw_keys[..., cols], raw_values[..., cols]], axis=-1)
        got = lax.all_to_all(sent, "stretch", split_axis=0, concat_axis=0, tiled=True)
        if results:
            got, earlier = lax.optimization_barrier((got, results[-1]))
            results[-1] = earlier
        got = got.reshape(flat, span, 2 * head_dim)[index]
        keys = got[..., :head_dim].astype(jnp.float32) * slot_scale[:, :, 0, head][:, :, None, None]
        keys = apply_rotary(keys, placement).astype(jnp.bfloat16)
        vals = got[..., head_dim:].astype(jnp.float32) * slot_scale[:, :, 1, head][:, :, None, None]
        vals = vals.astype(jnp.bfloat16)
        new_keys = apply_rotary(
            fresh_keys[..., cols].astype(jnp.float32), token_positions
        ).astype(jnp.bfloat16)
        keys_all = jnp.concatenate(
            [keys.reshape(rows, cache_length, head_dim), new_keys], axis=1
        )
        values_all = jnp.concatenate(
            [vals.reshape(rows, cache_length, head_dim), fresh_values[..., cols]], axis=1
        )
        group_cols = slice(head * request_group * head_dim, (head + 1) * request_group * head_dim)
        results.append(
            flash(query_rot[..., group_cols], keys_all, values_all, counts * span, request_group, cache_length)
        )
    return jnp.concatenate(results, axis=-1)


def flash_kernel(bias_ref, q_ref, k_ref, v_ref, o_ref, *, cache_length, chunk, heads):
    tokens = q_ref.shape[0]
    lanes = 128
    new_mask = lax.broadcasted_iota(jnp.int32, (tokens, tokens), 1) <= lax.broadcasted_iota(
        jnp.int32, (tokens, tokens), 0
    )

    def fold(acc, s, op):
        for b in range(s.shape[1] // lanes):
            acc = op(acc, s[:, b * lanes:(b + 1) * lanes])
        return acc

    for head in range(heads):
        q = q_ref[:, head * lanes:(head + 1) * lanes]

        def scores(first, size):
            return lax.dot_general(
                q, k_ref[:, first:first + size], (((1,), (0,)), ((), ())),
                preferred_element_type=jnp.float32,
            )

        def masked(first, size):
            return scores(first, size) + bias_ref[:, first:first + size]

        fresh = jnp.where(new_mask, scores(cache_length, tokens), -1e30)
        top = fold(jnp.full((tokens, lanes), -1e30, jnp.float32), fresh, jnp.maximum)
        for first in range(0, cache_length, chunk):
            top = fold(top, masked(first, chunk), jnp.maximum)
        top = jnp.max(top, axis=1, keepdims=True)

        def mix(s, first, size):
            p = jnp.exp(s - top)
            return p, lax.dot_general(
                p.astype(jnp.bfloat16), v_ref[first:first + size, :], (((1,), (0,)), ((), ())),
                preferred_element_type=jnp.float32,
            )

        p, acc = mix(fresh, cache_length, tokens)
        total = fold(jnp.zeros((tokens, lanes), jnp.float32), p, jnp.add)
        for first in range(0, cache_length, chunk):
            p, part = mix(masked(first, chunk), first, chunk)
            total = fold(total, p, jnp.add)
            acc = acc + part
        total = jnp.sum(total, axis=1, keepdims=True)
        o_ref[:, head * lanes:(head + 1) * lanes] = (acc / total).astype(o_ref.dtype)


CHUNK = 512
HEADS = 4


def flash(query_rot, keys_all, values_all, live, request_group, cache_length):
    rows, tokens, q_width = query_rot.shape
    length, width = keys_all.shape[1:]
    head_dim = 128
    kv_heads = width // head_dim
    chunk = CHUNK if cache_length % CHUNK == 0 else 128
    heads = HEADS
    keys_t = jnp.swapaxes(keys_all, 1, 2)
    bias = jnp.where(
        jnp.arange(cache_length, dtype=jnp.int32)[None, :] < live[:, None], 0.0, -1e30
    ).astype(jnp.float32)[:, None, :]
    kernel = functools.partial(flash_kernel, cache_length=cache_length, chunk=chunk, heads=heads)
    per = request_group // heads
    return pl.pallas_call(
        kernel,
        grid=(rows, kv_heads, per),
        in_specs=[
            pl.BlockSpec((None, 1, cache_length), lambda r, h, g: (r, 0, 0)),
            pl.BlockSpec((None, tokens, head_dim * heads), lambda r, h, g: (r, 0, h * per + g)),
            pl.BlockSpec((None, head_dim, length), lambda r, h, g: (r, h, 0)),
            pl.BlockSpec((None, length, head_dim), lambda r, h, g: (r, 0, h)),
        ],
        out_specs=pl.BlockSpec(
            (None, tokens, head_dim * heads), lambda r, h, g: (r, 0, h * per + g)
        ),
        out_shape=jax.ShapeDtypeStruct((rows, tokens, q_width), jnp.bfloat16),
        cost_estimate=pl.CostEstimate(
            flops=6 * rows * tokens * q_width * length,
            transcendentals=rows * tokens * (q_width // head_dim) * length,
            bytes_accessed=2 * rows * (2 * tokens * q_width + 2 * length * width),
        ),
    )(bias, query_rot, keys_t, values_all)


def solution(mesh):
    return jax.shard_map(
        shards,
        mesh=mesh,
        in_specs=(
            P(("grp", "stretch"), None, "req"),
            P(("grp", "stretch"), None, "req"),
            P(("grp", "stretch"), None, "req"),
            P(("grp", "stretch"), None, "req"),
            P(("grp", "stretch"), None, "req"),
            P(("grp", "stretch"), None, "req"),
            P(("grp", "stretch"), None),
            P(("grp", "stretch")),
            P(("grp", "stretch"), None),
        ),
        out_specs=P(("grp", "stretch"), None, "req"),
        check_vma=False,
    )
```

```python
import functools

import jax
import jax.numpy as jnp
from jax import lax
from jax.experimental import pallas as pl
from jax.experimental.pallas import tpu as pltpu
from jax.sharding import PartitionSpec as P

rope_base = 500000.0


def apply_rotary(x, pos):
    half = x.shape[-1] // 2
    inv = rope_base ** (-(jnp.arange(half, dtype=jnp.float32) * 2.0 / x.shape[-1]))
    angle = pos.astype(jnp.float32)[..., None] * inv
    cosine = jnp.cos(angle)
    sine = jnp.sin(angle)
    first = x[..., :half]
    second = x[..., half:]
    return jnp.concatenate(
        [first * cosine - second * sine, second * cosine + first * sine], axis=-1
    )


def slot_tables(slot_stretch_ids, counts, positions, owners, capacity, per_owner):
    rows, slots = slot_stretch_ids.shape
    owner = slot_stretch_ids // per_owner
    local = slot_stretch_ids % per_owner
    slot_iota = jnp.arange(slots, dtype=jnp.int32)
    live = slot_iota[None, :] < counts[:, None]
    same = owner[:, :, None] == owner[:, None, :]
    earlier = slot_iota[:, None] < slot_iota[None, :]
    rank = jnp.sum((same & earlier[None, :, :] & live[:, :, None]).astype(jnp.int32), axis=1)
    target = owner * capacity + rank
    hits = (
        target[:, :, None] == jnp.arange(owners * capacity, dtype=jnp.int32)[None, None, :]
    ) & live[:, :, None]
    hits = hits.astype(jnp.int32)
    local_table = jnp.sum(hits * (local + 1)[:, :, None], axis=1) - 1
    place_table = jnp.sum(hits * positions[:, :, None], axis=1)
    return (
        local_table.reshape(rows, owners, capacity),
        place_table.reshape(rows, owners, capacity),
        owner,
        rank,
        live,
    )


def shards(
    queries,
    fresh_keys,
    fresh_values,
    stored_stretch_keys,
    stored_stretch_values,
    scales,
    stretch_ids,
    counts,
    stretch_pos,
):
    owners = lax.axis_size("stretch")
    rows, slots = stretch_ids.shape
    per_owner, span, width = stored_stretch_keys.shape
    kv_heads = scales.shape[2]
    head_dim = width // kv_heads
    q_heads = queries.shape[2] // head_dim
    request_group = q_heads // kv_heads
    tokens = queries.shape[1]
    capacity = 2 * slots // owners
    cache_length = slots * span
    mine = slot_tables(stretch_ids, counts, stretch_pos, owners, capacity, per_owner)
    owner, rank, live = (mine[2], mine[3], mine[4])
    scale_code = (scales.astype(jnp.float32) * 65536.0).astype(jnp.int32).reshape(1, 1, -1)
    requests = jnp.concatenate(
        [
            jnp.transpose(mine[0], (1, 0, 2)),
            jnp.broadcast_to(scale_code, (owners, rows, scale_code.shape[2])),
        ],
        axis=2,
    )
    answers = lax.all_to_all(requests, "stretch", split_axis=0, concat_axis=0, tiled=True)
    wanted = answers[:, :, :capacity]
    chosen = jnp.maximum(wanted, 0)
    all_scales = (answers[:, 0, capacity:].astype(jnp.float32) * (1.0 / 65536.0)).reshape(
        owners * per_owner, 2, scales.shape[2]
    )
    store = jnp.stack(
        [
            jnp.concatenate(
                [
                    stored_stretch_keys[..., h * head_dim:(h + 1) * head_dim],
                    stored_stretch_values[..., h * head_dim:(h + 1) * head_dim],
                ],
                axis=-1,
            )
            for h in range(kv_heads)
        ],
        axis=0,
    )
    flat = owners * rows * capacity
    index = (owner * rows + jnp.arange(rows, dtype=jnp.int32)[:, None]) * capacity + rank
    index = jnp.where(live, index, 0)
    slot_scale = all_scales[stretch_ids]
    placement = stretch_pos[:, :, None] + jnp.arange(span, dtype=jnp.int32)
    token_positions = cache_length + jnp.arange(tokens, dtype=jnp.int32)
    query_rot = (
        apply_rotary(
            queries.reshape(rows, tokens, q_heads, head_dim).astype(jnp.float32),
            token_positions[:, None],
        )
        * head_dim ** (-0.5)
    ).astype(jnp.bfloat16)
    query_rot = query_rot.reshape(rows, tokens, q_heads * head_dim)
    results = []
    for head in range(kv_heads):
        cols = slice(head * head_dim, (head + 1) * head_dim)
        sent = store[head][chosen]
        got = lax.all_to_all(sent, "stretch", split_axis=0, concat_axis=0, tiled=True)
        if results:
            got, earlier = lax.optimization_barrier((got, results[-1]))
            results[-1] = earlier
        got = got.reshape(flat, span, 2 * head_dim)[index]
        keys = got[..., :head_dim].astype(jnp.float32) * slot_scale[:, :, 0, head][:, :, None, None]
        keys = apply_rotary(keys, placement).astype(jnp.bfloat16)
        vals = got[..., head_dim:].astype(jnp.float32) * slot_scale[:, :, 1, head][:, :, None, None]
        vals = vals.astype(jnp.bfloat16)
        new_keys = apply_rotary(
            fresh_keys[..., cols].astype(jnp.float32), token_positions
        ).astype(jnp.bfloat16)
        keys_all = jnp.concatenate(
            [keys.reshape(rows, cache_length, head_dim), new_keys], axis=1
        )
        values_all = jnp.concatenate(
            [vals.reshape(rows, cache_length, head_dim), fresh_values[..., cols]], axis=1
        )
        group_cols = slice(head * request_group * head_dim, (head + 1) * request_group * head_dim)
        results.append(
            flash(
                query_rot[..., group_cols], keys_all, values_all, counts * span, request_group,
                cache_length, head * request_group, results[-1] if results else None, queries.shape[2],
            )
        )
    return results[-1]


def flash_kernel(bias_ref, q_ref, k_ref, v_ref, *refs, cache_length, chunk, heads):
    o_ref = refs[-1]
    tokens = q_ref.shape[0]
    lanes = 128
    new_mask = lax.broadcasted_iota(jnp.int32, (tokens, tokens), 1) <= lax.broadcasted_iota(
        jnp.int32, (tokens, tokens), 0
    )

    def fold(acc, s, op):
        for b in range(s.shape[1] // lanes):
            acc = op(acc, s[:, b * lanes:(b + 1) * lanes])
        return acc

    for head in range(heads):
        q = q_ref[:, head * lanes:(head + 1) * lanes]

        def scores(first, size):
            return lax.dot_general(
                q, k_ref[:, first:first + size], (((1,), (0,)), ((), ())),
                preferred_element_type=jnp.float32,
            )

        def masked(first, size):
            return scores(first, size) + bias_ref[:, first:first + size]

        fresh = jnp.where(new_mask, scores(cache_length, tokens), -1e30)
        top = fold(jnp.full((tokens, lanes), -1e30, jnp.float32), fresh, jnp.maximum)
        for first in range(0, cache_length, chunk):
            top = fold(top, masked(first, chunk), jnp.maximum)
        top = jnp.max(top, axis=1, keepdims=True)

        def mix(s, first, size):
            p = jnp.exp(s - top)
            return p, lax.dot_general(
                p.astype(jnp.bfloat16), v_ref[first:first + size, :], (((1,), (0,)), ((), ())),
                preferred_element_type=jnp.float32,
            )

        p, acc = mix(fresh, cache_length, tokens)
        total = fold(jnp.zeros((tokens, lanes), jnp.float32), p, jnp.add)
        for first in range(0, cache_length, chunk):
            p, part = mix(masked(first, chunk), first, chunk)
            total = fold(total, p, jnp.add)
            acc = acc + part
        total = jnp.sum(total, axis=1, keepdims=True)
        o_ref[:, head * lanes:(head + 1) * lanes] = (acc / total).astype(o_ref.dtype)


CHUNK = 512
HEADS = 4


def flash(query_rot, keys_all, values_all, live, request_group, cache_length, offset, into, out_width):
    rows, tokens, q_width = query_rot.shape
    length, width = keys_all.shape[1:]
    head_dim = 128
    kv_heads = width // head_dim
    chunk = CHUNK if cache_length % CHUNK == 0 else 128
    heads = HEADS
    keys_t = jnp.swapaxes(keys_all, 1, 2)
    bias = jnp.where(
        jnp.arange(cache_length, dtype=jnp.int32)[None, :] < live[:, None], 0.0, -1e30
    ).astype(jnp.float32)[:, None, :]
    kernel = functools.partial(flash_kernel, cache_length=cache_length, chunk=chunk, heads=heads)
    per = request_group // heads
    block = offset // heads
    in_specs = [
        pl.BlockSpec((None, 1, cache_length), lambda r, h, g: (r, 0, 0)),
        pl.BlockSpec((None, tokens, head_dim * heads), lambda r, h, g: (r, 0, h * per + g)),
        pl.BlockSpec((None, head_dim, length), lambda r, h, g: (r, h, 0)),
        pl.BlockSpec((None, length, head_dim), lambda r, h, g: (r, 0, h)),
    ]
    operands = [bias, query_rot, keys_t, values_all]
    aliases = {}
    if into is not None:
        in_specs.append(pl.BlockSpec(memory_space=pl.ANY))
        operands.append(into)
        aliases = {4: 0}
    return pl.pallas_call(
        kernel,
        grid=(rows, kv_heads, per),
        in_specs=in_specs,
        out_specs=pl.BlockSpec(
            (None, tokens, head_dim * heads), lambda r, h, g: (r, 0, block + h * per + g)
        ),
        out_shape=jax.ShapeDtypeStruct((rows, tokens, out_width), jnp.bfloat16),
        input_output_aliases=aliases,
        cost_estimate=pl.CostEstimate(
            flops=6 * rows * tokens * q_width * length,
            transcendentals=rows * tokens * (q_width // head_dim) * length,
            bytes_accessed=2 * rows * (2 * tokens * q_width + 2 * length * width),
        ),
    )(*operands)


def solution(mesh):
    return jax.shard_map(
        shards,
        mesh=mesh,
        in_specs=(
            P(("grp", "stretch"), None, "req"),
            P(("grp", "stretch"), None, "req"),
            P(("grp", "stretch"), None, "req"),
            P(("grp", "stretch"), None, "req"),
            P(("grp", "stretch"), None, "req"),
            P(("grp", "stretch"), None, "req"),
            P(("grp", "stretch"), None),
            P(("grp", "stretch")),
            P(("grp", "stretch"), None),
        ),
        out_specs=P(("grp", "stretch"), None, "req"),
        check_vma=False,
    )
```

```python
import functools

import jax
import jax.numpy as jnp
from jax import lax
from jax.experimental import pallas as pl
from jax.experimental.pallas import tpu as pltpu
from jax.sharding import PartitionSpec as P

rope_base = 500000.0


def apply_rotary(x, pos):
    half = x.shape[-1] // 2
    inv = rope_base ** (-(jnp.arange(half, dtype=jnp.float32) * 2.0 / x.shape[-1]))
    angle = pos.astype(jnp.float32)[..., None] * inv
    cosine = jnp.cos(angle)
    sine = jnp.sin(angle)
    first = x[..., :half]
    second = x[..., half:]
    return jnp.concatenate(
        [first * cosine - second * sine, second * cosine + first * sine], axis=-1
    )


def slot_tables(slot_stretch_ids, counts, positions, owners, capacity, per_owner):
    rows, slots = slot_stretch_ids.shape
    owner = slot_stretch_ids // per_owner
    local = slot_stretch_ids % per_owner
    slot_iota = jnp.arange(slots, dtype=jnp.int32)
    live = slot_iota[None, :] < counts[:, None]
    same = owner[:, :, None] == owner[:, None, :]
    earlier = slot_iota[:, None] < slot_iota[None, :]
    rank = jnp.sum((same & earlier[None, :, :] & live[:, :, None]).astype(jnp.int32), axis=1)
    target = owner * capacity + rank
    hits = (
        target[:, :, None] == jnp.arange(owners * capacity, dtype=jnp.int32)[None, None, :]
    ) & live[:, :, None]
    hits = hits.astype(jnp.int32)
    local_table = jnp.sum(hits * (local + 1)[:, :, None], axis=1) - 1
    place_table = jnp.sum(hits * positions[:, :, None], axis=1)
    return (
        local_table.reshape(rows, owners, capacity),
        place_table.reshape(rows, owners, capacity),
        owner,
        rank,
        live,
    )


def shards(
    queries,
    fresh_keys,
    fresh_values,
    stored_stretch_keys,
    stored_stretch_values,
    scales,
    stretch_ids,
    counts,
    stretch_pos,
):
    owners = lax.axis_size("stretch")
    rows, slots = stretch_ids.shape
    per_owner, span, width = stored_stretch_keys.shape
    kv_heads = scales.shape[2]
    head_dim = width // kv_heads
    q_heads = queries.shape[2] // head_dim
    request_group = q_heads // kv_heads
    tokens = queries.shape[1]
    capacity = 2 * slots // owners
    cache_length = slots * span
    mine = slot_tables(stretch_ids, counts, stretch_pos, owners, capacity, per_owner)
    owner, rank, live = (mine[2], mine[3], mine[4])
    scale_code = (scales.astype(jnp.float32) * 65536.0).astype(jnp.int32).reshape(1, 1, -1)
    requests = jnp.concatenate(
        [
            jnp.transpose(mine[0], (1, 0, 2)),
            jnp.broadcast_to(scale_code, (owners, rows, scale_code.shape[2])),
        ],
        axis=2,
    )
    answers = lax.all_to_all(requests, "stretch", split_axis=0, concat_axis=0, tiled=True)
    wanted = answers[:, :, :capacity]
    chosen = jnp.maximum(wanted, 0)
    all_scales = (answers[:, 0, capacity:].astype(jnp.float32) * (1.0 / 65536.0)).reshape(
        owners * per_owner, 2, scales.shape[2]
    )
    store = jnp.stack(
        [
            jnp.concatenate(
                [
                    stored_stretch_keys[..., h * head_dim:(h + 1) * head_dim],
                    stored_stretch_values[..., h * head_dim:(h + 1) * head_dim],
                ],
                axis=-1,
            )
            for h in range(kv_heads)
        ],
        axis=0,
    )
    flat = owners * rows * capacity
    index = (owner * rows + jnp.arange(rows, dtype=jnp.int32)[:, None]) * capacity + rank
    index = jnp.where(live, index, 0)
    slot_scale = all_scales[stretch_ids]
    placement = stretch_pos[:, :, None] + jnp.arange(span, dtype=jnp.int32)
    token_positions = cache_length + jnp.arange(tokens, dtype=jnp.int32)
    query_rot = (
        apply_rotary(
            queries.reshape(rows, tokens, q_heads, head_dim).astype(jnp.float32),
            token_positions[:, None],
        )
        * head_dim ** (-0.5)
    ).astype(jnp.bfloat16)
    query_rot = query_rot.reshape(rows, tokens, q_heads * head_dim)
    results = []
    for head in range(kv_heads):
        cols = slice(head * head_dim, (head + 1) * head_dim)
        last = head == kv_heads - 1
        new_keys = apply_rotary(
            fresh_keys[..., cols].astype(jnp.float32), token_positions
        ).astype(jnp.bfloat16)
        group_cols = slice(head * request_group * head_dim, (head + 1) * request_group * head_dim)
        query_head = query_rot[..., group_cols]
        if last:
            got_keys = lax.all_to_all(
                store[head][chosen][..., :head_dim], "stretch", split_axis=0, concat_axis=0, tiled=True
            )
            if results:
                got_keys, earlier = lax.optimization_barrier((got_keys, results[-1]))
                results[-1] = earlier
            got_vals = lax.all_to_all(
                store[head][chosen][..., head_dim:], "stretch", split_axis=0, concat_axis=0, tiled=True
            )
            raw_k = got_keys.reshape(flat, span, head_dim)[index]
        else:
            got = lax.all_to_all(store[head][chosen], "stretch", split_axis=0, concat_axis=0, tiled=True)
            if results:
                got, earlier = lax.optimization_barrier((got, results[-1]))
                results[-1] = earlier
            got = got.reshape(flat, span, 2 * head_dim)[index]
            raw_k = got[..., :head_dim]
        keys = raw_k.astype(jnp.float32) * slot_scale[:, :, 0, head][:, :, None, None]
        keys = apply_rotary(keys, placement).astype(jnp.bfloat16)
        keys_t = jnp.swapaxes(
            jnp.concatenate([keys.reshape(rows, cache_length, head_dim), new_keys], axis=1), 1, 2
        )
        top = None
        if last:
            top = flash(
                query_head, keys_t, None, counts * span, request_group, cache_length, 0, None, 0, "top"
            )
            got_vals, top = lax.optimization_barrier((got_vals, top))
            raw_v = got_vals.reshape(flat, span, head_dim)[index]
        else:
            raw_v = got[..., head_dim:]
        vals = raw_v.astype(jnp.float32) * slot_scale[:, :, 1, head][:, :, None, None]
        vals = vals.astype(jnp.bfloat16)
        values_all = jnp.concatenate(
            [vals.reshape(rows, cache_length, head_dim), fresh_values[..., cols]], axis=1
        )
        results.append(
            flash(
                query_head, keys_t, values_all, counts * span, request_group,
                cache_length, head * request_group, results[-1] if results else None, queries.shape[2],
                "mix" if last else "both", top,
            )
        )
    return results[-1]


def flash_kernel(*refs, cache_length, chunk, heads, mode):
    bias_ref, q_ref, k_ref = refs[:3]
    v_ref = refs[3] if mode != "top" else None
    top_ref = refs[4] if mode == "mix" else None
    o_ref = refs[-1]
    tokens = q_ref.shape[0]
    lanes = 128
    new_mask = lax.broadcasted_iota(jnp.int32, (tokens, tokens), 1) <= lax.broadcasted_iota(
        jnp.int32, (tokens, tokens), 0
    )

    def fold(acc, s, op):
        for b in range(s.shape[1] // lanes):
            acc = op(acc, s[:, b * lanes:(b + 1) * lanes])
        return acc

    for head in range(heads):
        q = q_ref[:, head * lanes:(head + 1) * lanes]

        def scores(first, size):
            return lax.dot_general(
                q, k_ref[:, first:first + size], (((1,), (0,)), ((), ())),
                preferred_element_type=jnp.float32,
            )

        def masked(first, size):
            return scores(first, size) + bias_ref[:, first:first + size]

        fresh = jnp.where(new_mask, scores(cache_length, tokens), -1e30)
        if mode == "mix":
            top = top_ref[:, head * lanes:head * lanes + 1]
        else:
            top = fold(jnp.full((tokens, lanes), -1e30, jnp.float32), fresh, jnp.maximum)
            for first in range(0, cache_length, chunk):
                top = fold(top, masked(first, chunk), jnp.maximum)
            top = jnp.max(top, axis=1, keepdims=True)
        if mode == "top":
            o_ref[:, head * lanes:(head + 1) * lanes] = jnp.broadcast_to(top, (tokens, lanes))
            continue

        def mix(s, first, size):
            p = jnp.exp(s - top)
            return p, lax.dot_general(
                p.astype(jnp.bfloat16), v_ref[first:first + size, :], (((1,), (0,)), ((), ())),
                preferred_element_type=jnp.float32,
            )

        p, acc = mix(fresh, cache_length, tokens)
        total = fold(jnp.zeros((tokens, lanes), jnp.float32), p, jnp.add)
        for first in range(0, cache_length, chunk):
            p, part = mix(masked(first, chunk), first, chunk)
            total = fold(total, p, jnp.add)
            acc = acc + part
        total = jnp.sum(total, axis=1, keepdims=True)
        o_ref[:, head * lanes:(head + 1) * lanes] = (acc / total).astype(o_ref.dtype)


CHUNK = 512
HEADS = 4


def flash(query_rot, keys_t, values_all, live, request_group, cache_length, offset, into, out_width,
          mode="both", top=None):
    rows, tokens, q_width = query_rot.shape
    head_dim, length = keys_t.shape[1:]
    kv_heads = 1
    chunk = CHUNK if cache_length % CHUNK == 0 else 128
    heads = HEADS
    bias = jnp.where(
        jnp.arange(cache_length, dtype=jnp.int32)[None, :] < live[:, None], 0.0, -1e30
    ).astype(jnp.float32)[:, None, :]
    kernel = functools.partial(
        flash_kernel, cache_length=cache_length, chunk=chunk, heads=heads, mode=mode
    )
    per = request_group // heads
    block = offset // heads
    in_specs = [
        pl.BlockSpec((None, 1, cache_length), lambda r, h, g: (r, 0, 0)),
        pl.BlockSpec((None, tokens, head_dim * heads), lambda r, h, g: (r, 0, h * per + g)),
        pl.BlockSpec((None, head_dim, length), lambda r, h, g: (r, h, 0)),
    ]
    operands = [bias, query_rot, keys_t]
    if mode != "top":
        in_specs.append(pl.BlockSpec((None, length, head_dim), lambda r, h, g: (r, 0, h)))
        operands.append(values_all)
    if mode == "mix":
        in_specs.append(pl.BlockSpec((None, tokens, head_dim * heads), lambda r, h, g: (r, 0, h * per + g)))
        operands.append(top)
    aliases = {}
    if into is not None:
        in_specs.append(pl.BlockSpec(memory_space=pl.ANY))
        aliases = {len(operands): 0}
        operands.append(into)
    if mode == "top":
        out_specs = pl.BlockSpec((None, tokens, head_dim * heads), lambda r, h, g: (r, 0, h * per + g))
        out_shape = jax.ShapeDtypeStruct((rows, tokens, q_width), jnp.float32)
    else:
        out_specs = pl.BlockSpec(
            (None, tokens, head_dim * heads), lambda r, h, g: (r, 0, block + h * per + g)
        )
        out_shape = jax.ShapeDtypeStruct((rows, tokens, out_width), jnp.bfloat16)
    passes = {"both": 3, "top": 1, "mix": 2}[mode]
    return pl.pallas_call(
        kernel,
        grid=(rows, kv_heads, per),
        in_specs=in_specs,
        out_specs=out_specs,
        out_shape=out_shape,
        input_output_aliases=aliases,
        cost_estimate=pl.CostEstimate(
            flops=2 * passes * rows * tokens * q_width * length,
            transcendentals=rows * tokens * (q_width // head_dim) * length,
            bytes_accessed=2 * rows * (2 * tokens * q_width + 2 * length * head_dim),
        ),
    )(*operands)


def solution(mesh):
    return jax.shard_map(
        shards,
        mesh=mesh,
        in_specs=(
            P(("grp", "stretch"), None, "req"),
            P(("grp", "stretch"), None, "req"),
            P(("grp", "stretch"), None, "req"),
            P(("grp", "stretch"), None, "req"),
            P(("grp", "stretch"), None, "req"),
            P(("grp", "stretch"), None, "req"),
            P(("grp", "stretch"), None),
            P(("grp", "stretch")),
            P(("grp", "stretch"), None),
        ),
        out_specs=P(("grp", "stretch"), None, "req"),
        check_vma=False,
    )
```

```python
import functools

import jax
import jax.numpy as jnp
from jax import lax
from jax.experimental import pallas as pl
from jax.experimental.pallas import tpu as pltpu
from jax.sharding import PartitionSpec as P

rope_base = 500000.0


def apply_rotary(x, pos):
    half = x.shape[-1] // 2
    inv = rope_base ** (-(jnp.arange(half, dtype=jnp.float32) * 2.0 / x.shape[-1]))
    angle = pos.astype(jnp.float32)[..., None] * inv
    cosine = jnp.cos(angle)
    sine = jnp.sin(angle)
    first = x[..., :half]
    second = x[..., half:]
    return jnp.concatenate(
        [first * cosine - second * sine, second * cosine + first * sine], axis=-1
    )


def slot_tables(slot_stretch_ids, counts, positions, owners, capacity, per_owner):
    rows, slots = slot_stretch_ids.shape
    owner = slot_stretch_ids // per_owner
    local = slot_stretch_ids % per_owner
    slot_iota = jnp.arange(slots, dtype=jnp.int32)
    live = slot_iota[None, :] < counts[:, None]
    same = owner[:, :, None] == owner[:, None, :]
    earlier = slot_iota[:, None] < slot_iota[None, :]
    rank = jnp.sum((same & earlier[None, :, :] & live[:, :, None]).astype(jnp.int32), axis=1)
    target = owner * capacity + rank
    hits = (
        target[:, :, None] == jnp.arange(owners * capacity, dtype=jnp.int32)[None, None, :]
    ) & live[:, :, None]
    hits = hits.astype(jnp.int32)
    local_table = jnp.sum(hits * (local + 1)[:, :, None], axis=1) - 1
    place_table = jnp.sum(hits * positions[:, :, None], axis=1)
    return (
        local_table.reshape(rows, owners, capacity),
        place_table.reshape(rows, owners, capacity),
        owner,
        rank,
        live,
    )


def shards(
    queries,
    fresh_keys,
    fresh_values,
    stored_stretch_keys,
    stored_stretch_values,
    scales,
    stretch_ids,
    counts,
    stretch_pos,
):
    owners = lax.axis_size("stretch")
    half = owners // 2
    rows, slots = stretch_ids.shape
    per_owner, span, width = stored_stretch_keys.shape
    kv_heads = scales.shape[2]
    head_dim = width // kv_heads
    q_heads = queries.shape[2] // head_dim
    request_group = q_heads // kv_heads
    tokens = queries.shape[1]
    capacity = 2 * slots // owners
    cache_length = slots * span
    me = lax.axis_index("stretch")
    across = [(i, (i + half) % owners) for i in range(owners)]
    mine = slot_tables(stretch_ids, counts, stretch_pos, owners, capacity, per_owner)
    owner, rank, live = (mine[2], mine[3], mine[4])
    scale_code = (scales.astype(jnp.float32) * 65536.0).astype(jnp.int32).reshape(1, 1, -1)
    requests = jnp.concatenate(
        [
            jnp.transpose(mine[0], (1, 0, 2)),
            jnp.broadcast_to(scale_code, (owners, rows, scale_code.shape[2])),
        ],
        axis=2,
    )
    answers = lax.all_to_all(requests, "stretch", split_axis=0, concat_axis=0, tiled=True)
    wanted = jnp.maximum(answers[:, :, :capacity], 0)
    all_scales = (answers[:, 0, capacity:].astype(jnp.float32) * (1.0 / 65536.0)).reshape(
        owners * per_owner, 2, kv_heads
    )
    meta = jnp.concatenate([stretch_ids, stretch_pos, counts[:, None]], axis=1)
    meta_far = lax.ppermute(meta, "stretch", across)
    ids_far, pos_far, counts_far = (
        meta_far[:, :slots], meta_far[:, slots:2 * slots], meta_far[:, 2 * slots]
    )
    queries_far = lax.ppermute(queries, "stretch", across)
    far = slot_tables(ids_far, counts_far, pos_far, owners, capacity, per_owner)
    owner_far, rank_far, live_far = (far[2], far[3], far[4])

    store = jnp.concatenate(
        [
            jnp.concatenate(
                [
                    stored_stretch_keys[..., h * head_dim:(h + 1) * head_dim],
                    stored_stretch_values[..., h * head_dim:(h + 1) * head_dim],
                ],
                axis=-1,
            )
            for h in range(kv_heads)
        ],
        axis=-1,
    )
    side = me // half
    local = me % half
    received = []
    for shift in range(half):
        target_local = (local + shift) % half
        target = side * half + target_local
        partner = (target + half) % owners
        choice = jnp.concatenate(
            [
                lax.dynamic_index_in_dim(wanted, target, 0, keepdims=False),
                lax.dynamic_index_in_dim(wanted, partner, 0, keepdims=False),
            ],
            axis=1,
        )
        payload = store[choice]
        if shift:
            pairs = [
                (i, (i // half) * half + (i % half + shift) % half) for i in range(owners)
            ]
            payload = lax.ppermute(payload, "stretch", pairs)
        received.append(payload)
    received = jnp.stack(received, axis=0).reshape(half * rows * 2 * capacity, span, 2 * width)

    def entries(owner_of, rank_of, live_of, second):
        near = (owner_of // half) == side
        shift = (local - owner_of % half) % half
        position = ((shift * rows + jnp.arange(rows, dtype=jnp.int32)[:, None]) * 2 + second) * capacity + rank_of
        use = live_of & near
        return jnp.where(use, position, 0), use

    token_positions = cache_length + jnp.arange(tokens, dtype=jnp.int32)

    def rotate_queries(raw):
        rotated = (
            apply_rotary(
                raw.reshape(rows, tokens, q_heads, head_dim).astype(jnp.float32),
                token_positions[:, None],
            )
            * head_dim ** (-0.5)
        ).astype(jnp.bfloat16)
        return rotated.reshape(rows, tokens, q_heads * head_dim)

    def partial(raw_queries, ids_of, pos_of, owner_of, rank_of, live_of, second, with_fresh, out_dtype):
        position, use = entries(owner_of, rank_of, live_of, second)
        got = received[position]
        slot_scale = all_scales[ids_of]
        placement = pos_of[:, :, None] + jnp.arange(span, dtype=jnp.int32)
        query_rot = rotate_queries(raw_queries)
        bias = jnp.where(jnp.repeat(use, span, axis=1), 0.0, -1e30).astype(jnp.float32)[:, None, :]
        outs = []
        for head in range(kv_heads):
            base = head * 2 * head_dim
            keys = got[..., base:base + head_dim].astype(jnp.float32) * slot_scale[:, :, 0, head][:, :, None, None]
            keys = apply_rotary(keys, placement).astype(jnp.bfloat16).reshape(rows, cache_length, head_dim)
            vals = got[..., base + head_dim:base + 2 * head_dim].astype(jnp.float32)
            vals = (vals * slot_scale[:, :, 1, head][:, :, None, None]).astype(jnp.bfloat16)
            vals = vals.reshape(rows, cache_length, head_dim)
            if with_fresh:
                cols = slice(head * head_dim, (head + 1) * head_dim)
                new_keys = apply_rotary(
                    fresh_keys[..., cols].astype(jnp.float32), token_positions
                ).astype(jnp.bfloat16)
                keys = jnp.concatenate([keys, new_keys], axis=1)
                vals = jnp.concatenate([vals, fresh_values[..., cols]], axis=1)
            group_cols = slice(head * request_group * head_dim, (head + 1) * request_group * head_dim)
            outs.append(
                flash(query_rot[..., group_cols], jnp.swapaxes(keys, 1, 2), vals, bias,
                      request_group, cache_length, out_dtype)
            )
        return [jnp.concatenate([o[i] for o in outs], axis=-1) for i in range(3)]

    far_out, far_top, far_total = partial(
        queries_far, ids_far, pos_far, owner_far, rank_far, live_far, 1, False, jnp.bfloat16
    )
    far_stats = jnp.concatenate([far_top[..., ::head_dim], far_total[..., ::head_dim]], axis=-1)
    back_out = lax.ppermute(far_out, "stretch", across)
    back_stats = lax.ppermute(far_stats, "stretch", across)
    near_out, near_top, near_total = partial(
        queries, stretch_ids, stretch_pos, owner, rank, live, 0, True, jnp.float32
    )
    back_top = jnp.repeat(back_stats[..., :q_heads], head_dim, axis=-1)
    back_total = jnp.repeat(back_stats[..., q_heads:], head_dim, axis=-1)
    top = jnp.maximum(near_top, back_top)
    near_weight = near_total * jnp.exp(near_top - top)
    back_weight = back_total * jnp.exp(back_top - top)
    mixed = near_out * near_weight + back_out.astype(jnp.float32) * back_weight
    return (mixed / (near_weight + back_weight)).astype(jnp.bfloat16)


def flash_kernel(*refs, cache_length, chunk, heads, fresh):
    bias_ref, q_ref, k_ref, v_ref = refs[:4]
    o_ref, m_ref, l_ref = refs[-3:]
    tokens = q_ref.shape[0]
    lanes = 128
    new_mask = lax.broadcasted_iota(jnp.int32, (tokens, tokens), 1) <= lax.broadcasted_iota(
        jnp.int32, (tokens, tokens), 0
    )

    def fold(acc, s, op):
        for b in range(s.shape[1] // lanes):
            acc = op(acc, s[:, b * lanes:(b + 1) * lanes])
        return acc

    for head in range(heads):
        q = q_ref[:, head * lanes:(head + 1) * lanes]

        def scores(first, size):
            return lax.dot_general(
                q, k_ref[:, first:first + size], (((1,), (0,)), ((), ())),
                preferred_element_type=jnp.float32,
            )

        def masked(first, size):
            return scores(first, size) + bias_ref[:, first:first + size]

        top = jnp.full((tokens, lanes), -1e30, jnp.float32)
        if fresh:
            recent = jnp.where(new_mask, scores(cache_length, tokens), -1e30)
            top = fold(top, recent, jnp.maximum)
        for first in range(0, cache_length, chunk):
            top = fold(top, masked(first, chunk), jnp.maximum)
        top = jnp.max(top, axis=1, keepdims=True)

        def mix(s, first, size):
            p = jnp.exp(s - top)
            return p, lax.dot_general(
                p.astype(jnp.bfloat16), v_ref[first:first + size, :], (((1,), (0,)), ((), ())),
                preferred_element_type=jnp.float32,
            )

        total = jnp.zeros((tokens, lanes), jnp.float32)
        acc = jnp.zeros((tokens, lanes), jnp.float32)
        if fresh:
            p, acc = mix(recent, cache_length, tokens)
            total = fold(total, p, jnp.add)
        for first in range(0, cache_length, chunk):
            p, part = mix(masked(first, chunk), first, chunk)
            total = fold(total, p, jnp.add)
            acc = acc + part
        total = jnp.sum(total, axis=1, keepdims=True)
        cols = slice(head * lanes, (head + 1) * lanes)
        o_ref[:, cols] = (acc / total).astype(o_ref.dtype)
        m_ref[:, cols] = jnp.broadcast_to(top, (tokens, lanes))
        l_ref[:, cols] = jnp.broadcast_to(total, (tokens, lanes))


CHUNK = 512
HEADS = 4


def flash(query_rot, keys_t, values_all, bias, request_group, cache_length, out_dtype):
    rows, tokens, q_width = query_rot.shape
    head_dim, length = keys_t.shape[1:]
    fresh = length > cache_length
    chunk = CHUNK if cache_length % CHUNK == 0 else 128
    heads = HEADS
    kernel = functools.partial(
        flash_kernel, cache_length=cache_length, chunk=chunk, heads=heads, fresh=fresh
    )
    per = request_group // heads
    q_spec = pl.BlockSpec((None, tokens, head_dim * heads), lambda r, g: (r, 0, g))
    passes = 3
    return pl.pallas_call(
        kernel,
        grid=(rows, per),
        in_specs=[
            pl.BlockSpec((None, 1, cache_length), lambda r, g: (r, 0, 0)),
            q_spec,
            pl.BlockSpec((None, head_dim, length), lambda r, g: (r, 0, 0)),
            pl.BlockSpec((None, length, head_dim), lambda r, g: (r, 0, 0)),
        ],
        out_specs=[q_spec, q_spec, q_spec],
        out_shape=[
            jax.ShapeDtypeStruct((rows, tokens, q_width), out_dtype),
            jax.ShapeDtypeStruct((rows, tokens, q_width), jnp.float32),
            jax.ShapeDtypeStruct((rows, tokens, q_width), jnp.float32),
        ],
        cost_estimate=pl.CostEstimate(
            flops=2 * passes * rows * tokens * q_width * length,
            transcendentals=rows * tokens * (q_width // head_dim) * length,
            bytes_accessed=2 * rows * (2 * tokens * q_width + 2 * length * head_dim),
        ),
    )(bias, query_rot, keys_t, values_all)


def solution(mesh):
    return jax.shard_map(
        shards,
        mesh=mesh,
        in_specs=(
            P(("grp", "stretch"), None, "req"),
            P(("grp", "stretch"), None, "req"),
            P(("grp", "stretch"), None, "req"),
            P(("grp", "stretch"), None, "req"),
            P(("grp", "stretch"), None, "req"),
            P(("grp", "stretch"), None, "req"),
            P(("grp", "stretch"), None),
            P(("grp", "stretch")),
            P(("grp", "stretch"), None),
        ),
        out_specs=P(("grp", "stretch"), None, "req"),
        check_vma=False,
    )
```

```python
import functools

import jax
import jax.numpy as jnp
from jax import lax
from jax.experimental import pallas as pl
from jax.experimental.pallas import tpu as pltpu
from jax.sharding import PartitionSpec as P

rope_base = 500000.0


def apply_rotary(x, pos):
    half = x.shape[-1] // 2
    inv = rope_base ** (-(jnp.arange(half, dtype=jnp.float32) * 2.0 / x.shape[-1]))
    angle = pos.astype(jnp.float32)[..., None] * inv
    cosine = jnp.cos(angle)
    sine = jnp.sin(angle)
    first = x[..., :half]
    second = x[..., half:]
    return jnp.concatenate(
        [first * cosine - second * sine, second * cosine + first * sine], axis=-1
    )


def slot_tables(slot_stretch_ids, counts, positions, owners, capacity, per_owner):
    rows, slots = slot_stretch_ids.shape
    owner = slot_stretch_ids // per_owner
    local = slot_stretch_ids % per_owner
    slot_iota = jnp.arange(slots, dtype=jnp.int32)
    live = slot_iota[None, :] < counts[:, None]
    same = owner[:, :, None] == owner[:, None, :]
    earlier = slot_iota[:, None] < slot_iota[None, :]
    rank = jnp.sum((same & earlier[None, :, :] & live[:, :, None]).astype(jnp.int32), axis=1)
    target = owner * capacity + rank
    hits = (
        target[:, :, None] == jnp.arange(owners * capacity, dtype=jnp.int32)[None, None, :]
    ) & live[:, :, None]
    hits = hits.astype(jnp.int32)
    local_table = jnp.sum(hits * (local + 1)[:, :, None], axis=1) - 1
    place_table = jnp.sum(hits * positions[:, :, None], axis=1)
    return (
        local_table.reshape(rows, owners, capacity),
        place_table.reshape(rows, owners, capacity),
        owner,
        rank,
        live,
    )


def shards(
    queries,
    fresh_keys,
    fresh_values,
    stored_stretch_keys,
    stored_stretch_values,
    scales,
    stretch_ids,
    counts,
    stretch_pos,
):
    owners = lax.axis_size("stretch")
    half = owners // 2
    rows, slots = stretch_ids.shape
    per_owner, span, width = stored_stretch_keys.shape
    kv_heads = scales.shape[2]
    head_dim = width // kv_heads
    q_heads = queries.shape[2] // head_dim
    request_group = q_heads // kv_heads
    tokens = queries.shape[1]
    capacity = 2 * slots // owners
    cache_length = slots * span
    me = lax.axis_index("stretch")
    across = [(i, (i + half) % owners) for i in range(owners)]
    mine = slot_tables(stretch_ids, counts, stretch_pos, owners, capacity, per_owner)
    owner, rank, live = (mine[2], mine[3], mine[4])
    scale_code = (scales.astype(jnp.float32) * 65536.0).astype(jnp.int32).reshape(1, 1, -1)
    requests = jnp.concatenate(
        [
            jnp.transpose(mine[0], (1, 0, 2)),
            jnp.broadcast_to(scale_code, (owners, rows, scale_code.shape[2])),
        ],
        axis=2,
    )
    answers = lax.all_to_all(requests, "stretch", split_axis=0, concat_axis=0, tiled=True)
    wanted = jnp.maximum(answers[:, :, :capacity], 0)
    all_scales = (answers[:, 0, capacity:].astype(jnp.float32) * (1.0 / 65536.0)).reshape(
        owners * per_owner, 2, kv_heads
    )
    meta = jnp.concatenate([stretch_ids, stretch_pos, counts[:, None]], axis=1)
    meta_far = lax.ppermute(meta, "stretch", across)
    ids_far, pos_far, counts_far = (
        meta_far[:, :slots], meta_far[:, slots:2 * slots], meta_far[:, 2 * slots]
    )
    queries, answers = lax.optimization_barrier((queries, answers))
    queries_far = lax.ppermute(queries, "stretch", across)
    far = slot_tables(ids_far, counts_far, pos_far, owners, capacity, per_owner)
    owner_far, rank_far, live_far = (far[2], far[3], far[4])

    store = jnp.concatenate(
        [
            jnp.concatenate(
                [
                    stored_stretch_keys[..., h * head_dim:(h + 1) * head_dim],
                    stored_stretch_values[..., h * head_dim:(h + 1) * head_dim],
                ],
                axis=-1,
            )
            for h in range(kv_heads)
        ],
        axis=-1,
    )
    side = me // half
    local = me % half

    def exchange(for_partner, after):
        pieces = []
        for shift in range(half):
            target = side * half + (local + shift) % half
            if for_partner:
                target = (target + half) % owners
            choice = lax.dynamic_index_in_dim(wanted, target, 0, keepdims=False)
            if after is not None:
                choice, after = lax.optimization_barrier((choice, after))
            payload = store[choice]
            if shift:
                pairs = [
                    (i, (i // half) * half + (i % half + shift) % half) for i in range(owners)
                ]
                payload = lax.ppermute(payload, "stretch", pairs)
            pieces.append(payload)
        return jnp.stack(pieces, axis=0).reshape(half * rows * capacity, span, 2 * width)

    received_far = exchange(True, None)
    received_near = exchange(False, received_far)

    def entries(owner_of, rank_of, live_of):
        near = (owner_of // half) == side
        shift = (local - owner_of % half) % half
        position = (shift * rows + jnp.arange(rows, dtype=jnp.int32)[:, None]) * capacity + rank_of
        use = live_of & near
        return jnp.where(use, position, 0), use

    token_positions = cache_length + jnp.arange(tokens, dtype=jnp.int32)

    def rotate_queries(raw):
        rotated = (
            apply_rotary(
                raw.reshape(rows, tokens, q_heads, head_dim).astype(jnp.float32),
                token_positions[:, None],
            )
            * head_dim ** (-0.5)
        ).astype(jnp.bfloat16)
        return rotated.reshape(rows, tokens, q_heads * head_dim)

    def partial(received, raw_queries, ids_of, pos_of, owner_of, rank_of, live_of, with_fresh, out_dtype):
        position, use = entries(owner_of, rank_of, live_of)
        got = received[position]
        slot_scale = all_scales[ids_of]
        placement = pos_of[:, :, None] + jnp.arange(span, dtype=jnp.int32)
        query_rot = rotate_queries(raw_queries)
        bias = jnp.where(jnp.repeat(use, span, axis=1), 0.0, -1e30).astype(jnp.float32)[:, None, :]
        outs = []
        for head in range(kv_heads):
            base = head * 2 * head_dim
            keys = got[..., base:base + head_dim].astype(jnp.float32) * slot_scale[:, :, 0, head][:, :, None, None]
            keys = apply_rotary(keys, placement).astype(jnp.bfloat16).reshape(rows, cache_length, head_dim)
            vals = got[..., base + head_dim:base + 2 * head_dim].astype(jnp.float32)
            vals = (vals * slot_scale[:, :, 1, head][:, :, None, None]).astype(jnp.bfloat16)
            vals = vals.reshape(rows, cache_length, head_dim)
            if with_fresh:
                cols = slice(head * head_dim, (head + 1) * head_dim)
                new_keys = apply_rotary(
                    fresh_keys[..., cols].astype(jnp.float32), token_positions
                ).astype(jnp.bfloat16)
                keys = jnp.concatenate([keys, new_keys], axis=1)
                vals = jnp.concatenate([vals, fresh_values[..., cols]], axis=1)
            group_cols = slice(head * request_group * head_dim, (head + 1) * request_group * head_dim)
            outs.append(
                flash(query_rot[..., group_cols], jnp.swapaxes(keys, 1, 2), vals, bias,
                      request_group, cache_length, out_dtype)
            )
        return [jnp.concatenate([o[i] for o in outs], axis=-1) for i in range(3)]

    far_out, far_top, far_total = partial(
        received_far, queries_far, ids_far, pos_far, owner_far, rank_far, live_far, False, jnp.bfloat16
    )
    far_stats = jnp.concatenate([far_top[..., ::head_dim], far_total[..., ::head_dim]], axis=-1)
    back_out = lax.ppermute(far_out, "stretch", across)
    back_stats = lax.ppermute(far_stats, "stretch", across)
    received_near, far_stats = lax.optimization_barrier((received_near, far_stats))
    near_out, near_top, near_total = partial(
        received_near, queries, stretch_ids, stretch_pos, owner, rank, live, True, jnp.float32
    )
    back_top = jnp.repeat(back_stats[..., :q_heads], head_dim, axis=-1)
    back_total = jnp.repeat(back_stats[..., q_heads:], head_dim, axis=-1)
    top = jnp.maximum(near_top, back_top)
    near_weight = near_total * jnp.exp(near_top - top)
    back_weight = back_total * jnp.exp(back_top - top)
    mixed = near_out * near_weight + back_out.astype(jnp.float32) * back_weight
    return (mixed / (near_weight + back_weight)).astype(jnp.bfloat16)


def flash_kernel(*refs, cache_length, chunk, heads, fresh):
    bias_ref, q_ref, k_ref, v_ref = refs[:4]
    o_ref, m_ref, l_ref = refs[-3:]
    tokens = q_ref.shape[0]
    lanes = 128
    new_mask = lax.broadcasted_iota(jnp.int32, (tokens, tokens), 1) <= lax.broadcasted_iota(
        jnp.int32, (tokens, tokens), 0
    )

    def fold(acc, s, op):
        for b in range(s.shape[1] // lanes):
            acc = op(acc, s[:, b * lanes:(b + 1) * lanes])
        return acc

    for head in range(heads):
        q = q_ref[:, head * lanes:(head + 1) * lanes]

        def scores(first, size):
            return lax.dot_general(
                q, k_ref[:, first:first + size], (((1,), (0,)), ((), ())),
                preferred_element_type=jnp.float32,
            )

        def masked(first, size):
            return scores(first, size) + bias_ref[:, first:first + size]

        top = jnp.full((tokens, lanes), -1e30, jnp.float32)
        if fresh:
            recent = jnp.where(new_mask, scores(cache_length, tokens), -1e30)
            top = fold(top, recent, jnp.maximum)
        for first in range(0, cache_length, chunk):
            top = fold(top, masked(first, chunk), jnp.maximum)
        top = jnp.max(top, axis=1, keepdims=True)

        def mix(s, first, size):
            p = jnp.exp(s - top)
            return p, lax.dot_general(
                p.astype(jnp.bfloat16), v_ref[first:first + size, :], (((1,), (0,)), ((), ())),
                preferred_element_type=jnp.float32,
            )

        total = jnp.zeros((tokens, lanes), jnp.float32)
        acc = jnp.zeros((tokens, lanes), jnp.float32)
        if fresh:
            p, acc = mix(recent, cache_length, tokens)
            total = fold(total, p, jnp.add)
        for first in range(0, cache_length, chunk):
            p, part = mix(masked(first, chunk), first, chunk)
            total = fold(total, p, jnp.add)
            acc = acc + part
        total = jnp.sum(total, axis=1, keepdims=True)
        cols = slice(head * lanes, (head + 1) * lanes)
        o_ref[:, cols] = (acc / total).astype(o_ref.dtype)
        m_ref[:, cols] = jnp.broadcast_to(top, (tokens, lanes))
        l_ref[:, cols] = jnp.broadcast_to(total, (tokens, lanes))


CHUNK = 512
HEADS = 4


def flash(query_rot, keys_t, values_all, bias, request_group, cache_length, out_dtype):
    rows, tokens, q_width = query_rot.shape
    head_dim, length = keys_t.shape[1:]
    fresh = length > cache_length
    chunk = CHUNK if cache_length % CHUNK == 0 else 128
    heads = HEADS
    kernel = functools.partial(
        flash_kernel, cache_length=cache_length, chunk=chunk, heads=heads, fresh=fresh
    )
    per = request_group // heads
    q_spec = pl.BlockSpec((None, tokens, head_dim * heads), lambda r, g: (r, 0, g))
    passes = 3
    return pl.pallas_call(
        kernel,
        grid=(rows, per),
        in_specs=[
            pl.BlockSpec((None, 1, cache_length), lambda r, g: (r, 0, 0)),
            q_spec,
            pl.BlockSpec((None, head_dim, length), lambda r, g: (r, 0, 0)),
            pl.BlockSpec((None, length, head_dim), lambda r, g: (r, 0, 0)),
        ],
        out_specs=[q_spec, q_spec, q_spec],
        out_shape=[
            jax.ShapeDtypeStruct((rows, tokens, q_width), out_dtype),
            jax.ShapeDtypeStruct((rows, tokens, q_width), jnp.float32),
            jax.ShapeDtypeStruct((rows, tokens, q_width), jnp.float32),
        ],
        cost_estimate=pl.CostEstimate(
            flops=2 * passes * rows * tokens * q_width * length,
            transcendentals=rows * tokens * (q_width // head_dim) * length,
            bytes_accessed=2 * rows * (2 * tokens * q_width + 2 * length * head_dim),
        ),
    )(bias, query_rot, keys_t, values_all)


def solution(mesh):
    return jax.shard_map(
        shards,
        mesh=mesh,
        in_specs=(
            P(("grp", "stretch"), None, "req"),
            P(("grp", "stretch"), None, "req"),
            P(("grp", "stretch"), None, "req"),
            P(("grp", "stretch"), None, "req"),
            P(("grp", "stretch"), None, "req"),
            P(("grp", "stretch"), None, "req"),
            P(("grp", "stretch"), None),
            P(("grp", "stretch")),
            P(("grp", "stretch"), None),
        ),
        out_specs=P(("grp", "stretch"), None, "req"),
        check_vma=False,
    )
```

```python
import functools

import jax
import jax.numpy as jnp
from jax import lax
from jax.experimental import pallas as pl
from jax.experimental.pallas import tpu as pltpu
from jax.sharding import PartitionSpec as P

rope_base = 500000.0


def apply_rotary(x, pos):
    half = x.shape[-1] // 2
    inv = rope_base ** (-(jnp.arange(half, dtype=jnp.float32) * 2.0 / x.shape[-1]))
    angle = pos.astype(jnp.float32)[..., None] * inv
    cosine = jnp.cos(angle)
    sine = jnp.sin(angle)
    first = x[..., :half]
    second = x[..., half:]
    return jnp.concatenate(
        [first * cosine - second * sine, second * cosine + first * sine], axis=-1
    )


def slot_tables(slot_stretch_ids, counts, positions, owners, capacity, per_owner):
    rows, slots = slot_stretch_ids.shape
    owner = slot_stretch_ids // per_owner
    local = slot_stretch_ids % per_owner
    slot_iota = jnp.arange(slots, dtype=jnp.int32)
    live = slot_iota[None, :] < counts[:, None]
    same = owner[:, :, None] == owner[:, None, :]
    earlier = slot_iota[:, None] < slot_iota[None, :]
    rank = jnp.sum((same & earlier[None, :, :] & live[:, :, None]).astype(jnp.int32), axis=1)
    target = owner * capacity + rank
    hits = (
        target[:, :, None] == jnp.arange(owners * capacity, dtype=jnp.int32)[None, None, :]
    ) & live[:, :, None]
    hits = hits.astype(jnp.int32)
    local_table = jnp.sum(hits * (local + 1)[:, :, None], axis=1) - 1
    place_table = jnp.sum(hits * positions[:, :, None], axis=1)
    return (
        local_table.reshape(rows, owners, capacity),
        place_table.reshape(rows, owners, capacity),
        owner,
        rank,
        live,
    )


def shards(
    queries,
    fresh_keys,
    fresh_values,
    stored_stretch_keys,
    stored_stretch_values,
    scales,
    stretch_ids,
    counts,
    stretch_pos,
):
    owners = lax.axis_size("stretch")
    rows, slots = stretch_ids.shape
    per_owner, span, width = stored_stretch_keys.shape
    kv_heads = scales.shape[2]
    head_dim = width // kv_heads
    q_heads = queries.shape[2] // head_dim
    request_group = q_heads // kv_heads
    tokens = queries.shape[1]
    capacity = 2 * slots // owners
    cache_length = slots * span
    mine = slot_tables(stretch_ids, counts, stretch_pos, owners, capacity, per_owner)
    owner, rank, live = (mine[2], mine[3], mine[4])
    scale_code = (scales.astype(jnp.float32) * 65536.0).astype(jnp.int32).reshape(1, 1, -1)
    requests = jnp.concatenate(
        [
            jnp.transpose(mine[0], (1, 0, 2)),
            jnp.broadcast_to(scale_code, (owners, rows, scale_code.shape[2])),
        ],
        axis=2,
    )
    answers = lax.all_to_all(requests, "stretch", split_axis=0, concat_axis=0, tiled=True)
    wanted = answers[:, :, :capacity]
    chosen = jnp.maximum(wanted, 0)
    all_scales = (answers[:, 0, capacity:].astype(jnp.float32) * (1.0 / 65536.0)).reshape(
        owners * per_owner, 2, scales.shape[2]
    )
    store = jnp.stack(
        [
            jnp.concatenate(
                [
                    stored_stretch_keys[..., h * head_dim:(h + 1) * head_dim],
                    stored_stretch_values[..., h * head_dim:(h + 1) * head_dim],
                ],
                axis=-1,
            )
            for h in range(kv_heads)
        ],
        axis=0,
    )
    flat = owners * rows * capacity
    index = (owner * rows + jnp.arange(rows, dtype=jnp.int32)[:, None]) * capacity + rank
    index = jnp.where(live, index, 0)
    slot_scale = all_scales[stretch_ids]
    placement = stretch_pos[:, :, None] + jnp.arange(span, dtype=jnp.int32)
    token_positions = cache_length + jnp.arange(tokens, dtype=jnp.int32)
    query_rot = (
        apply_rotary(
            queries.reshape(rows, tokens, q_heads, head_dim).astype(jnp.float32),
            token_positions[:, None],
        )
        * head_dim ** (-0.5)
    ).astype(jnp.bfloat16)
    query_rot = query_rot.reshape(rows, tokens, q_heads * head_dim)
    results = []
    for head in range(kv_heads):
        cols = slice(head * head_dim, (head + 1) * head_dim)
        last = head == kv_heads - 1
        new_keys = apply_rotary(
            fresh_keys[..., cols].astype(jnp.float32), token_positions
        ).astype(jnp.bfloat16)
        group_cols = slice(head * request_group * head_dim, (head + 1) * request_group * head_dim)
        query_head = query_rot[..., group_cols]
        if last:
            got_keys = lax.all_to_all(
                store[head][chosen][..., :head_dim], "stretch", split_axis=0, concat_axis=0, tiled=True
            )
            if results:
                got_keys, earlier = lax.optimization_barrier((got_keys, results[-1]))
                results[-1] = earlier
            got_vals = lax.all_to_all(
                store[head][chosen][..., head_dim:], "stretch", split_axis=0, concat_axis=0, tiled=True
            )
            raw_k = got_keys.reshape(flat, span, head_dim)[index]
        else:
            got = lax.all_to_all(store[head][chosen], "stretch", split_axis=0, concat_axis=0, tiled=True)
            if results:
                got, earlier = lax.optimization_barrier((got, results[-1]))
                results[-1] = earlier
            got = got.reshape(flat, span, 2 * head_dim)[index]
            raw_k = got[..., :head_dim]
        keys = raw_k.astype(jnp.float32) * slot_scale[:, :, 0, head][:, :, None, None]
        keys = apply_rotary(keys, placement).astype(jnp.bfloat16)
        keys_t = jnp.swapaxes(
            jnp.concatenate([keys.reshape(rows, cache_length, head_dim), new_keys], axis=1), 1, 2
        )
        top = None
        if last:
            top = flash(
                query_head, keys_t, None, counts * span, request_group, cache_length, 0, None, 0, "top"
            )
            got_vals, top = lax.optimization_barrier((got_vals, top))
            raw_v = got_vals.reshape(flat, span, head_dim)[index]
        else:
            raw_v = got[..., head_dim:]
        vals = raw_v.astype(jnp.float32) * slot_scale[:, :, 1, head][:, :, None, None]
        vals = vals.astype(jnp.bfloat16)
        values_all = jnp.concatenate(
            [vals.reshape(rows, cache_length, head_dim), fresh_values[..., cols]], axis=1
        )
        results.append(
            flash(
                query_head, keys_t, values_all, counts * span, request_group,
                cache_length, head * request_group, results[-1] if results else None, queries.shape[2],
                "mix" if last else "both", top,
            )
        )
    return results[-1]


def flash_kernel(*refs, cache_length, chunk, heads, mode):
    bias_ref, q_ref, k_ref = refs[:3]
    v_ref = refs[3] if mode != "top" else None
    top_ref = refs[4] if mode == "mix" else None
    o_ref = refs[-1]
    tokens = q_ref.shape[0]
    lanes = 128
    new_mask = lax.broadcasted_iota(jnp.int32, (tokens, tokens), 1) <= lax.broadcasted_iota(
        jnp.int32, (tokens, tokens), 0
    )

    def fold(acc, s, op):
        for b in range(s.shape[1] // lanes):
            acc = op(acc, s[:, b * lanes:(b + 1) * lanes])
        return acc

    for head in range(heads):
        q = q_ref[:, head * lanes:(head + 1) * lanes]

        def scores(first, size):
            return lax.dot_general(
                q, k_ref[:, first:first + size], (((1,), (0,)), ((), ())),
                preferred_element_type=jnp.float32,
            )

        def masked(first, size):
            return scores(first, size) + bias_ref[:, first:first + size]

        fresh = jnp.where(new_mask, scores(cache_length, tokens), -1e30)
        if mode == "mix":
            top = top_ref[:, head * lanes:(head + 1) * lanes]
        else:
            top = fold(jnp.full((tokens, lanes), -1e30, jnp.float32), fresh, jnp.maximum)
            for first in range(0, cache_length, chunk):
                top = fold(top, masked(first, chunk), jnp.maximum)
            top = jnp.max(top, axis=1, keepdims=True)
        if mode == "top":
            o_ref[:, head * lanes:(head + 1) * lanes] = jnp.broadcast_to(top, (tokens, lanes))
            continue

        def mix(s, first, size):
            if mode == "mix":
                p = jnp.exp(s - jnp.tile(top, (1, size // lanes)))
            else:
                p = jnp.exp(s - top)
            return p, lax.dot_general(
                p.astype(jnp.bfloat16), v_ref[first:first + size, :], (((1,), (0,)), ((), ())),
                preferred_element_type=jnp.float32,
            )

        p, acc = mix(fresh, cache_length, tokens)
        total = fold(jnp.zeros((tokens, lanes), jnp.float32), p, jnp.add)
        for first in range(0, cache_length, chunk):
            p, part = mix(masked(first, chunk), first, chunk)
            total = fold(total, p, jnp.add)
            acc = acc + part
        total = jnp.sum(total, axis=1, keepdims=True)
        o_ref[:, head * lanes:(head + 1) * lanes] = (acc / total).astype(o_ref.dtype)


CHUNK = 512
HEADS = 4


def flash(query_rot, keys_t, values_all, live, request_group, cache_length, offset, into, out_width,
          mode="both", top=None):
    rows, tokens, q_width = query_rot.shape
    head_dim, length = keys_t.shape[1:]
    kv_heads = 1
    chunk = CHUNK if cache_length % CHUNK == 0 else 128
    heads = HEADS
    bias = jnp.where(
        jnp.arange(cache_length, dtype=jnp.int32)[None, :] < live[:, None], 0.0, -1e30
    ).astype(jnp.float32)[:, None, :]
    kernel = functools.partial(
        flash_kernel, cache_length=cache_length, chunk=chunk, heads=heads, mode=mode
    )
    per = request_group // heads
    block = offset // heads
    in_specs = [
        pl.BlockSpec((None, 1, cache_length), lambda r, h, g: (r, 0, 0)),
        pl.BlockSpec((None, tokens, head_dim * heads), lambda r, h, g: (r, 0, h * per + g)),
        pl.BlockSpec((None, head_dim, length), lambda r, h, g: (r, h, 0)),
    ]
    operands = [bias, query_rot, keys_t]
    if mode != "top":
        in_specs.append(pl.BlockSpec((None, length, head_dim), lambda r, h, g: (r, 0, h)))
        operands.append(values_all)
    if mode == "mix":
        in_specs.append(pl.BlockSpec((None, tokens, head_dim * heads), lambda r, h, g: (r, 0, h * per + g)))
        operands.append(top)
    aliases = {}
    if into is not None:
        in_specs.append(pl.BlockSpec(memory_space=pl.ANY))
        aliases = {len(operands): 0}
        operands.append(into)
    if mode == "top":
        out_specs = pl.BlockSpec((None, tokens, head_dim * heads), lambda r, h, g: (r, 0, h * per + g))
        out_shape = jax.ShapeDtypeStruct((rows, tokens, q_width), jnp.float32)
    else:
        out_specs = pl.BlockSpec(
            (None, tokens, head_dim * heads), lambda r, h, g: (r, 0, block + h * per + g)
        )
        out_shape = jax.ShapeDtypeStruct((rows, tokens, out_width), jnp.bfloat16)
    passes = {"both": 3, "top": 1, "mix": 2}[mode]
    return pl.pallas_call(
        kernel,
        grid=(rows, kv_heads, per),
        in_specs=in_specs,
        out_specs=out_specs,
        out_shape=out_shape,
        input_output_aliases=aliases,
        cost_estimate=pl.CostEstimate(
            flops=2 * passes * rows * tokens * q_width * length,
            transcendentals=rows * tokens * (q_width // head_dim) * length,
            bytes_accessed=2 * rows * (2 * tokens * q_width + 2 * length * head_dim),
        ),
    )(*operands)


def solution(mesh):
    return jax.shard_map(
        shards,
        mesh=mesh,
        in_specs=(
            P(("grp", "stretch"), None, "req"),
            P(("grp", "stretch"), None, "req"),
            P(("grp", "stretch"), None, "req"),
            P(("grp", "stretch"), None, "req"),
            P(("grp", "stretch"), None, "req"),
            P(("grp", "stretch"), None, "req"),
            P(("grp", "stretch"), None),
            P(("grp", "stretch")),
            P(("grp", "stretch"), None),
        ),
        out_specs=P(("grp", "stretch"), None, "req"),
        check_vma=False,
    )
```

```python
import functools

import jax
import jax.numpy as jnp
from jax import lax
from jax.experimental import pallas as pl
from jax.experimental.pallas import tpu as pltpu
from jax.sharding import PartitionSpec as P

rope_base = 500000.0


def apply_rotary(x, pos):
    half = x.shape[-1] // 2
    inv = rope_base ** (-(jnp.arange(half, dtype=jnp.float32) * 2.0 / x.shape[-1]))
    angle = pos.astype(jnp.float32)[..., None] * inv
    cosine = jnp.cos(angle)
    sine = jnp.sin(angle)
    first = x[..., :half]
    second = x[..., half:]
    return jnp.concatenate(
        [first * cosine - second * sine, second * cosine + first * sine], axis=-1
    )


def slot_tables(slot_stretch_ids, counts, positions, owners, capacity, per_owner):
    rows, slots = slot_stretch_ids.shape
    owner = slot_stretch_ids // per_owner
    local = slot_stretch_ids % per_owner
    slot_iota = jnp.arange(slots, dtype=jnp.int32)
    live = slot_iota[None, :] < counts[:, None]
    same = owner[:, :, None] == owner[:, None, :]
    earlier = slot_iota[:, None] < slot_iota[None, :]
    rank = jnp.sum((same & earlier[None, :, :] & live[:, :, None]).astype(jnp.int32), axis=1)
    target = owner * capacity + rank
    hits = (
        target[:, :, None] == jnp.arange(owners * capacity, dtype=jnp.int32)[None, None, :]
    ) & live[:, :, None]
    hits = hits.astype(jnp.int32)
    local_table = jnp.sum(hits * (local + 1)[:, :, None], axis=1) - 1
    place_table = jnp.sum(hits * positions[:, :, None], axis=1)
    return (
        local_table.reshape(rows, owners, capacity),
        place_table.reshape(rows, owners, capacity),
        owner,
        rank,
        live,
    )


def shards(
    queries,
    fresh_keys,
    fresh_values,
    stored_stretch_keys,
    stored_stretch_values,
    scales,
    stretch_ids,
    counts,
    stretch_pos,
):
    owners = lax.axis_size("stretch")
    rows, slots = stretch_ids.shape
    per_owner, span, width = stored_stretch_keys.shape
    kv_heads = scales.shape[2]
    head_dim = width // kv_heads
    q_heads = queries.shape[2] // head_dim
    request_group = q_heads // kv_heads
    tokens = queries.shape[1]
    capacity = 2 * slots // owners
    cache_length = slots * span
    mine = slot_tables(stretch_ids, counts, stretch_pos, owners, capacity, per_owner)
    owner, rank, live = (mine[2], mine[3], mine[4])
    scale_code = (scales.astype(jnp.float32) * 65536.0).astype(jnp.int32).reshape(1, 1, -1)
    requests = jnp.concatenate(
        [
            jnp.transpose(mine[0], (1, 0, 2)),
            jnp.broadcast_to(scale_code, (owners, rows, scale_code.shape[2])),
        ],
        axis=2,
    )
    answers = lax.all_to_all(requests, "stretch", split_axis=0, concat_axis=0, tiled=True)
    wanted = answers[:, :, :capacity]
    chosen = jnp.maximum(wanted, 0)
    all_scales = (answers[:, 0, capacity:].astype(jnp.float32) * (1.0 / 65536.0)).reshape(
        owners * per_owner, 2, scales.shape[2]
    )
    store = jnp.stack(
        [
            jnp.concatenate(
                [
                    stored_stretch_keys[..., h * head_dim:(h + 1) * head_dim],
                    stored_stretch_values[..., h * head_dim:(h + 1) * head_dim],
                ],
                axis=-1,
            )
            for h in range(kv_heads)
        ],
        axis=0,
    )
    flat = owners * rows * capacity
    index = (owner * rows + jnp.arange(rows, dtype=jnp.int32)[:, None]) * capacity + rank
    index = jnp.where(live, index, 0)
    slot_scale = all_scales[stretch_ids]
    placement = stretch_pos[:, :, None] + jnp.arange(span, dtype=jnp.int32)
    token_positions = cache_length + jnp.arange(tokens, dtype=jnp.int32)
    query_rot = (
        apply_rotary(
            queries.reshape(rows, tokens, q_heads, head_dim).astype(jnp.float32),
            token_positions[:, None],
        )
        * head_dim ** (-0.5)
    ).astype(jnp.bfloat16)
    query_rot = query_rot.reshape(rows, tokens, q_heads * head_dim)
    results = []
    for head in range(kv_heads):
        cols = slice(head * head_dim, (head + 1) * head_dim)
        last = head == kv_heads - 1
        new_keys = apply_rotary(
            fresh_keys[..., cols].astype(jnp.float32), token_positions
        ).astype(jnp.bfloat16)
        group_cols = slice(head * request_group * head_dim, (head + 1) * request_group * head_dim)
        query_head = query_rot[..., group_cols]
        if last:
            got_keys = lax.all_to_all(
                store[head][chosen][..., :head_dim], "stretch", split_axis=0, concat_axis=0, tiled=True
            )
            if results:
                got_keys, earlier = lax.optimization_barrier((got_keys, results[-1]))
                results[-1] = earlier
            got_vals = lax.all_to_all(
                store[head][chosen][..., head_dim:], "stretch", split_axis=0, concat_axis=0, tiled=True
            )
            raw_k = got_keys.reshape(flat, span, head_dim)[index]
        else:
            got = lax.all_to_all(store[head][chosen], "stretch", split_axis=0, concat_axis=0, tiled=True)
            if results:
                got, earlier = lax.optimization_barrier((got, results[-1]))
                results[-1] = earlier
            got = got.reshape(flat, span, 2 * head_dim)[index]
            raw_k = got[..., :head_dim]
        keys = raw_k.astype(jnp.float32) * slot_scale[:, :, 0, head][:, :, None, None]
        keys = apply_rotary(keys, placement).astype(jnp.bfloat16)
        keys_t = jnp.swapaxes(
            jnp.concatenate([keys.reshape(rows, cache_length, head_dim), new_keys], axis=1), 1, 2
        )
        top = None
        if last:
            probs, total = flash(
                query_head, keys_t, None, counts * span, request_group, cache_length, 0, None, 0, "prob"
            )
            got_vals, probs, total = lax.optimization_barrier((got_vals, probs, total))
            raw_v = got_vals.reshape(flat, span, head_dim)[index]
        else:
            raw_v = got[..., head_dim:]
        vals = raw_v.astype(jnp.float32) * slot_scale[:, :, 1, head][:, :, None, None]
        vals = vals.astype(jnp.bfloat16)
        values_all = jnp.concatenate(
            [vals.reshape(rows, cache_length, head_dim), fresh_values[..., cols]], axis=1
        )
        if last and results:
            mixed = jnp.einsum(
                "rgtl,rld->rtgd", probs, values_all, preferred_element_type=jnp.float32
            )
            mixed = mixed / total.reshape(rows, tokens, request_group, head_dim)
            mixed = mixed.astype(jnp.bfloat16).reshape(rows, tokens, request_group * head_dim)
            results.append(lax.dynamic_update_slice_in_dim(
                results[-1], mixed, head * request_group * head_dim, axis=2
            ))
            continue
        results.append(
            flash(
                query_head, keys_t, values_all, counts * span, request_group,
                cache_length, head * request_group, results[-1] if results else None, queries.shape[2],
                "both", top,
            )
        )
    return results[-1]


def flash_kernel(*refs, cache_length, chunk, heads, mode):
    bias_ref, q_ref, k_ref = refs[:3]
    v_ref = refs[3] if mode not in ("top", "prob") else None
    top_ref = refs[4] if mode == "mix" else None
    o_ref = refs[-1]
    pb_ref = refs[-2] if mode == "prob" else None
    tokens = q_ref.shape[0]
    lanes = 128
    new_mask = lax.broadcasted_iota(jnp.int32, (tokens, tokens), 1) <= lax.broadcasted_iota(
        jnp.int32, (tokens, tokens), 0
    )

    def fold(acc, s, op):
        for b in range(s.shape[1] // lanes):
            acc = op(acc, s[:, b * lanes:(b + 1) * lanes])
        return acc

    for head in range(heads):
        q = q_ref[:, head * lanes:(head + 1) * lanes]

        def scores(first, size):
            return lax.dot_general(
                q, k_ref[:, first:first + size], (((1,), (0,)), ((), ())),
                preferred_element_type=jnp.float32,
            )

        def masked(first, size):
            return scores(first, size) + bias_ref[:, first:first + size]

        fresh = jnp.where(new_mask, scores(cache_length, tokens), -1e30)
        if mode == "mix":
            top = top_ref[:, head * lanes:(head + 1) * lanes]
        else:
            top = fold(jnp.full((tokens, lanes), -1e30, jnp.float32), fresh, jnp.maximum)
            for first in range(0, cache_length, chunk):
                top = fold(top, masked(first, chunk), jnp.maximum)
            top = jnp.max(top, axis=1, keepdims=True)
        if mode == "top":
            o_ref[:, head * lanes:(head + 1) * lanes] = jnp.broadcast_to(top, (tokens, lanes))
            continue

        def mix(s, first, size):
            if mode == "mix":
                p = jnp.exp(s - jnp.tile(top, (1, size // lanes)))
            else:
                p = jnp.exp(s - top)
            return p, lax.dot_general(
                p.astype(jnp.bfloat16), v_ref[first:first + size, :], (((1,), (0,)), ((), ())),
                preferred_element_type=jnp.float32,
            )

        if mode == "prob":
            p = jnp.exp(fresh - top)
            pb_ref[head, :, cache_length:cache_length + tokens] = p.astype(pb_ref.dtype)
            total = fold(jnp.zeros((tokens, lanes), jnp.float32), p, jnp.add)
            for first in range(0, cache_length, chunk):
                p = jnp.exp(masked(first, chunk) - top)
                pb_ref[head, :, first:first + chunk] = p.astype(pb_ref.dtype)
                total = fold(total, p, jnp.add)
            total = jnp.sum(total, axis=1, keepdims=True)
            o_ref[:, head * lanes:(head + 1) * lanes] = jnp.broadcast_to(total, (tokens, lanes))
            continue

        p, acc = mix(fresh, cache_length, tokens)
        total = fold(jnp.zeros((tokens, lanes), jnp.float32), p, jnp.add)
        for first in range(0, cache_length, chunk):
            p, part = mix(masked(first, chunk), first, chunk)
            total = fold(total, p, jnp.add)
            acc = acc + part
        total = jnp.sum(total, axis=1, keepdims=True)
        o_ref[:, head * lanes:(head + 1) * lanes] = (acc / total).astype(o_ref.dtype)


CHUNK = 512
HEADS = 4


def flash(query_rot, keys_t, values_all, live, request_group, cache_length, offset, into, out_width,
          mode="both", top=None):
    rows, tokens, q_width = query_rot.shape
    head_dim, length = keys_t.shape[1:]
    kv_heads = 1
    chunk = CHUNK if cache_length % CHUNK == 0 else 128
    heads = HEADS
    bias = jnp.where(
        jnp.arange(cache_length, dtype=jnp.int32)[None, :] < live[:, None], 0.0, -1e30
    ).astype(jnp.float32)[:, None, :]
    kernel = functools.partial(
        flash_kernel, cache_length=cache_length, chunk=chunk, heads=heads, mode=mode
    )
    per = request_group // heads
    block = offset // heads
    in_specs = [
        pl.BlockSpec((None, 1, cache_length), lambda r, h, g: (r, 0, 0)),
        pl.BlockSpec((None, tokens, head_dim * heads), lambda r, h, g: (r, 0, h * per + g)),
        pl.BlockSpec((None, head_dim, length), lambda r, h, g: (r, h, 0)),
    ]
    operands = [bias, query_rot, keys_t]
    if mode not in ("top", "prob"):
        in_specs.append(pl.BlockSpec((None, length, head_dim), lambda r, h, g: (r, 0, h)))
        operands.append(values_all)
    if mode == "mix":
        in_specs.append(pl.BlockSpec((None, tokens, head_dim * heads), lambda r, h, g: (r, 0, h * per + g)))
        operands.append(top)
    aliases = {}
    if into is not None:
        in_specs.append(pl.BlockSpec(memory_space=pl.ANY))
        aliases = {len(operands): 0}
        operands.append(into)
    if mode == "prob":
        out_specs = [
            pl.BlockSpec((None, heads, tokens, length), lambda r, h, g: (r, h * per + g, 0, 0)),
            pl.BlockSpec((None, tokens, head_dim * heads), lambda r, h, g: (r, 0, h * per + g)),
        ]
        out_shape = [
            jax.ShapeDtypeStruct((rows, q_width // head_dim, tokens, length), jnp.bfloat16),
            jax.ShapeDtypeStruct((rows, tokens, q_width), jnp.float32),
        ]
    elif mode == "top":
        out_specs = pl.BlockSpec((None, tokens, head_dim * heads), lambda r, h, g: (r, 0, h * per + g))
        out_shape = jax.ShapeDtypeStruct((rows, tokens, q_width), jnp.float32)
    else:
        out_specs = pl.BlockSpec(
            (None, tokens, head_dim * heads), lambda r, h, g: (r, 0, block + h * per + g)
        )
        out_shape = jax.ShapeDtypeStruct((rows, tokens, out_width), jnp.bfloat16)
    passes = {"both": 3, "top": 1, "mix": 2, "prob": 2}[mode]
    return pl.pallas_call(
        kernel,
        grid=(rows, kv_heads, per),
        in_specs=in_specs,
        out_specs=out_specs,
        out_shape=out_shape,
        input_output_aliases=aliases,
        cost_estimate=pl.CostEstimate(
            flops=2 * passes * rows * tokens * q_width * length,
            transcendentals=rows * tokens * (q_width // head_dim) * length,
            bytes_accessed=2 * rows * (2 * tokens * q_width + 2 * length * head_dim),
        ),
    )(*operands)


def solution(mesh):
    return jax.shard_map(
        shards,
        mesh=mesh,
        in_specs=(
            P(("grp", "stretch"), None, "req"),
            P(("grp", "stretch"), None, "req"),
            P(("grp", "stretch"), None, "req"),
            P(("grp", "stretch"), None, "req"),
            P(("grp", "stretch"), None, "req"),
            P(("grp", "stretch"), None, "req"),
            P(("grp", "stretch"), None),
            P(("grp", "stretch")),
            P(("grp", "stretch"), None),
        ),
        out_specs=P(("grp", "stretch"), None, "req"),
        check_vma=False,
    )
```

```python
import functools

import jax
import jax.numpy as jnp
from jax import lax
from jax.experimental import pallas as pl
from jax.experimental.pallas import tpu as pltpu
from jax.sharding import PartitionSpec as P

rope_base = 500000.0


def apply_rotary(x, pos):
    half = x.shape[-1] // 2
    inv = rope_base ** (-(jnp.arange(half, dtype=jnp.float32) * 2.0 / x.shape[-1]))
    angle = pos.astype(jnp.float32)[..., None] * inv
    cosine = jnp.cos(angle)
    sine = jnp.sin(angle)
    first = x[..., :half]
    second = x[..., half:]
    return jnp.concatenate(
        [first * cosine - second * sine, second * cosine + first * sine], axis=-1
    )


def slot_tables(slot_stretch_ids, counts, positions, owners, capacity, per_owner):
    rows, slots = slot_stretch_ids.shape
    owner = slot_stretch_ids // per_owner
    local = slot_stretch_ids % per_owner
    slot_iota = jnp.arange(slots, dtype=jnp.int32)
    live = slot_iota[None, :] < counts[:, None]
    same = owner[:, :, None] == owner[:, None, :]
    earlier = slot_iota[:, None] < slot_iota[None, :]
    rank = jnp.sum((same & earlier[None, :, :] & live[:, :, None]).astype(jnp.int32), axis=1)
    target = owner * capacity + rank
    hits = (
        target[:, :, None] == jnp.arange(owners * capacity, dtype=jnp.int32)[None, None, :]
    ) & live[:, :, None]
    hits = hits.astype(jnp.int32)
    local_table = jnp.sum(hits * (local + 1)[:, :, None], axis=1) - 1
    place_table = jnp.sum(hits * positions[:, :, None], axis=1)
    return (
        local_table.reshape(rows, owners, capacity),
        place_table.reshape(rows, owners, capacity),
        owner,
        rank,
        live,
    )


def shards(
    queries,
    fresh_keys,
    fresh_values,
    stored_stretch_keys,
    stored_stretch_values,
    scales,
    stretch_ids,
    counts,
    stretch_pos,
):
    owners = lax.axis_size("stretch")
    rows, slots = stretch_ids.shape
    per_owner, span, width = stored_stretch_keys.shape
    kv_heads = scales.shape[2]
    head_dim = width // kv_heads
    q_heads = queries.shape[2] // head_dim
    request_group = q_heads // kv_heads
    tokens = queries.shape[1]
    capacity = 2 * slots // owners
    cache_length = slots * span
    mine = slot_tables(stretch_ids, counts, stretch_pos, owners, capacity, per_owner)
    owner, rank, live = (mine[2], mine[3], mine[4])
    scale_code = (scales.astype(jnp.float32) * 65536.0).astype(jnp.int32).reshape(1, 1, -1)
    requests = jnp.concatenate(
        [
            jnp.transpose(mine[0], (1, 0, 2)),
            jnp.broadcast_to(scale_code, (owners, rows, scale_code.shape[2])),
        ],
        axis=2,
    )
    answers = lax.all_to_all(requests, "stretch", split_axis=0, concat_axis=0, tiled=True)
    wanted = answers[:, :, :capacity]
    chosen = jnp.maximum(wanted, 0)
    all_scales = (answers[:, 0, capacity:].astype(jnp.float32) * (1.0 / 65536.0)).reshape(
        owners * per_owner, 2, scales.shape[2]
    )
    store = jnp.stack(
        [
            jnp.concatenate(
                [
                    stored_stretch_keys[..., h * head_dim:(h + 1) * head_dim],
                    stored_stretch_values[..., h * head_dim:(h + 1) * head_dim],
                ],
                axis=-1,
            )
            for h in range(kv_heads)
        ],
        axis=0,
    )
    flat = owners * rows * capacity
    me = lax.axis_index("stretch")
    order = (me + jnp.arange(owners, dtype=jnp.int32)) % owners
    chosen = jnp.take(chosen, order, axis=0)
    source_shift = (me - owner) % owners
    index = (source_shift * rows + jnp.arange(rows, dtype=jnp.int32)[:, None]) * capacity + rank
    index = jnp.where(live, index, 0)
    slot_scale = all_scales[stretch_ids]
    placement = stretch_pos[:, :, None] + jnp.arange(span, dtype=jnp.int32)
    token_positions = cache_length + jnp.arange(tokens, dtype=jnp.int32)
    query_rot = (
        apply_rotary(
            queries.reshape(rows, tokens, q_heads, head_dim).astype(jnp.float32),
            token_positions[:, None],
        )
        * head_dim ** (-0.5)
    ).astype(jnp.bfloat16)
    query_rot = query_rot.reshape(rows, tokens, q_heads * head_dim)
    def swap(by_shift, after=None):
        if after is not None:
            by_shift, after = lax.optimization_barrier((by_shift, after))
        pieces = [by_shift[0]]
        for shift in range(1, owners):
            pairs = [(i, (i + shift) % owners) for i in range(owners)]
            pieces.append(lax.ppermute(by_shift[shift], "stretch", pairs))
        return jnp.stack(pieces, axis=0)

    results = []
    for head in range(kv_heads):
        cols = slice(head * head_dim, (head + 1) * head_dim)
        last = head == kv_heads - 1
        new_keys = apply_rotary(
            fresh_keys[..., cols].astype(jnp.float32), token_positions
        ).astype(jnp.bfloat16)
        group_cols = slice(head * request_group * head_dim, (head + 1) * request_group * head_dim)
        query_head = query_rot[..., group_cols]
        if last:
            got_keys = swap(store[head][chosen][..., :head_dim], previous)
            if results:
                got_keys, earlier = lax.optimization_barrier((got_keys, results[-1]))
                results[-1] = earlier
            got_vals = swap(store[head][chosen][..., head_dim:], got_keys)
            raw_k = got_keys.reshape(flat, span, head_dim)[index]
        else:
            got = swap(store[head][chosen])
            previous = got
            if results:
                got, earlier = lax.optimization_barrier((got, results[-1]))
                results[-1] = earlier
            got = got.reshape(flat, span, 2 * head_dim)[index]
            raw_k = got[..., :head_dim]
        keys = raw_k.astype(jnp.float32) * slot_scale[:, :, 0, head][:, :, None, None]
        keys = apply_rotary(keys, placement).astype(jnp.bfloat16)
        keys_t = jnp.swapaxes(
            jnp.concatenate([keys.reshape(rows, cache_length, head_dim), new_keys], axis=1), 1, 2
        )
        top = None
        if last:
            top = flash(
                query_head, keys_t, None, counts * span, request_group, cache_length, 0, None, 0, "top"
            )
            got_vals, top = lax.optimization_barrier((got_vals, top))
            raw_v = got_vals.reshape(flat, span, head_dim)[index]
        else:
            raw_v = got[..., head_dim:]
        vals = raw_v.astype(jnp.float32) * slot_scale[:, :, 1, head][:, :, None, None]
        vals = vals.astype(jnp.bfloat16)
        values_all = jnp.concatenate(
            [vals.reshape(rows, cache_length, head_dim), fresh_values[..., cols]], axis=1
        )
        results.append(
            flash(
                query_head, keys_t, values_all, counts * span, request_group,
                cache_length, head * request_group, results[-1] if results else None, queries.shape[2],
                "mix" if last else "both", top,
            )
        )
    return results[-1]


def flash_kernel(*refs, cache_length, chunk, heads, mode):
    bias_ref, q_ref, k_ref = refs[:3]
    v_ref = refs[3] if mode != "top" else None
    top_ref = refs[4] if mode == "mix" else None
    o_ref = refs[-1]
    tokens = q_ref.shape[0]
    lanes = 128
    new_mask = lax.broadcasted_iota(jnp.int32, (tokens, tokens), 1) <= lax.broadcasted_iota(
        jnp.int32, (tokens, tokens), 0
    )

    def fold(acc, s, op):
        for b in range(s.shape[1] // lanes):
            acc = op(acc, s[:, b * lanes:(b + 1) * lanes])
        return acc

    for head in range(heads):
        q = q_ref[:, head * lanes:(head + 1) * lanes]

        def scores(first, size):
            return lax.dot_general(
                q, k_ref[:, first:first + size], (((1,), (0,)), ((), ())),
                preferred_element_type=jnp.float32,
            )

        def masked(first, size):
            return scores(first, size) + bias_ref[:, first:first + size]

        fresh = jnp.where(new_mask, scores(cache_length, tokens), -1e30)
        if mode == "mix":
            top = top_ref[:, head * lanes:(head + 1) * lanes]
        else:
            top = fold(jnp.full((tokens, lanes), -1e30, jnp.float32), fresh, jnp.maximum)
            for first in range(0, cache_length, chunk):
                top = fold(top, masked(first, chunk), jnp.maximum)
            top = jnp.max(top, axis=1, keepdims=True)
        if mode == "top":
            o_ref[:, head * lanes:(head + 1) * lanes] = jnp.broadcast_to(top, (tokens, lanes))
            continue

        def mix(s, first, size):
            if mode == "mix":
                p = jnp.exp(s - jnp.tile(top, (1, size // lanes)))
            else:
                p = jnp.exp(s - top)
            return p, lax.dot_general(
                p.astype(jnp.bfloat16), v_ref[first:first + size, :], (((1,), (0,)), ((), ())),
                preferred_element_type=jnp.float32,
            )

        p, acc = mix(fresh, cache_length, tokens)
        total = fold(jnp.zeros((tokens, lanes), jnp.float32), p, jnp.add)
        for first in range(0, cache_length, chunk):
            p, part = mix(masked(first, chunk), first, chunk)
            total = fold(total, p, jnp.add)
            acc = acc + part
        total = jnp.sum(total, axis=1, keepdims=True)
        o_ref[:, head * lanes:(head + 1) * lanes] = (acc / total).astype(o_ref.dtype)


CHUNK = 512
HEADS = 4


def flash(query_rot, keys_t, values_all, live, request_group, cache_length, offset, into, out_width,
          mode="both", top=None):
    rows, tokens, q_width = query_rot.shape
    head_dim, length = keys_t.shape[1:]
    kv_heads = 1
    chunk = CHUNK if cache_length % CHUNK == 0 else 128
    heads = HEADS
    bias = jnp.where(
        jnp.arange(cache_length, dtype=jnp.int32)[None, :] < live[:, None], 0.0, -1e30
    ).astype(jnp.float32)[:, None, :]
    kernel = functools.partial(
        flash_kernel, cache_length=cache_length, chunk=chunk, heads=heads, mode=mode
    )
    per = request_group // heads
    block = offset // heads
    in_specs = [
        pl.BlockSpec((None, 1, cache_length), lambda r, h, g: (r, 0, 0)),
        pl.BlockSpec((None, tokens, head_dim * heads), lambda r, h, g: (r, 0, h * per + g)),
        pl.BlockSpec((None, head_dim, length), lambda r, h, g: (r, h, 0)),
    ]
    operands = [bias, query_rot, keys_t]
    if mode != "top":
        in_specs.append(pl.BlockSpec((None, length, head_dim), lambda r, h, g: (r, 0, h)))
        operands.append(values_all)
    if mode == "mix":
        in_specs.append(pl.BlockSpec((None, tokens, head_dim * heads), lambda r, h, g: (r, 0, h * per + g)))
        operands.append(top)
    aliases = {}
    if into is not None:
        in_specs.append(pl.BlockSpec(memory_space=pl.ANY))
        aliases = {len(operands): 0}
        operands.append(into)
    if mode == "top":
        out_specs = pl.BlockSpec((None, tokens, head_dim * heads), lambda r, h, g: (r, 0, h * per + g))
        out_shape = jax.ShapeDtypeStruct((rows, tokens, q_width), jnp.float32)
    else:
        out_specs = pl.BlockSpec(
            (None, tokens, head_dim * heads), lambda r, h, g: (r, 0, block + h * per + g)
        )
        out_shape = jax.ShapeDtypeStruct((rows, tokens, out_width), jnp.bfloat16)
    passes = {"both": 3, "top": 1, "mix": 2}[mode]
    return pl.pallas_call(
        kernel,
        grid=(rows, kv_heads, per),
        in_specs=in_specs,
        out_specs=out_specs,
        out_shape=out_shape,
        input_output_aliases=aliases,
        cost_estimate=pl.CostEstimate(
            flops=2 * passes * rows * tokens * q_width * length,
            transcendentals=rows * tokens * (q_width // head_dim) * length,
            bytes_accessed=2 * rows * (2 * tokens * q_width + 2 * length * head_dim),
        ),
    )(*operands)


def solution(mesh):
    return jax.shard_map(
        shards,
        mesh=mesh,
        in_specs=(
            P(("grp", "stretch"), None, "req"),
            P(("grp", "stretch"), None, "req"),
            P(("grp", "stretch"), None, "req"),
            P(("grp", "stretch"), None, "req"),
            P(("grp", "stretch"), None, "req"),
            P(("grp", "stretch"), None, "req"),
            P(("grp", "stretch"), None),
            P(("grp", "stretch")),
            P(("grp", "stretch"), None),
        ),
        out_specs=P(("grp", "stretch"), None, "req"),
        check_vma=False,
    )
```

```python
import functools

import jax
import jax.numpy as jnp
from jax import lax
from jax.experimental import pallas as pl
from jax.experimental.pallas import tpu as pltpu
from jax.sharding import PartitionSpec as P

rope_base = 500000.0


def apply_rotary(x, pos):
    half = x.shape[-1] // 2
    inv = rope_base ** (-(jnp.arange(half, dtype=jnp.float32) * 2.0 / x.shape[-1]))
    angle = pos.astype(jnp.float32)[..., None] * inv
    cosine = jnp.cos(angle)
    sine = jnp.sin(angle)
    first = x[..., :half]
    second = x[..., half:]
    return jnp.concatenate(
        [first * cosine - second * sine, second * cosine + first * sine], axis=-1
    )


def slot_tables(slot_stretch_ids, counts, positions, owners, capacity, per_owner):
    rows, slots = slot_stretch_ids.shape
    owner = slot_stretch_ids // per_owner
    local = slot_stretch_ids % per_owner
    slot_iota = jnp.arange(slots, dtype=jnp.int32)
    live = slot_iota[None, :] < counts[:, None]
    same = owner[:, :, None] == owner[:, None, :]
    earlier = slot_iota[:, None] < slot_iota[None, :]
    rank = jnp.sum((same & earlier[None, :, :] & live[:, :, None]).astype(jnp.int32), axis=1)
    target = owner * capacity + rank
    hits = (
        target[:, :, None] == jnp.arange(owners * capacity, dtype=jnp.int32)[None, None, :]
    ) & live[:, :, None]
    hits = hits.astype(jnp.int32)
    local_table = jnp.sum(hits * (local + 1)[:, :, None], axis=1) - 1
    place_table = jnp.sum(hits * positions[:, :, None], axis=1)
    return (
        local_table.reshape(rows, owners, capacity),
        place_table.reshape(rows, owners, capacity),
        owner,
        rank,
        live,
    )


def shards(
    queries,
    fresh_keys,
    fresh_values,
    stored_stretch_keys,
    stored_stretch_values,
    scales,
    stretch_ids,
    counts,
    stretch_pos,
):
    owners = lax.axis_size("stretch")
    rows, slots = stretch_ids.shape
    per_owner, span, width = stored_stretch_keys.shape
    kv_heads = scales.shape[2]
    head_dim = width // kv_heads
    q_heads = queries.shape[2] // head_dim
    request_group = q_heads // kv_heads
    tokens = queries.shape[1]
    capacity = 2 * slots // owners
    cache_length = slots * span
    mine = slot_tables(stretch_ids, counts, stretch_pos, owners, capacity, per_owner)
    owner, rank, live = (mine[2], mine[3], mine[4])
    scale_code = (scales.astype(jnp.float32) * 65536.0).astype(jnp.int32).reshape(1, 1, -1)
    requests = jnp.concatenate(
        [
            jnp.transpose(mine[0], (1, 0, 2)),
            jnp.broadcast_to(scale_code, (owners, rows, scale_code.shape[2])),
        ],
        axis=2,
    )
    answers = lax.all_to_all(requests, "stretch", split_axis=0, concat_axis=0, tiled=True)
    wanted = answers[:, :, :capacity]
    chosen = jnp.maximum(wanted, 0)
    all_scales = (answers[:, 0, capacity:].astype(jnp.float32) * (1.0 / 65536.0)).reshape(
        owners * per_owner, 2, scales.shape[2]
    )
    store = jnp.stack(
        [
            jnp.concatenate(
                [
                    stored_stretch_keys[..., h * head_dim:(h + 1) * head_dim],
                    stored_stretch_values[..., h * head_dim:(h + 1) * head_dim],
                ],
                axis=-1,
            )
            for h in range(kv_heads)
        ],
        axis=0,
    )
    flat = owners * rows * capacity
    index = (owner * rows + jnp.arange(rows, dtype=jnp.int32)[:, None]) * capacity + rank
    index = jnp.where(live, index, 0)
    slot_scale = all_scales[stretch_ids]
    placement = stretch_pos[:, :, None] + jnp.arange(span, dtype=jnp.int32)
    token_positions = cache_length + jnp.arange(tokens, dtype=jnp.int32)
    query_rot = (
        apply_rotary(
            queries.reshape(rows, tokens, q_heads, head_dim).astype(jnp.float32),
            token_positions[:, None],
        )
        * head_dim ** (-0.5)
    ).astype(jnp.bfloat16)
    query_rot = query_rot.reshape(rows, tokens, q_heads * head_dim)
    early = lax.all_to_all(
        jnp.concatenate(
            [store[h][chosen] for h in range(kv_heads - 1)]
            + [store[kv_heads - 1][chosen][..., :head_dim]],
            axis=-1,
        ),
        "stretch", split_axis=0, concat_axis=0, tiled=True,
    )
    late = lax.all_to_all(
        store[kv_heads - 1][chosen][..., head_dim:], "stretch", split_axis=0, concat_axis=0, tiled=True
    )
    results = []
    for head in range(kv_heads):
        cols = slice(head * head_dim, (head + 1) * head_dim)
        last = head == kv_heads - 1
        new_keys = apply_rotary(
            fresh_keys[..., cols].astype(jnp.float32), token_positions
        ).astype(jnp.bfloat16)
        group_cols = slice(head * request_group * head_dim, (head + 1) * request_group * head_dim)
        query_head = query_rot[..., group_cols]
        if last:
            got_keys = early[..., 2 * head * head_dim:]
            if results:
                got_keys, earlier = lax.optimization_barrier((got_keys, results[-1]))
                results[-1] = earlier
            got_vals = late
            raw_k = got_keys.reshape(flat, span, head_dim)[index]
        else:
            got = early[..., 2 * head * head_dim:2 * (head + 1) * head_dim]
            if results:
                got, earlier = lax.optimization_barrier((got, results[-1]))
                results[-1] = earlier
            got = got.reshape(flat, span, 2 * head_dim)[index]
            raw_k = got[..., :head_dim]
        keys = raw_k.astype(jnp.float32) * slot_scale[:, :, 0, head][:, :, None, None]
        keys = apply_rotary(keys, placement).astype(jnp.bfloat16)
        keys_t = jnp.swapaxes(
            jnp.concatenate([keys.reshape(rows, cache_length, head_dim), new_keys], axis=1), 1, 2
        )
        top = None
        if last:
            top = flash(
                query_head, keys_t, None, counts * span, request_group, cache_length, 0, None, 0, "top"
            )
            got_vals, top = lax.optimization_barrier((got_vals, top))
            raw_v = got_vals.reshape(flat, span, head_dim)[index]
        else:
            raw_v = got[..., head_dim:]
        vals = raw_v.astype(jnp.float32) * slot_scale[:, :, 1, head][:, :, None, None]
        vals = vals.astype(jnp.bfloat16)
        values_all = jnp.concatenate(
            [vals.reshape(rows, cache_length, head_dim), fresh_values[..., cols]], axis=1
        )
        results.append(
            flash(
                query_head, keys_t, values_all, counts * span, request_group,
                cache_length, head * request_group, results[-1] if results else None, queries.shape[2],
                "mix" if last else "both", top,
            )
        )
    return results[-1]


def flash_kernel(*refs, cache_length, chunk, heads, mode):
    bias_ref, q_ref, k_ref = refs[:3]
    v_ref = refs[3] if mode != "top" else None
    top_ref = refs[4] if mode == "mix" else None
    o_ref = refs[-1]
    tokens = q_ref.shape[0]
    lanes = 128
    new_mask = lax.broadcasted_iota(jnp.int32, (tokens, tokens), 1) <= lax.broadcasted_iota(
        jnp.int32, (tokens, tokens), 0
    )

    def fold(acc, s, op):
        for b in range(s.shape[1] // lanes):
            acc = op(acc, s[:, b * lanes:(b + 1) * lanes])
        return acc

    for head in range(heads):
        q = q_ref[:, head * lanes:(head + 1) * lanes]

        def scores(first, size):
            return lax.dot_general(
                q, k_ref[:, first:first + size], (((1,), (0,)), ((), ())),
                preferred_element_type=jnp.float32,
            )

        def masked(first, size):
            return scores(first, size) + bias_ref[:, first:first + size]

        fresh = jnp.where(new_mask, scores(cache_length, tokens), -1e30)
        if mode == "mix":
            top = top_ref[:, head * lanes:(head + 1) * lanes]
        else:
            top = fold(jnp.full((tokens, lanes), -1e30, jnp.float32), fresh, jnp.maximum)
            for first in range(0, cache_length, chunk):
                top = fold(top, masked(first, chunk), jnp.maximum)
            top = jnp.max(top, axis=1, keepdims=True)
        if mode == "top":
            o_ref[:, head * lanes:(head + 1) * lanes] = jnp.broadcast_to(top, (tokens, lanes))
            continue

        def mix(s, first, size):
            if mode == "mix":
                p = jnp.exp(s - jnp.tile(top, (1, size // lanes)))
            else:
                p = jnp.exp(s - top)
            return p, lax.dot_general(
                p.astype(jnp.bfloat16), v_ref[first:first + size, :], (((1,), (0,)), ((), ())),
                preferred_element_type=jnp.float32,
            )

        p, acc = mix(fresh, cache_length, tokens)
        total = fold(jnp.zeros((tokens, lanes), jnp.float32), p, jnp.add)
        for first in range(0, cache_length, chunk):
            p, part = mix(masked(first, chunk), first, chunk)
            total = fold(total, p, jnp.add)
            acc = acc + part
        total = jnp.sum(total, axis=1, keepdims=True)
        o_ref[:, head * lanes:(head + 1) * lanes] = (acc / total).astype(o_ref.dtype)


CHUNK = 512
HEADS = 4


def flash(query_rot, keys_t, values_all, live, request_group, cache_length, offset, into, out_width,
          mode="both", top=None):
    rows, tokens, q_width = query_rot.shape
    head_dim, length = keys_t.shape[1:]
    kv_heads = 1
    chunk = CHUNK if cache_length % CHUNK == 0 else 128
    heads = HEADS
    bias = jnp.where(
        jnp.arange(cache_length, dtype=jnp.int32)[None, :] < live[:, None], 0.0, -1e30
    ).astype(jnp.float32)[:, None, :]
    kernel = functools.partial(
        flash_kernel, cache_length=cache_length, chunk=chunk, heads=heads, mode=mode
    )
    per = request_group // heads
    block = offset // heads
    in_specs = [
        pl.BlockSpec((None, 1, cache_length), lambda r, h, g: (r, 0, 0)),
        pl.BlockSpec((None, tokens, head_dim * heads), lambda r, h, g: (r, 0, h * per + g)),
        pl.BlockSpec((None, head_dim, length), lambda r, h, g: (r, h, 0)),
    ]
    operands = [bias, query_rot, keys_t]
    if mode != "top":
        in_specs.append(pl.BlockSpec((None, length, head_dim), lambda r, h, g: (r, 0, h)))
        operands.append(values_all)
    if mode == "mix":
        in_specs.append(pl.BlockSpec((None, tokens, head_dim * heads), lambda r, h, g: (r, 0, h * per + g)))
        operands.append(top)
    aliases = {}
    if into is not None:
        in_specs.append(pl.BlockSpec(memory_space=pl.ANY))
        aliases = {len(operands): 0}
        operands.append(into)
    if mode == "top":
        out_specs = pl.BlockSpec((None, tokens, head_dim * heads), lambda r, h, g: (r, 0, h * per + g))
        out_shape = jax.ShapeDtypeStruct((rows, tokens, q_width), jnp.float32)
    else:
        out_specs = pl.BlockSpec(
            (None, tokens, head_dim * heads), lambda r, h, g: (r, 0, block + h * per + g)
        )
        out_shape = jax.ShapeDtypeStruct((rows, tokens, out_width), jnp.bfloat16)
    passes = {"both": 3, "top": 1, "mix": 2}[mode]
    return pl.pallas_call(
        kernel,
        grid=(rows, kv_heads, per),
        in_specs=in_specs,
        out_specs=out_specs,
        out_shape=out_shape,
        input_output_aliases=aliases,
        cost_estimate=pl.CostEstimate(
            flops=2 * passes * rows * tokens * q_width * length,
            transcendentals=rows * tokens * (q_width // head_dim) * length,
            bytes_accessed=2 * rows * (2 * tokens * q_width + 2 * length * head_dim),
        ),
    )(*operands)


def solution(mesh):
    return jax.shard_map(
        shards,
        mesh=mesh,
        in_specs=(
            P(("grp", "stretch"), None, "req"),
            P(("grp", "stretch"), None, "req"),
            P(("grp", "stretch"), None, "req"),
            P(("grp", "stretch"), None, "req"),
            P(("grp", "stretch"), None, "req"),
            P(("grp", "stretch"), None, "req"),
            P(("grp", "stretch"), None),
            P(("grp", "stretch")),
            P(("grp", "stretch"), None),
        ),
        out_specs=P(("grp", "stretch"), None, "req"),
        check_vma=False,
    )
```

```python
import functools

import jax
import jax.numpy as jnp
from jax import lax
from jax.experimental import pallas as pl
from jax.experimental.pallas import tpu as pltpu
from jax.sharding import PartitionSpec as P

rope_base = 500000.0


def apply_rotary(x, pos):
    half = x.shape[-1] // 2
    inv = rope_base ** (-(jnp.arange(half, dtype=jnp.float32) * 2.0 / x.shape[-1]))
    angle = pos.astype(jnp.float32)[..., None] * inv
    cosine = jnp.cos(angle)
    sine = jnp.sin(angle)
    first = x[..., :half]
    second = x[..., half:]
    return jnp.concatenate(
        [first * cosine - second * sine, second * cosine + first * sine], axis=-1
    )


def slot_tables(slot_stretch_ids, counts, positions, owners, capacity, per_owner):
    rows, slots = slot_stretch_ids.shape
    owner = slot_stretch_ids // per_owner
    local = slot_stretch_ids % per_owner
    slot_iota = jnp.arange(slots, dtype=jnp.int32)
    live = slot_iota[None, :] < counts[:, None]
    same = owner[:, :, None] == owner[:, None, :]
    earlier = slot_iota[:, None] < slot_iota[None, :]
    rank = jnp.sum((same & earlier[None, :, :] & live[:, :, None]).astype(jnp.int32), axis=1)
    target = owner * capacity + rank
    hits = (
        target[:, :, None] == jnp.arange(owners * capacity, dtype=jnp.int32)[None, None, :]
    ) & live[:, :, None]
    hits = hits.astype(jnp.int32)
    local_table = jnp.sum(hits * (local + 1)[:, :, None], axis=1) - 1
    place_table = jnp.sum(hits * positions[:, :, None], axis=1)
    return (
        local_table.reshape(rows, owners, capacity),
        place_table.reshape(rows, owners, capacity),
        owner,
        rank,
        live,
    )


def shards(
    queries,
    fresh_keys,
    fresh_values,
    stored_stretch_keys,
    stored_stretch_values,
    scales,
    stretch_ids,
    counts,
    stretch_pos,
):
    owners = lax.axis_size("stretch")
    rows, slots = stretch_ids.shape
    per_owner, span, width = stored_stretch_keys.shape
    kv_heads = scales.shape[2]
    head_dim = width // kv_heads
    q_heads = queries.shape[2] // head_dim
    request_group = q_heads // kv_heads
    tokens = queries.shape[1]
    capacity = 2 * slots // owners
    cache_length = slots * span
    mine = slot_tables(stretch_ids, counts, stretch_pos, owners, capacity, per_owner)
    owner, rank, live = (mine[2], mine[3], mine[4])
    scale_code = (scales.astype(jnp.float32) * 65536.0).astype(jnp.int32).reshape(1, 1, -1)
    requests = jnp.concatenate(
        [
            jnp.transpose(mine[0], (1, 0, 2)),
            jnp.broadcast_to(scale_code, (owners, rows, scale_code.shape[2])),
        ],
        axis=2,
    )
    answers = lax.all_to_all(requests, "stretch", split_axis=0, concat_axis=0, tiled=True)
    wanted = answers[:, :, :capacity]
    chosen = jnp.maximum(wanted, 0)
    all_scales = (answers[:, 0, capacity:].astype(jnp.float32) * (1.0 / 65536.0)).reshape(
        owners * per_owner, 2, scales.shape[2]
    )
    store = jnp.stack(
        [
            jnp.concatenate(
                [
                    stored_stretch_keys[..., h * head_dim:(h + 1) * head_dim],
                    stored_stretch_values[..., h * head_dim:(h + 1) * head_dim],
                ],
                axis=-1,
            )
            for h in range(kv_heads)
        ],
        axis=0,
    )
    flat = owners * rows * capacity
    index = (owner * rows + jnp.arange(rows, dtype=jnp.int32)[:, None]) * capacity + rank
    index = jnp.where(live, index, 0)
    slot_scale = all_scales[stretch_ids]
    placement = stretch_pos[:, :, None] + jnp.arange(span, dtype=jnp.int32)
    token_positions = cache_length + jnp.arange(tokens, dtype=jnp.int32)
    query_rot = (
        apply_rotary(
            queries.reshape(rows, tokens, q_heads, head_dim).astype(jnp.float32),
            token_positions[:, None],
        )
        * head_dim ** (-0.5)
    ).astype(jnp.bfloat16)
    query_rot = query_rot.reshape(rows, tokens, q_heads * head_dim)
    results = []
    for head in range(kv_heads):
        cols = slice(head * head_dim, (head + 1) * head_dim)
        last = head == kv_heads - 1
        new_keys = apply_rotary(
            fresh_keys[..., cols].astype(jnp.float32), token_positions
        ).astype(jnp.bfloat16)
        group_cols = slice(head * request_group * head_dim, (head + 1) * request_group * head_dim)
        query_head = query_rot[..., group_cols]
        if last:
            got_keys = lax.all_to_all(
                store[head][chosen][..., :head_dim], "stretch", split_axis=0, concat_axis=0, tiled=True
            )
            if results:
                got_keys, earlier = lax.optimization_barrier((got_keys, results[-1]))
                results[-1] = earlier
            got_vals = lax.all_to_all(
                store[head][chosen][..., head_dim:], "stretch", split_axis=0, concat_axis=0, tiled=True
            )
            raw_k = got_keys.reshape(flat, span, head_dim)[index]
        else:
            got = lax.all_to_all(store[head][chosen], "stretch", split_axis=0, concat_axis=0, tiled=True)
            if results:
                got, earlier = lax.optimization_barrier((got, results[-1]))
                results[-1] = earlier
            got = got.reshape(flat, span, 2 * head_dim)[index]
            raw_k = got[..., :head_dim]
        keys = raw_k.astype(jnp.float32) * slot_scale[:, :, 0, head][:, :, None, None]
        keys = apply_rotary(keys, placement).astype(jnp.bfloat16)
        keys_t = jnp.swapaxes(
            jnp.concatenate([keys.reshape(rows, cache_length, head_dim), new_keys], axis=1), 1, 2
        )
        top = None
        if last:
            probs, total = flash(
                query_head, keys_t, None, counts * span, request_group, cache_length, 0, None, 0, "prob"
            )
            got_vals, probs, total = lax.optimization_barrier((got_vals, probs, total))
            raw_v = got_vals.reshape(flat, span, head_dim)[index]
        else:
            raw_v = got[..., head_dim:]
        vals = raw_v.astype(jnp.float32) * slot_scale[:, :, 1, head][:, :, None, None]
        vals = vals.astype(jnp.bfloat16)
        values_all = jnp.concatenate(
            [vals.reshape(rows, cache_length, head_dim), fresh_values[..., cols]], axis=1
        )
        if last and results:
            results.append(weigh(probs, values_all, total, results[-1], head * request_group))
            continue
        results.append(
            flash(
                query_head, keys_t, values_all, counts * span, request_group,
                cache_length, head * request_group, results[-1] if results else None, queries.shape[2],
                "both", top,
            )
        )
    return results[-1]


def flash_kernel(*refs, cache_length, chunk, heads, mode):
    bias_ref, q_ref, k_ref = refs[:3]
    v_ref = refs[3] if mode not in ("top", "prob") else None
    top_ref = refs[4] if mode == "mix" else None
    o_ref = refs[-1]
    pb_ref = refs[-2] if mode == "prob" else None
    tokens = q_ref.shape[0]
    lanes = 128
    new_mask = lax.broadcasted_iota(jnp.int32, (tokens, tokens), 1) <= lax.broadcasted_iota(
        jnp.int32, (tokens, tokens), 0
    )

    def fold(acc, s, op):
        for b in range(s.shape[1] // lanes):
            acc = op(acc, s[:, b * lanes:(b + 1) * lanes])
        return acc

    for head in range(heads):
        q = q_ref[:, head * lanes:(head + 1) * lanes]

        def scores(first, size):
            return lax.dot_general(
                q, k_ref[:, first:first + size], (((1,), (0,)), ((), ())),
                preferred_element_type=jnp.float32,
            )

        def masked(first, size):
            return scores(first, size) + bias_ref[:, first:first + size]

        fresh = jnp.where(new_mask, scores(cache_length, tokens), -1e30)
        if mode == "mix":
            top = top_ref[:, head * lanes:(head + 1) * lanes]
        else:
            top = fold(jnp.full((tokens, lanes), -1e30, jnp.float32), fresh, jnp.maximum)
            for first in range(0, cache_length, chunk):
                top = fold(top, masked(first, chunk), jnp.maximum)
            top = jnp.max(top, axis=1, keepdims=True)
        if mode == "top":
            o_ref[:, head * lanes:(head + 1) * lanes] = jnp.broadcast_to(top, (tokens, lanes))
            continue

        def mix(s, first, size):
            if mode == "mix":
                p = jnp.exp(s - jnp.tile(top, (1, size // lanes)))
            else:
                p = jnp.exp(s - top)
            return p, lax.dot_general(
                p.astype(jnp.bfloat16), v_ref[first:first + size, :], (((1,), (0,)), ((), ())),
                preferred_element_type=jnp.float32,
            )

        if mode == "prob":
            p = jnp.exp(fresh - top)
            pb_ref[head, :, cache_length:cache_length + tokens] = p.astype(pb_ref.dtype)
            total = fold(jnp.zeros((tokens, lanes), jnp.float32), p, jnp.add)
            for first in range(0, cache_length, chunk):
                p = jnp.exp(masked(first, chunk) - top)
                pb_ref[head, :, first:first + chunk] = p.astype(pb_ref.dtype)
                total = fold(total, p, jnp.add)
            total = jnp.sum(total, axis=1, keepdims=True)
            o_ref[:, head * lanes:(head + 1) * lanes] = jnp.broadcast_to(total, (tokens, lanes))
            continue

        p, acc = mix(fresh, cache_length, tokens)
        total = fold(jnp.zeros((tokens, lanes), jnp.float32), p, jnp.add)
        for first in range(0, cache_length, chunk):
            p, part = mix(masked(first, chunk), first, chunk)
            total = fold(total, p, jnp.add)
            acc = acc + part
        total = jnp.sum(total, axis=1, keepdims=True)
        o_ref[:, head * lanes:(head + 1) * lanes] = (acc / total).astype(o_ref.dtype)


def weigh_kernel(p_ref, v_ref, t_ref, into_ref, o_ref):
    lanes = 128
    for head in range(p_ref.shape[0]):
        acc = lax.dot_general(
            p_ref[head], v_ref[...], (((1,), (0,)), ((), ())), preferred_element_type=jnp.float32
        )
        cols = slice(head * lanes, (head + 1) * lanes)
        o_ref[:, cols] = (acc / t_ref[:, cols]).astype(o_ref.dtype)


def weigh(probs, values_all, total, into, offset):
    rows, q_heads, tokens, length = probs.shape
    head_dim = values_all.shape[2]
    heads = HEADS
    per = q_heads // heads
    block = offset // heads
    return pl.pallas_call(
        weigh_kernel,
        grid=(rows, per),
        in_specs=[
            pl.BlockSpec((None, heads, tokens, length), lambda r, g: (r, g, 0, 0)),
            pl.BlockSpec((None, length, head_dim), lambda r, g: (r, 0, 0)),
            pl.BlockSpec((None, tokens, head_dim * heads), lambda r, g: (r, 0, g)),
            pl.BlockSpec(memory_space=pl.ANY),
        ],
        out_specs=pl.BlockSpec((None, tokens, head_dim * heads), lambda r, g: (r, 0, block + g)),
        out_shape=jax.ShapeDtypeStruct(into.shape, jnp.bfloat16),
        input_output_aliases={3: 0},
    )(probs, values_all, total, into)


CHUNK = 512
HEADS = 4


def flash(query_rot, keys_t, values_all, live, request_group, cache_length, offset, into, out_width,
          mode="both", top=None):
    rows, tokens, q_width = query_rot.shape
    head_dim, length = keys_t.shape[1:]
    kv_heads = 1
    chunk = CHUNK if cache_length % CHUNK == 0 else 128
    heads = HEADS
    bias = jnp.where(
        jnp.arange(cache_length, dtype=jnp.int32)[None, :] < live[:, None], 0.0, -1e30
    ).astype(jnp.float32)[:, None, :]
    kernel = functools.partial(
        flash_kernel, cache_length=cache_length, chunk=chunk, heads=heads, mode=mode
    )
    per = request_group // heads
    block = offset // heads
    in_specs = [
        pl.BlockSpec((None, 1, cache_length), lambda r, h, g: (r, 0, 0)),
        pl.BlockSpec((None, tokens, head_dim * heads), lambda r, h, g: (r, 0, h * per + g)),
        pl.BlockSpec((None, head_dim, length), lambda r, h, g: (r, h, 0)),
    ]
    operands = [bias, query_rot, keys_t]
    if mode not in ("top", "prob"):
        in_specs.append(pl.BlockSpec((None, length, head_dim), lambda r, h, g: (r, 0, h)))
        operands.append(values_all)
    if mode == "mix":
        in_specs.append(pl.BlockSpec((None, tokens, head_dim * heads), lambda r, h, g: (r, 0, h * per + g)))
        operands.append(top)
    aliases = {}
    if into is not None:
        in_specs.append(pl.BlockSpec(memory_space=pl.ANY))
        aliases = {len(operands): 0}
        operands.append(into)
    if mode == "prob":
        out_specs = [
            pl.BlockSpec((None, heads, tokens, length), lambda r, h, g: (r, h * per + g, 0, 0)),
            pl.BlockSpec((None, tokens, head_dim * heads), lambda r, h, g: (r, 0, h * per + g)),
        ]
        out_shape = [
            jax.ShapeDtypeStruct((rows, q_width // head_dim, tokens, length), jnp.bfloat16),
            jax.ShapeDtypeStruct((rows, tokens, q_width), jnp.float32),
        ]
    elif mode == "top":
        out_specs = pl.BlockSpec((None, tokens, head_dim * heads), lambda r, h, g: (r, 0, h * per + g))
        out_shape = jax.ShapeDtypeStruct((rows, tokens, q_width), jnp.float32)
    else:
        out_specs = pl.BlockSpec(
            (None, tokens, head_dim * heads), lambda r, h, g: (r, 0, block + h * per + g)
        )
        out_shape = jax.ShapeDtypeStruct((rows, tokens, out_width), jnp.bfloat16)
    passes = {"both": 3, "top": 1, "mix": 2, "prob": 2}[mode]
    return pl.pallas_call(
        kernel,
        grid=(rows, kv_heads, per),
        in_specs=in_specs,
        out_specs=out_specs,
        out_shape=out_shape,
        input_output_aliases=aliases,
        cost_estimate=pl.CostEstimate(
            flops=2 * passes * rows * tokens * q_width * length,
            transcendentals=rows * tokens * (q_width // head_dim) * length,
            bytes_accessed=2 * rows * (2 * tokens * q_width + 2 * length * head_dim),
        ),
    )(*operands)


def solution(mesh):
    return jax.shard_map(
        shards,
        mesh=mesh,
        in_specs=(
            P(("grp", "stretch"), None, "req"),
            P(("grp", "stretch"), None, "req"),
            P(("grp", "stretch"), None, "req"),
            P(("grp", "stretch"), None, "req"),
            P(("grp", "stretch"), None, "req"),
            P(("grp", "stretch"), None, "req"),
            P(("grp", "stretch"), None),
            P(("grp", "stretch")),
            P(("grp", "stretch"), None),
        ),
        out_specs=P(("grp", "stretch"), None, "req"),
        check_vma=False,
    )
```

```python
import functools

import jax
import jax.numpy as jnp
from jax import lax
from jax.experimental import pallas as pl
from jax.experimental.pallas import tpu as pltpu
from jax.sharding import PartitionSpec as P

rope_base = 500000.0


def apply_rotary(x, pos):
    half = x.shape[-1] // 2
    inv = rope_base ** (-(jnp.arange(half, dtype=jnp.float32) * 2.0 / x.shape[-1]))
    angle = pos.astype(jnp.float32)[..., None] * inv
    cosine = jnp.cos(angle)
    sine = jnp.sin(angle)
    first = x[..., :half]
    second = x[..., half:]
    return jnp.concatenate(
        [first * cosine - second * sine, second * cosine + first * sine], axis=-1
    )


def slot_tables(slot_stretch_ids, counts, positions, owners, capacity, per_owner):
    rows, slots = slot_stretch_ids.shape
    owner = slot_stretch_ids // per_owner
    local = slot_stretch_ids % per_owner
    slot_iota = jnp.arange(slots, dtype=jnp.int32)
    live = slot_iota[None, :] < counts[:, None]
    same = owner[:, :, None] == owner[:, None, :]
    earlier = slot_iota[:, None] < slot_iota[None, :]
    rank = jnp.sum((same & earlier[None, :, :] & live[:, :, None]).astype(jnp.int32), axis=1)
    target = owner * capacity + rank
    hits = (
        target[:, :, None] == jnp.arange(owners * capacity, dtype=jnp.int32)[None, None, :]
    ) & live[:, :, None]
    hits = hits.astype(jnp.int32)
    local_table = jnp.sum(hits * (local + 1)[:, :, None], axis=1) - 1
    place_table = jnp.sum(hits * positions[:, :, None], axis=1)
    return (
        local_table.reshape(rows, owners, capacity),
        place_table.reshape(rows, owners, capacity),
        owner,
        rank,
        live,
    )


def shards(
    queries,
    fresh_keys,
    fresh_values,
    stored_stretch_keys,
    stored_stretch_values,
    scales,
    stretch_ids,
    counts,
    stretch_pos,
):
    owners = lax.axis_size("stretch")
    rows, slots = stretch_ids.shape
    per_owner, span, width = stored_stretch_keys.shape
    kv_heads = scales.shape[2]
    head_dim = width // kv_heads
    q_heads = queries.shape[2] // head_dim
    request_group = q_heads // kv_heads
    tokens = queries.shape[1]
    capacity = 2 * slots // owners
    cache_length = slots * span
    mine = slot_tables(stretch_ids, counts, stretch_pos, owners, capacity, per_owner)
    owner, rank, live = (mine[2], mine[3], mine[4])
    scale_code = (scales.astype(jnp.float32) * 65536.0).astype(jnp.int32).reshape(1, 1, -1)
    requests = jnp.concatenate(
        [
            jnp.transpose(mine[0], (1, 0, 2)),
            jnp.broadcast_to(scale_code, (owners, rows, scale_code.shape[2])),
        ],
        axis=2,
    )
    answers = lax.all_to_all(requests, "stretch", split_axis=0, concat_axis=0, tiled=True)
    wanted = answers[:, :, :capacity]
    chosen = jnp.maximum(wanted, 0)
    all_scales = (answers[:, 0, capacity:].astype(jnp.float32) * (1.0 / 65536.0)).reshape(
        owners * per_owner, 2, scales.shape[2]
    )
    store = jnp.stack(
        [
            jnp.concatenate(
                [
                    stored_stretch_keys[..., h * head_dim:(h + 1) * head_dim],
                    stored_stretch_values[..., h * head_dim:(h + 1) * head_dim],
                ],
                axis=-1,
            )
            for h in range(kv_heads)
        ],
        axis=0,
    )
    flat = owners * rows * capacity
    index = (owner * rows + jnp.arange(rows, dtype=jnp.int32)[:, None]) * capacity + rank
    index = jnp.where(live, index, 0)
    slot_scale = all_scales[stretch_ids]
    placement = stretch_pos[:, :, None] + jnp.arange(span, dtype=jnp.int32)
    token_positions = cache_length + jnp.arange(tokens, dtype=jnp.int32)
    query_rot = (
        apply_rotary(
            queries.reshape(rows, tokens, q_heads, head_dim).astype(jnp.float32),
            token_positions[:, None],
        )
        * head_dim ** (-0.5)
    ).astype(jnp.bfloat16)
    query_rot = query_rot.reshape(rows, tokens, q_heads * head_dim)
    results = []
    for head in range(kv_heads):
        cols = slice(head * head_dim, (head + 1) * head_dim)
        last = head == kv_heads - 1
        new_keys = apply_rotary(
            fresh_keys[..., cols].astype(jnp.float32), token_positions
        ).astype(jnp.bfloat16)
        group_cols = slice(head * request_group * head_dim, (head + 1) * request_group * head_dim)
        query_head = query_rot[..., group_cols]
        if last:
            got_keys = lax.all_to_all(
                store[head][chosen][..., :head_dim], "stretch", split_axis=0, concat_axis=0, tiled=True
            )
            if results:
                got_keys, earlier = lax.optimization_barrier((got_keys, results[-1]))
                results[-1] = earlier
            send_vals = store[head][chosen][..., head_dim:]
            if results:
                send_vals, earlier = lax.optimization_barrier((send_vals, results[-1]))
                results[-1] = earlier
            got_vals = lax.all_to_all(send_vals, "stretch", split_axis=0, concat_axis=0, tiled=True)
            raw_k = got_keys.reshape(flat, span, head_dim)[index]
        else:
            got = lax.all_to_all(store[head][chosen], "stretch", split_axis=0, concat_axis=0, tiled=True)
            if results:
                got, earlier = lax.optimization_barrier((got, results[-1]))
                results[-1] = earlier
            got = got.reshape(flat, span, 2 * head_dim)[index]
            raw_k = got[..., :head_dim]
        keys = raw_k.astype(jnp.float32) * slot_scale[:, :, 0, head][:, :, None, None]
        keys = apply_rotary(keys, placement).astype(jnp.bfloat16)
        keys_t = jnp.swapaxes(
            jnp.concatenate([keys.reshape(rows, cache_length, head_dim), new_keys], axis=1), 1, 2
        )
        top = None
        if last:
            probs, total = flash(
                query_head, keys_t, None, counts * span, request_group, cache_length, 0, None, 0, "prob"
            )
            got_vals, probs, total = lax.optimization_barrier((got_vals, probs, total))
            raw_v = got_vals.reshape(flat, span, head_dim)[index]
        else:
            raw_v = got[..., head_dim:]
        vals = raw_v.astype(jnp.float32) * slot_scale[:, :, 1, head][:, :, None, None]
        vals = vals.astype(jnp.bfloat16)
        values_all = jnp.concatenate(
            [vals.reshape(rows, cache_length, head_dim), fresh_values[..., cols]], axis=1
        )
        if last and results:
            results.append(weigh(probs, values_all, total, results[-1], head * request_group))
            continue
        results.append(
            flash(
                query_head, keys_t, values_all, counts * span, request_group,
                cache_length, head * request_group, results[-1] if results else None, queries.shape[2],
                "both", top,
            )
        )
    return results[-1]


def flash_kernel(*refs, cache_length, chunk, heads, mode):
    bias_ref, q_ref, k_ref = refs[:3]
    v_ref = refs[3] if mode not in ("top", "prob") else None
    top_ref = refs[4] if mode == "mix" else None
    o_ref = refs[-1]
    pb_ref = refs[-2] if mode == "prob" else None
    tokens = q_ref.shape[0]
    lanes = 128
    new_mask = lax.broadcasted_iota(jnp.int32, (tokens, tokens), 1) <= lax.broadcasted_iota(
        jnp.int32, (tokens, tokens), 0
    )

    def fold(acc, s, op):
        for b in range(s.shape[1] // lanes):
            acc = op(acc, s[:, b * lanes:(b + 1) * lanes])
        return acc

    for head in range(heads):
        q = q_ref[:, head * lanes:(head + 1) * lanes]

        def scores(first, size):
            return lax.dot_general(
                q, k_ref[:, first:first + size], (((1,), (0,)), ((), ())),
                preferred_element_type=jnp.float32,
            )

        def masked(first, size):
            return scores(first, size) + bias_ref[:, first:first + size]

        fresh = jnp.where(new_mask, scores(cache_length, tokens), -1e30)
        if mode == "mix":
            top = top_ref[:, head * lanes:(head + 1) * lanes]
        else:
            top = fold(jnp.full((tokens, lanes), -1e30, jnp.float32), fresh, jnp.maximum)
            for first in range(0, cache_length, chunk):
                top = fold(top, masked(first, chunk), jnp.maximum)
            top = jnp.max(top, axis=1, keepdims=True)
        if mode == "top":
            o_ref[:, head * lanes:(head + 1) * lanes] = jnp.broadcast_to(top, (tokens, lanes))
            continue

        def mix(s, first, size):
            if mode == "mix":
                p = jnp.exp(s - jnp.tile(top, (1, size // lanes)))
            else:
                p = jnp.exp(s - top)
            return p, lax.dot_general(
                p.astype(jnp.bfloat16), v_ref[first:first + size, :], (((1,), (0,)), ((), ())),
                preferred_element_type=jnp.float32,
            )

        if mode == "prob":
            p = jnp.exp(fresh - top)
            pb_ref[head, :, cache_length:cache_length + tokens] = p.astype(pb_ref.dtype)
            total = fold(jnp.zeros((tokens, lanes), jnp.float32), p, jnp.add)
            for first in range(0, cache_length, chunk):
                p = jnp.exp(masked(first, chunk) - top)
                pb_ref[head, :, first:first + chunk] = p.astype(pb_ref.dtype)
                total = fold(total, p, jnp.add)
            total = jnp.sum(total, axis=1, keepdims=True)
            o_ref[:, head * lanes:(head + 1) * lanes] = jnp.broadcast_to(total, (tokens, lanes))
            continue

        p, acc = mix(fresh, cache_length, tokens)
        total = fold(jnp.zeros((tokens, lanes), jnp.float32), p, jnp.add)
        for first in range(0, cache_length, chunk):
            p, part = mix(masked(first, chunk), first, chunk)
            total = fold(total, p, jnp.add)
            acc = acc + part
        total = jnp.sum(total, axis=1, keepdims=True)
        o_ref[:, head * lanes:(head + 1) * lanes] = (acc / total).astype(o_ref.dtype)


def weigh_kernel(p_ref, v_ref, t_ref, into_ref, o_ref):
    lanes = 128
    for head in range(p_ref.shape[0]):
        acc = lax.dot_general(
            p_ref[head], v_ref[...], (((1,), (0,)), ((), ())), preferred_element_type=jnp.float32
        )
        cols = slice(head * lanes, (head + 1) * lanes)
        o_ref[:, cols] = (acc / t_ref[:, cols]).astype(o_ref.dtype)


def weigh(probs, values_all, total, into, offset):
    rows, q_heads, tokens, length = probs.shape
    head_dim = values_all.shape[2]
    heads = HEADS
    per = q_heads // heads
    block = offset // heads
    return pl.pallas_call(
        weigh_kernel,
        grid=(rows, per),
        in_specs=[
            pl.BlockSpec((None, heads, tokens, length), lambda r, g: (r, g, 0, 0)),
            pl.BlockSpec((None, length, head_dim), lambda r, g: (r, 0, 0)),
            pl.BlockSpec((None, tokens, head_dim * heads), lambda r, g: (r, 0, g)),
            pl.BlockSpec(memory_space=pl.ANY),
        ],
        out_specs=pl.BlockSpec((None, tokens, head_dim * heads), lambda r, g: (r, 0, block + g)),
        out_shape=jax.ShapeDtypeStruct(into.shape, jnp.bfloat16),
        input_output_aliases={3: 0},
    )(probs, values_all, total, into)


CHUNK = 512
HEADS = 4


def flash(query_rot, keys_t, values_all, live, request_group, cache_length, offset, into, out_width,
          mode="both", top=None):
    rows, tokens, q_width = query_rot.shape
    head_dim, length = keys_t.shape[1:]
    kv_heads = 1
    chunk = CHUNK if cache_length % CHUNK == 0 else 128
    heads = HEADS
    bias = jnp.where(
        jnp.arange(cache_length, dtype=jnp.int32)[None, :] < live[:, None], 0.0, -1e30
    ).astype(jnp.float32)[:, None, :]
    kernel = functools.partial(
        flash_kernel, cache_length=cache_length, chunk=chunk, heads=heads, mode=mode
    )
    per = request_group // heads
    block = offset // heads
    in_specs = [
        pl.BlockSpec((None, 1, cache_length), lambda r, h, g: (r, 0, 0)),
        pl.BlockSpec((None, tokens, head_dim * heads), lambda r, h, g: (r, 0, h * per + g)),
        pl.BlockSpec((None, head_dim, length), lambda r, h, g: (r, h, 0)),
    ]
    operands = [bias, query_rot, keys_t]
    if mode not in ("top", "prob"):
        in_specs.append(pl.BlockSpec((None, length, head_dim), lambda r, h, g: (r, 0, h)))
        operands.append(values_all)
    if mode == "mix":
        in_specs.append(pl.BlockSpec((None, tokens, head_dim * heads), lambda r, h, g: (r, 0, h * per + g)))
        operands.append(top)
    aliases = {}
    if into is not None:
        in_specs.append(pl.BlockSpec(memory_space=pl.ANY))
        aliases = {len(operands): 0}
        operands.append(into)
    if mode == "prob":
        out_specs = [
            pl.BlockSpec((None, heads, tokens, length), lambda r, h, g: (r, h * per + g, 0, 0)),
            pl.BlockSpec((None, tokens, head_dim * heads), lambda r, h, g: (r, 0, h * per + g)),
        ]
        out_shape = [
            jax.ShapeDtypeStruct((rows, q_width // head_dim, tokens, length), jnp.bfloat16),
            jax.ShapeDtypeStruct((rows, tokens, q_width), jnp.float32),
        ]
    elif mode == "top":
        out_specs = pl.BlockSpec((None, tokens, head_dim * heads), lambda r, h, g: (r, 0, h * per + g))
        out_shape = jax.ShapeDtypeStruct((rows, tokens, q_width), jnp.float32)
    else:
        out_specs = pl.BlockSpec(
            (None, tokens, head_dim * heads), lambda r, h, g: (r, 0, block + h * per + g)
        )
        out_shape = jax.ShapeDtypeStruct((rows, tokens, out_width), jnp.bfloat16)
    passes = {"both": 3, "top": 1, "mix": 2, "prob": 2}[mode]
    return pl.pallas_call(
        kernel,
        grid=(rows, kv_heads, per),
        in_specs=in_specs,
        out_specs=out_specs,
        out_shape=out_shape,
        input_output_aliases=aliases,
        cost_estimate=pl.CostEstimate(
            flops=2 * passes * rows * tokens * q_width * length,
            transcendentals=rows * tokens * (q_width // head_dim) * length,
            bytes_accessed=2 * rows * (2 * tokens * q_width + 2 * length * head_dim),
        ),
    )(*operands)


def solution(mesh):
    return jax.shard_map(
        shards,
        mesh=mesh,
        in_specs=(
            P(("grp", "stretch"), None, "req"),
            P(("grp", "stretch"), None, "req"),
            P(("grp", "stretch"), None, "req"),
            P(("grp", "stretch"), None, "req"),
            P(("grp", "stretch"), None, "req"),
            P(("grp", "stretch"), None, "req"),
            P(("grp", "stretch"), None),
            P(("grp", "stretch")),
            P(("grp", "stretch"), None),
        ),
        out_specs=P(("grp", "stretch"), None, "req"),
        check_vma=False,
    )
```

```python
import functools

import jax
import jax.numpy as jnp
from jax import lax
from jax.experimental import pallas as pl
from jax.experimental.pallas import tpu as pltpu
from jax.sharding import PartitionSpec as P

rope_base = 500000.0


def apply_rotary(x, pos):
    half = x.shape[-1] // 2
    inv = rope_base ** (-(jnp.arange(half, dtype=jnp.float32) * 2.0 / x.shape[-1]))
    angle = pos.astype(jnp.float32)[..., None] * inv
    cosine = jnp.cos(angle)
    sine = jnp.sin(angle)
    first = x[..., :half]
    second = x[..., half:]
    return jnp.concatenate(
        [first * cosine - second * sine, second * cosine + first * sine], axis=-1
    )


def slot_tables(slot_stretch_ids, counts, positions, owners, capacity, per_owner):
    rows, slots = slot_stretch_ids.shape
    owner = slot_stretch_ids // per_owner
    local = slot_stretch_ids % per_owner
    slot_iota = jnp.arange(slots, dtype=jnp.int32)
    live = slot_iota[None, :] < counts[:, None]
    same = owner[:, :, None] == owner[:, None, :]
    earlier = slot_iota[:, None] < slot_iota[None, :]
    rank = jnp.sum((same & earlier[None, :, :] & live[:, :, None]).astype(jnp.int32), axis=1)
    target = owner * capacity + rank
    hits = (
        target[:, :, None] == jnp.arange(owners * capacity, dtype=jnp.int32)[None, None, :]
    ) & live[:, :, None]
    hits = hits.astype(jnp.int32)
    local_table = jnp.sum(hits * (local + 1)[:, :, None], axis=1) - 1
    place_table = jnp.sum(hits * positions[:, :, None], axis=1)
    return (
        local_table.reshape(rows, owners, capacity),
        place_table.reshape(rows, owners, capacity),
        owner,
        rank,
        live,
    )


def shards(
    queries,
    fresh_keys,
    fresh_values,
    stored_stretch_keys,
    stored_stretch_values,
    scales,
    stretch_ids,
    counts,
    stretch_pos,
):
    owners = lax.axis_size("stretch")
    rows, slots = stretch_ids.shape
    per_owner, span, width = stored_stretch_keys.shape
    kv_heads = scales.shape[2]
    head_dim = width // kv_heads
    q_heads = queries.shape[2] // head_dim
    request_group = q_heads // kv_heads
    tokens = queries.shape[1]
    capacity = 2 * slots // owners
    cache_length = slots * span
    mine = slot_tables(stretch_ids, counts, stretch_pos, owners, capacity, per_owner)
    owner, rank, live = (mine[2], mine[3], mine[4])
    scale_code = (scales.astype(jnp.float32) * 65536.0).astype(jnp.int32).reshape(1, 1, -1)
    requests = jnp.concatenate(
        [
            jnp.transpose(mine[0], (1, 0, 2)),
            jnp.broadcast_to(scale_code, (owners, rows, scale_code.shape[2])),
        ],
        axis=2,
    )
    answers = lax.all_to_all(requests, "stretch", split_axis=0, concat_axis=0, tiled=True)
    wanted = answers[:, :, :capacity]
    chosen = jnp.maximum(wanted, 0)
    all_scales = (answers[:, 0, capacity:].astype(jnp.float32) * (1.0 / 65536.0)).reshape(
        owners * per_owner, 2, scales.shape[2]
    )
    store = jnp.stack(
        [
            jnp.concatenate(
                [
                    stored_stretch_keys[..., h * head_dim:(h + 1) * head_dim],
                    stored_stretch_values[..., h * head_dim:(h + 1) * head_dim],
                ],
                axis=-1,
            )
            for h in range(kv_heads)
        ],
        axis=0,
    )
    flat = owners * rows * capacity
    index = (owner * rows + jnp.arange(rows, dtype=jnp.int32)[:, None]) * capacity + rank
    index = jnp.where(live, index, 0)
    slot_scale = all_scales[stretch_ids]
    placement = stretch_pos[:, :, None] + jnp.arange(span, dtype=jnp.int32)
    token_positions = cache_length + jnp.arange(tokens, dtype=jnp.int32)
    query_rot = (
        apply_rotary(
            queries.reshape(rows, tokens, q_heads, head_dim).astype(jnp.float32),
            token_positions[:, None],
        )
        * head_dim ** (-0.5)
    ).astype(jnp.bfloat16)
    query_rot = query_rot.reshape(rows, tokens, q_heads * head_dim)
    results = []
    for head in range(kv_heads):
        cols = slice(head * head_dim, (head + 1) * head_dim)
        last = head == kv_heads - 1
        new_keys = apply_rotary(
            fresh_keys[..., cols].astype(jnp.float32), token_positions
        ).astype(jnp.bfloat16)
        group_cols = slice(head * request_group * head_dim, (head + 1) * request_group * head_dim)
        query_head = query_rot[..., group_cols]
        if last:
            got_keys = lax.all_to_all(
                store[head][chosen][..., :head_dim], "stretch", split_axis=0, concat_axis=0, tiled=True
            )
            if results:
                got_keys, earlier = lax.optimization_barrier((got_keys, results[-1]))
                results[-1] = earlier
            send_vals = store[head][chosen][..., head_dim:]
            if results:
                send_vals, earlier = lax.optimization_barrier((send_vals, results[-1]))
                results[-1] = earlier
            got_vals = lax.all_to_all(send_vals, "stretch", split_axis=0, concat_axis=0, tiled=True)
            raw_k = got_keys.reshape(flat, span, head_dim)[index]
        else:
            got = lax.all_to_all(store[head][chosen], "stretch", split_axis=0, concat_axis=0, tiled=True)
            if results:
                got, earlier = lax.optimization_barrier((got, results[-1]))
                results[-1] = earlier
            got = got.reshape(flat, span, 2 * head_dim)[index]
            raw_k = got[..., :head_dim]
        keys = raw_k.astype(jnp.float32) * slot_scale[:, :, 0, head][:, :, None, None]
        keys = apply_rotary(keys, placement).astype(jnp.bfloat16)
        keys_t = jnp.swapaxes(
            jnp.concatenate([keys.reshape(rows, cache_length, head_dim), new_keys], axis=1), 1, 2
        )
        top = None
        if last:
            probs, total = flash(
                query_head, keys_t, None, counts * span, request_group, cache_length, 0, None, 0, "prob"
            )
            got_vals, probs, total = lax.optimization_barrier((got_vals, probs, total))
            raw_v = got_vals.reshape(flat, span, head_dim)[index]
        else:
            raw_v = got[..., head_dim:]
        vals = raw_v.astype(jnp.float32) * slot_scale[:, :, 1, head][:, :, None, None]
        vals = vals.astype(jnp.bfloat16)
        values_all = jnp.concatenate(
            [vals.reshape(rows, cache_length, head_dim), fresh_values[..., cols]], axis=1
        )
        if last and results:
            results.append(weigh(probs, values_all, total, results[-1], head * request_group))
            continue
        results.append(
            flash(
                query_head, keys_t, values_all, counts * span, request_group,
                cache_length, head * request_group, results[-1] if results else None, queries.shape[2],
                "both", top,
            )
        )
    return results[-1]


def flash_kernel(*refs, cache_length, chunk, heads, mode):
    bias_ref, q_ref, k_ref = refs[:3]
    v_ref = refs[3] if mode not in ("top", "prob") else None
    top_ref = refs[4] if mode == "mix" else None
    o_ref = refs[-1]
    pb_ref = refs[-2] if mode == "prob" else None
    tokens = q_ref.shape[0]
    lanes = 128
    new_mask = lax.broadcasted_iota(jnp.int32, (tokens, tokens), 1) <= lax.broadcasted_iota(
        jnp.int32, (tokens, tokens), 0
    )

    def fold(acc, s, op):
        for b in range(s.shape[1] // lanes):
            acc = op(acc, s[:, b * lanes:(b + 1) * lanes])
        return acc

    for head in range(heads):
        q = q_ref[:, head * lanes:(head + 1) * lanes]

        def scores(first, size):
            return lax.dot_general(
                q, k_ref[:, first:first + size], (((1,), (0,)), ((), ())),
                preferred_element_type=jnp.float32,
            )

        def masked(first, size):
            return scores(first, size) + bias_ref[:, first:first + size]

        fresh = jnp.where(new_mask, scores(cache_length, tokens), -1e30)
        if mode == "mix":
            top = top_ref[:, head * lanes:(head + 1) * lanes]
        else:
            top = fold(jnp.full((tokens, lanes), -1e30, jnp.float32), fresh, jnp.maximum)
            for first in range(0, cache_length, chunk):
                top = fold(top, masked(first, chunk), jnp.maximum)
            top = jnp.max(top, axis=1, keepdims=True)
        if mode == "top":
            o_ref[:, head * lanes:(head + 1) * lanes] = jnp.broadcast_to(top, (tokens, lanes))
            continue

        def mix(s, first, size):
            if mode == "mix":
                p = jnp.exp(s - jnp.tile(top, (1, size // lanes)))
            else:
                p = jnp.exp(s - top)
            return p, lax.dot_general(
                p.astype(jnp.bfloat16), v_ref[first:first + size, :], (((1,), (0,)), ((), ())),
                preferred_element_type=jnp.float32,
            )

        if mode == "prob":
            p = jnp.exp(fresh - top)
            pb_ref[head, :, cache_length:cache_length + tokens] = p.astype(pb_ref.dtype)
            total = fold(jnp.zeros((tokens, lanes), jnp.float32), p, jnp.add)
            for first in range(0, cache_length, chunk):
                p = jnp.exp(masked(first, chunk) - top)
                pb_ref[head, :, first:first + chunk] = p.astype(pb_ref.dtype)
                total = fold(total, p, jnp.add)
            total = jnp.sum(total, axis=1, keepdims=True)
            o_ref[:, head * lanes:(head + 1) * lanes] = jnp.broadcast_to(total, (tokens, lanes))
            continue

        p, acc = mix(fresh, cache_length, tokens)
        total = fold(jnp.zeros((tokens, lanes), jnp.float32), p, jnp.add)
        for first in range(0, cache_length, chunk):
            p, part = mix(masked(first, chunk), first, chunk)
            total = fold(total, p, jnp.add)
            acc = acc + part
        total = jnp.sum(total, axis=1, keepdims=True)
        o_ref[:, head * lanes:(head + 1) * lanes] = (acc / total).astype(o_ref.dtype)


def weigh_kernel(p_ref, v_ref, t_ref, into_ref, o_ref):
    lanes = 128
    for head in range(p_ref.shape[0]):
        acc = lax.dot_general(
            p_ref[head], v_ref[...], (((1,), (0,)), ((), ())), preferred_element_type=jnp.float32
        )
        cols = slice(head * lanes, (head + 1) * lanes)
        o_ref[:, cols] = (acc / t_ref[:, cols]).astype(o_ref.dtype)


def weigh(probs, values_all, total, into, offset):
    rows, q_heads, tokens, length = probs.shape
    head_dim = values_all.shape[2]
    heads = 1
    per = q_heads // heads
    block = offset // heads
    return pl.pallas_call(
        weigh_kernel,
        grid=(rows, per),
        in_specs=[
            pl.BlockSpec((None, heads, tokens, length), lambda r, g: (r, g, 0, 0)),
            pl.BlockSpec((None, length, head_dim), lambda r, g: (r, 0, 0)),
            pl.BlockSpec((None, tokens, head_dim * heads), lambda r, g: (r, 0, g)),
            pl.BlockSpec(memory_space=pl.ANY),
        ],
        out_specs=pl.BlockSpec((None, tokens, head_dim * heads), lambda r, g: (r, 0, block + g)),
        out_shape=jax.ShapeDtypeStruct(into.shape, jnp.bfloat16),
        input_output_aliases={3: 0},
    )(probs, values_all, total, into)


CHUNK = 512
HEADS = 4


def flash(query_rot, keys_t, values_all, live, request_group, cache_length, offset, into, out_width,
          mode="both", top=None):
    rows, tokens, q_width = query_rot.shape
    head_dim, length = keys_t.shape[1:]
    kv_heads = 1
    chunk = CHUNK if cache_length % CHUNK == 0 else 128
    heads = HEADS
    bias = jnp.where(
        jnp.arange(cache_length, dtype=jnp.int32)[None, :] < live[:, None], 0.0, -1e30
    ).astype(jnp.float32)[:, None, :]
    kernel = functools.partial(
        flash_kernel, cache_length=cache_length, chunk=chunk, heads=heads, mode=mode
    )
    per = request_group // heads
    block = offset // heads
    in_specs = [
        pl.BlockSpec((None, 1, cache_length), lambda r, h, g: (r, 0, 0)),
        pl.BlockSpec((None, tokens, head_dim * heads), lambda r, h, g: (r, 0, h * per + g)),
        pl.BlockSpec((None, head_dim, length), lambda r, h, g: (r, h, 0)),
    ]
    operands = [bias, query_rot, keys_t]
    if mode not in ("top", "prob"):
        in_specs.append(pl.BlockSpec((None, length, head_dim), lambda r, h, g: (r, 0, h)))
        operands.append(values_all)
    if mode == "mix":
        in_specs.append(pl.BlockSpec((None, tokens, head_dim * heads), lambda r, h, g: (r, 0, h * per + g)))
        operands.append(top)
    aliases = {}
    if into is not None:
        in_specs.append(pl.BlockSpec(memory_space=pl.ANY))
        aliases = {len(operands): 0}
        operands.append(into)
    if mode == "prob":
        out_specs = [
            pl.BlockSpec((None, heads, tokens, length), lambda r, h, g: (r, h * per + g, 0, 0)),
            pl.BlockSpec((None, tokens, head_dim * heads), lambda r, h, g: (r, 0, h * per + g)),
        ]
        out_shape = [
            jax.ShapeDtypeStruct((rows, q_width // head_dim, tokens, length), jnp.bfloat16),
            jax.ShapeDtypeStruct((rows, tokens, q_width), jnp.float32),
        ]
    elif mode == "top":
        out_specs = pl.BlockSpec((None, tokens, head_dim * heads), lambda r, h, g: (r, 0, h * per + g))
        out_shape = jax.ShapeDtypeStruct((rows, tokens, q_width), jnp.float32)
    else:
        out_specs = pl.BlockSpec(
            (None, tokens, head_dim * heads), lambda r, h, g: (r, 0, block + h * per + g)
        )
        out_shape = jax.ShapeDtypeStruct((rows, tokens, out_width), jnp.bfloat16)
    passes = {"both": 3, "top": 1, "mix": 2, "prob": 2}[mode]
    return pl.pallas_call(
        kernel,
        grid=(rows, kv_heads, per),
        in_specs=in_specs,
        out_specs=out_specs,
        out_shape=out_shape,
        input_output_aliases=aliases,
        cost_estimate=pl.CostEstimate(
            flops=2 * passes * rows * tokens * q_width * length,
            transcendentals=rows * tokens * (q_width // head_dim) * length,
            bytes_accessed=2 * rows * (2 * tokens * q_width + 2 * length * head_dim),
        ),
    )(*operands)


def solution(mesh):
    return jax.shard_map(
        shards,
        mesh=mesh,
        in_specs=(
            P(("grp", "stretch"), None, "req"),
            P(("grp", "stretch"), None, "req"),
            P(("grp", "stretch"), None, "req"),
            P(("grp", "stretch"), None, "req"),
            P(("grp", "stretch"), None, "req"),
            P(("grp", "stretch"), None, "req"),
            P(("grp", "stretch"), None),
            P(("grp", "stretch")),
            P(("grp", "stretch"), None),
        ),
        out_specs=P(("grp", "stretch"), None, "req"),
        check_vma=False,
    )
```

```python
import functools

import jax
import jax.numpy as jnp
from jax import lax
from jax.experimental import pallas as pl
from jax.experimental.pallas import tpu as pltpu
from jax.sharding import PartitionSpec as P

rope_base = 500000.0


def apply_rotary(x, pos):
    half = x.shape[-1] // 2
    inv = rope_base ** (-(jnp.arange(half, dtype=jnp.float32) * 2.0 / x.shape[-1]))
    angle = pos.astype(jnp.float32)[..., None] * inv
    cosine = jnp.cos(angle)
    sine = jnp.sin(angle)
    first = x[..., :half]
    second = x[..., half:]
    return jnp.concatenate(
        [first * cosine - second * sine, second * cosine + first * sine], axis=-1
    )


def slot_tables(slot_stretch_ids, counts, positions, owners, capacity, per_owner):
    rows, slots = slot_stretch_ids.shape
    owner = slot_stretch_ids // per_owner
    local = slot_stretch_ids % per_owner
    slot_iota = jnp.arange(slots, dtype=jnp.int32)
    live = slot_iota[None, :] < counts[:, None]
    same = owner[:, :, None] == owner[:, None, :]
    earlier = slot_iota[:, None] < slot_iota[None, :]
    rank = jnp.sum((same & earlier[None, :, :] & live[:, :, None]).astype(jnp.int32), axis=1)
    target = owner * capacity + rank
    hits = (
        target[:, :, None] == jnp.arange(owners * capacity, dtype=jnp.int32)[None, None, :]
    ) & live[:, :, None]
    hits = hits.astype(jnp.int32)
    local_table = jnp.sum(hits * (local + 1)[:, :, None], axis=1) - 1
    place_table = jnp.sum(hits * positions[:, :, None], axis=1)
    return (
        local_table.reshape(rows, owners, capacity),
        place_table.reshape(rows, owners, capacity),
        owner,
        rank,
        live,
    )


def shards(
    queries,
    fresh_keys,
    fresh_values,
    stored_stretch_keys,
    stored_stretch_values,
    scales,
    stretch_ids,
    counts,
    stretch_pos,
):
    owners = lax.axis_size("stretch")
    rows, slots = stretch_ids.shape
    per_owner, span, width = stored_stretch_keys.shape
    kv_heads = scales.shape[2]
    head_dim = width // kv_heads
    q_heads = queries.shape[2] // head_dim
    request_group = q_heads // kv_heads
    tokens = queries.shape[1]
    capacity = 2 * slots // owners
    cache_length = slots * span
    mine = slot_tables(stretch_ids, counts, stretch_pos, owners, capacity, per_owner)
    owner, rank, live = (mine[2], mine[3], mine[4])
    scale_code = (scales.astype(jnp.float32) * 65536.0).astype(jnp.int32).reshape(1, 1, -1)
    requests = jnp.concatenate(
        [
            jnp.transpose(mine[0], (1, 0, 2)),
            jnp.broadcast_to(scale_code, (owners, rows, scale_code.shape[2])),
        ],
        axis=2,
    )
    answers = lax.all_to_all(requests, "stretch", split_axis=0, concat_axis=0, tiled=True)
    wanted = answers[:, :, :capacity]
    chosen = jnp.maximum(wanted, 0)
    all_scales = (answers[:, 0, capacity:].astype(jnp.float32) * (1.0 / 65536.0)).reshape(
        owners * per_owner, 2, scales.shape[2]
    )
    store = jnp.stack(
        [
            jnp.concatenate(
                [
                    stored_stretch_keys[..., h * head_dim:(h + 1) * head_dim],
                    stored_stretch_values[..., h * head_dim:(h + 1) * head_dim],
                ],
                axis=-1,
            )
            for h in range(kv_heads)
        ],
        axis=0,
    )
    flat = owners * rows * capacity
    index = (owner * rows + jnp.arange(rows, dtype=jnp.int32)[:, None]) * capacity + rank
    index = jnp.where(live, index, 0)
    slot_scale = all_scales[stretch_ids]
    placement = stretch_pos[:, :, None] + jnp.arange(span, dtype=jnp.int32)
    token_positions = cache_length + jnp.arange(tokens, dtype=jnp.int32)
    query_rot = (
        apply_rotary(
            queries.reshape(rows, tokens, q_heads, head_dim).astype(jnp.float32),
            token_positions[:, None],
        )
        * head_dim ** (-0.5)
    ).astype(jnp.bfloat16)
    query_rot = query_rot.reshape(rows, tokens, q_heads * head_dim)
    results = []
    for head in range(kv_heads):
        cols = slice(head * head_dim, (head + 1) * head_dim)
        last = head == kv_heads - 1
        new_keys = apply_rotary(
            fresh_keys[..., cols].astype(jnp.float32), token_positions
        ).astype(jnp.bfloat16)
        group_cols = slice(head * request_group * head_dim, (head + 1) * request_group * head_dim)
        query_head = query_rot[..., group_cols]
        if last:
            got_keys = lax.all_to_all(
                store[head][chosen][..., :head_dim], "stretch", split_axis=0, concat_axis=0, tiled=True
            )
            if results:
                got_keys, earlier = lax.optimization_barrier((got_keys, results[-1]))
                results[-1] = earlier
            send_vals = store[head][chosen][..., head_dim:]
            if results:
                send_vals, earlier = lax.optimization_barrier((send_vals, results[-1]))
                results[-1] = earlier
            got_vals = lax.all_to_all(send_vals, "stretch", split_axis=0, concat_axis=0, tiled=True)
            raw_k = got_keys.reshape(flat, span, head_dim)[index]
        else:
            got = lax.all_to_all(store[head][chosen], "stretch", split_axis=0, concat_axis=0, tiled=True)
            if results:
                got, earlier = lax.optimization_barrier((got, results[-1]))
                results[-1] = earlier
            got = got.reshape(flat, span, 2 * head_dim)[index]
            raw_k = got[..., :head_dim]
        keys = raw_k.astype(jnp.float32) * slot_scale[:, :, 0, head][:, :, None, None]
        keys = apply_rotary(keys, placement).astype(jnp.bfloat16)
        keys_t = jnp.swapaxes(
            jnp.concatenate([keys.reshape(rows, cache_length, head_dim), new_keys], axis=1), 1, 2
        )
        top = None
        if last:
            probs, total = flash(
                query_head, keys_t, None, counts * span, request_group, cache_length, 0, None, 0, "prob"
            )
            got_vals, probs, total = lax.optimization_barrier((got_vals, probs, total))
            raw_v = got_vals.reshape(flat, span, head_dim)[index]
        else:
            raw_v = got[..., head_dim:]
        vals = raw_v.astype(jnp.float32) * slot_scale[:, :, 1, head][:, :, None, None]
        vals = vals.astype(jnp.bfloat16)
        values_all = jnp.concatenate(
            [vals.reshape(rows, cache_length, head_dim), fresh_values[..., cols]], axis=1
        )
        if last and results:
            results.append(weigh(probs, values_all, total, results[-1], head * request_group))
            continue
        results.append(
            flash(
                query_head, keys_t, values_all, counts * span, request_group,
                cache_length, head * request_group, results[-1] if results else None, queries.shape[2],
                "both", top,
            )
        )
    return results[-1]


def flash_kernel(*refs, cache_length, chunk, heads, mode):
    bias_ref, q_ref, k_ref = refs[:3]
    v_ref = refs[3] if mode not in ("top", "prob") else None
    top_ref = refs[4] if mode == "mix" else None
    o_ref = refs[-1]
    pb_ref = refs[-2] if mode == "prob" else None
    tokens = q_ref.shape[0]
    lanes = 128
    new_mask = lax.broadcasted_iota(jnp.int32, (tokens, tokens), 1) <= lax.broadcasted_iota(
        jnp.int32, (tokens, tokens), 0
    )

    def fold(acc, s, op):
        for b in range(s.shape[1] // lanes):
            acc = op(acc, s[:, b * lanes:(b + 1) * lanes])
        return acc

    for head in range(heads):
        q = q_ref[:, head * lanes:(head + 1) * lanes]

        def scores(first, size):
            return lax.dot_general(
                q, k_ref[:, first:first + size], (((1,), (0,)), ((), ())),
                preferred_element_type=jnp.float32,
            )

        def masked(first, size):
            return scores(first, size) + bias_ref[:, first:first + size]

        fresh = jnp.where(new_mask, scores(cache_length, tokens), -1e30)
        if mode == "mix":
            top = top_ref[:, head * lanes:(head + 1) * lanes]
        else:
            top = fold(jnp.full((tokens, lanes), -1e30, jnp.float32), fresh, jnp.maximum)
            for first in range(0, cache_length, chunk):
                top = fold(top, masked(first, chunk), jnp.maximum)
            top = jnp.max(top, axis=1, keepdims=True)
        if mode == "top":
            o_ref[:, head * lanes:(head + 1) * lanes] = jnp.broadcast_to(top, (tokens, lanes))
            continue

        def mix(s, first, size):
            if mode == "mix":
                p = jnp.exp(s - jnp.tile(top, (1, size // lanes)))
            else:
                p = jnp.exp(s - top)
            return p, lax.dot_general(
                p.astype(jnp.bfloat16), v_ref[first:first + size, :], (((1,), (0,)), ((), ())),
                preferred_element_type=jnp.float32,
            )

        if mode == "prob":
            p = jnp.exp(fresh - top)
            pb_ref[head, :, cache_length:cache_length + tokens] = p.astype(pb_ref.dtype)
            total = fold(jnp.zeros((tokens, lanes), jnp.float32), p, jnp.add)
            for first in range(0, cache_length, chunk):
                p = jnp.exp(masked(first, chunk) - top)
                pb_ref[head, :, first:first + chunk] = p.astype(pb_ref.dtype)
                total = fold(total, p, jnp.add)
            total = jnp.sum(total, axis=1, keepdims=True)
            o_ref[:, head * lanes:(head + 1) * lanes] = jnp.broadcast_to(total, (tokens, lanes))
            continue

        p, acc = mix(fresh, cache_length, tokens)
        total = fold(jnp.zeros((tokens, lanes), jnp.float32), p, jnp.add)
        for first in range(0, cache_length, chunk):
            p, part = mix(masked(first, chunk), first, chunk)
            total = fold(total, p, jnp.add)
            acc = acc + part
        total = jnp.sum(total, axis=1, keepdims=True)
        o_ref[:, head * lanes:(head + 1) * lanes] = (acc / total).astype(o_ref.dtype)


def weigh_kernel(p_ref, v_ref, t_ref, into_ref, o_ref):
    lanes = 128
    for head in range(p_ref.shape[0]):
        acc = lax.dot_general(
            p_ref[head], v_ref[...], (((1,), (0,)), ((), ())), preferred_element_type=jnp.float32
        )
        cols = slice(head * lanes, (head + 1) * lanes)
        o_ref[:, cols] = (acc / t_ref[:, cols]).astype(o_ref.dtype)


def weigh(probs, values_all, total, into, offset):
    rows, q_heads, tokens, length = probs.shape
    head_dim = values_all.shape[2]
    heads = 2
    per = q_heads // heads
    block = offset // heads
    return pl.pallas_call(
        weigh_kernel,
        grid=(rows, per),
        in_specs=[
            pl.BlockSpec((None, heads, tokens, length), lambda r, g: (r, g, 0, 0)),
            pl.BlockSpec((None, length, head_dim), lambda r, g: (r, 0, 0)),
            pl.BlockSpec((None, tokens, head_dim * heads), lambda r, g: (r, 0, g)),
            pl.BlockSpec(memory_space=pl.ANY),
        ],
        out_specs=pl.BlockSpec((None, tokens, head_dim * heads), lambda r, g: (r, 0, block + g)),
        out_shape=jax.ShapeDtypeStruct(into.shape, jnp.bfloat16),
        input_output_aliases={3: 0},
    )(probs, values_all, total, into)


CHUNK = 512
HEADS = 4


def flash(query_rot, keys_t, values_all, live, request_group, cache_length, offset, into, out_width,
          mode="both", top=None):
    rows, tokens, q_width = query_rot.shape
    head_dim, length = keys_t.shape[1:]
    kv_heads = 1
    chunk = CHUNK if cache_length % CHUNK == 0 else 128
    heads = HEADS
    bias = jnp.where(
        jnp.arange(cache_length, dtype=jnp.int32)[None, :] < live[:, None], 0.0, -1e30
    ).astype(jnp.float32)[:, None, :]
    kernel = functools.partial(
        flash_kernel, cache_length=cache_length, chunk=chunk, heads=heads, mode=mode
    )
    per = request_group // heads
    block = offset // heads
    in_specs = [
        pl.BlockSpec((None, 1, cache_length), lambda r, h, g: (r, 0, 0)),
        pl.BlockSpec((None, tokens, head_dim * heads), lambda r, h, g: (r, 0, h * per + g)),
        pl.BlockSpec((None, head_dim, length), lambda r, h, g: (r, h, 0)),
    ]
    operands = [bias, query_rot, keys_t]
    if mode not in ("top", "prob"):
        in_specs.append(pl.BlockSpec((None, length, head_dim), lambda r, h, g: (r, 0, h)))
        operands.append(values_all)
    if mode == "mix":
        in_specs.append(pl.BlockSpec((None, tokens, head_dim * heads), lambda r, h, g: (r, 0, h * per + g)))
        operands.append(top)
    aliases = {}
    if into is not None:
        in_specs.append(pl.BlockSpec(memory_space=pl.ANY))
        aliases = {len(operands): 0}
        operands.append(into)
    if mode == "prob":
        out_specs = [
            pl.BlockSpec((None, heads, tokens, length), lambda r, h, g: (r, h * per + g, 0, 0)),
            pl.BlockSpec((None, tokens, head_dim * heads), lambda r, h, g: (r, 0, h * per + g)),
        ]
        out_shape = [
            jax.ShapeDtypeStruct((rows, q_width // head_dim, tokens, length), jnp.bfloat16),
            jax.ShapeDtypeStruct((rows, tokens, q_width), jnp.float32),
        ]
    elif mode == "top":
        out_specs = pl.BlockSpec((None, tokens, head_dim * heads), lambda r, h, g: (r, 0, h * per + g))
        out_shape = jax.ShapeDtypeStruct((rows, tokens, q_width), jnp.float32)
    else:
        out_specs = pl.BlockSpec(
            (None, tokens, head_dim * heads), lambda r, h, g: (r, 0, block + h * per + g)
        )
        out_shape = jax.ShapeDtypeStruct((rows, tokens, out_width), jnp.bfloat16)
    passes = {"both": 3, "top": 1, "mix": 2, "prob": 2}[mode]
    return pl.pallas_call(
        kernel,
        grid=(rows, kv_heads, per),
        in_specs=in_specs,
        out_specs=out_specs,
        out_shape=out_shape,
        input_output_aliases=aliases,
        cost_estimate=pl.CostEstimate(
            flops=2 * passes * rows * tokens * q_width * length,
            transcendentals=rows * tokens * (q_width // head_dim) * length,
            bytes_accessed=2 * rows * (2 * tokens * q_width + 2 * length * head_dim),
        ),
    )(*operands)


def solution(mesh):
    return jax.shard_map(
        shards,
        mesh=mesh,
        in_specs=(
            P(("grp", "stretch"), None, "req"),
            P(("grp", "stretch"), None, "req"),
            P(("grp", "stretch"), None, "req"),
            P(("grp", "stretch"), None, "req"),
            P(("grp", "stretch"), None, "req"),
            P(("grp", "stretch"), None, "req"),
            P(("grp", "stretch"), None),
            P(("grp", "stretch")),
            P(("grp", "stretch"), None),
        ),
        out_specs=P(("grp", "stretch"), None, "req"),
        check_vma=False,
    )
```

```python
import functools

import jax
import jax.numpy as jnp
from jax import lax
from jax.experimental import pallas as pl
from jax.experimental.pallas import tpu as pltpu
from jax.sharding import PartitionSpec as P

rope_base = 500000.0


def apply_rotary(x, pos):
    half = x.shape[-1] // 2
    inv = rope_base ** (-(jnp.arange(half, dtype=jnp.float32) * 2.0 / x.shape[-1]))
    angle = pos.astype(jnp.float32)[..., None] * inv
    cosine = jnp.cos(angle)
    sine = jnp.sin(angle)
    first = x[..., :half]
    second = x[..., half:]
    return jnp.concatenate(
        [first * cosine - second * sine, second * cosine + first * sine], axis=-1
    )


def slot_tables(slot_stretch_ids, counts, positions, owners, capacity, per_owner):
    rows, slots = slot_stretch_ids.shape
    owner = slot_stretch_ids // per_owner
    local = slot_stretch_ids % per_owner
    slot_iota = jnp.arange(slots, dtype=jnp.int32)
    live = slot_iota[None, :] < counts[:, None]
    same = owner[:, :, None] == owner[:, None, :]
    earlier = slot_iota[:, None] < slot_iota[None, :]
    rank = jnp.sum((same & earlier[None, :, :] & live[:, :, None]).astype(jnp.int32), axis=1)
    target = owner * capacity + rank
    hits = (
        target[:, :, None] == jnp.arange(owners * capacity, dtype=jnp.int32)[None, None, :]
    ) & live[:, :, None]
    hits = hits.astype(jnp.int32)
    local_table = jnp.sum(hits * (local + 1)[:, :, None], axis=1) - 1
    place_table = jnp.sum(hits * positions[:, :, None], axis=1)
    return (
        local_table.reshape(rows, owners, capacity),
        place_table.reshape(rows, owners, capacity),
        owner,
        rank,
        live,
    )


def shards(
    queries,
    fresh_keys,
    fresh_values,
    stored_stretch_keys,
    stored_stretch_values,
    scales,
    stretch_ids,
    counts,
    stretch_pos,
):
    owners = lax.axis_size("stretch")
    rows, slots = stretch_ids.shape
    per_owner, span, width = stored_stretch_keys.shape
    kv_heads = scales.shape[2]
    head_dim = width // kv_heads
    q_heads = queries.shape[2] // head_dim
    request_group = q_heads // kv_heads
    tokens = queries.shape[1]
    capacity = 2 * slots // owners
    cache_length = slots * span
    mine = slot_tables(stretch_ids, counts, stretch_pos, owners, capacity, per_owner)
    owner, rank, live = (mine[2], mine[3], mine[4])
    scale_code = (scales.astype(jnp.float32) * 65536.0).astype(jnp.int32).reshape(1, 1, -1)
    requests = jnp.concatenate(
        [
            jnp.transpose(mine[0], (1, 0, 2)),
            jnp.broadcast_to(scale_code, (owners, rows, scale_code.shape[2])),
        ],
        axis=2,
    )
    answers = lax.all_to_all(requests, "stretch", split_axis=0, concat_axis=0, tiled=True)
    wanted = answers[:, :, :capacity]
    chosen = jnp.maximum(wanted, 0)
    all_scales = (answers[:, 0, capacity:].astype(jnp.float32) * (1.0 / 65536.0)).reshape(
        owners * per_owner, 2, scales.shape[2]
    )
    store = jnp.stack(
        [
            jnp.concatenate(
                [
                    stored_stretch_keys[..., h * head_dim:(h + 1) * head_dim],
                    stored_stretch_values[..., h * head_dim:(h + 1) * head_dim],
                ],
                axis=-1,
            )
            for h in range(kv_heads)
        ],
        axis=0,
    )
    flat = owners * rows * capacity
    index = (owner * rows + jnp.arange(rows, dtype=jnp.int32)[:, None]) * capacity + rank
    index = jnp.where(live, index, 0)
    slot_scale = all_scales[stretch_ids]
    placement = stretch_pos[:, :, None] + jnp.arange(span, dtype=jnp.int32)
    token_positions = cache_length + jnp.arange(tokens, dtype=jnp.int32)
    query_rot = (
        apply_rotary(
            queries.reshape(rows, tokens, q_heads, head_dim).astype(jnp.float32),
            token_positions[:, None],
        )
        * head_dim ** (-0.5)
    ).astype(jnp.bfloat16)
    query_rot = query_rot.reshape(rows, tokens, q_heads * head_dim)
    results = []
    for head in range(kv_heads):
        cols = slice(head * head_dim, (head + 1) * head_dim)
        last = head == kv_heads - 1
        new_keys = apply_rotary(
            fresh_keys[..., cols].astype(jnp.float32), token_positions
        ).astype(jnp.bfloat16)
        group_cols = slice(head * request_group * head_dim, (head + 1) * request_group * head_dim)
        query_head = query_rot[..., group_cols]
        if last:
            got_keys = lax.all_to_all(
                store[head][chosen][..., :head_dim], "stretch", split_axis=0, concat_axis=0, tiled=True
            )
            if results:
                got_keys, earlier = lax.optimization_barrier((got_keys, results[-1]))
                results[-1] = earlier
            send_vals = store[head][chosen][..., head_dim:]
            if results:
                send_vals, earlier = lax.optimization_barrier((send_vals, results[-1]))
                results[-1] = earlier
            got_vals = lax.all_to_all(send_vals, "stretch", split_axis=0, concat_axis=0, tiled=True)
            raw_k = got_keys.reshape(flat, span, head_dim)[index]
        else:
            got = lax.all_to_all(store[head][chosen], "stretch", split_axis=0, concat_axis=0, tiled=True)
            if results:
                got, earlier = lax.optimization_barrier((got, results[-1]))
                results[-1] = earlier
            got = got.reshape(flat, span, 2 * head_dim)[index]
            raw_k = got[..., :head_dim]
        keys = raw_k.astype(jnp.float32) * slot_scale[:, :, 0, head][:, :, None, None]
        keys = apply_rotary(keys, placement).astype(jnp.bfloat16)
        keys_t = jnp.swapaxes(
            jnp.concatenate([keys.reshape(rows, cache_length, head_dim), new_keys], axis=1), 1, 2
        )
        top = None
        if last:
            probs, total = flash(
                query_head, keys_t, None, counts * span, request_group, cache_length, 0, None, 0, "prob"
            )
            got_vals, probs, total = lax.optimization_barrier((got_vals, probs, total))
            raw_v = got_vals.reshape(flat, span, head_dim)[index]
        else:
            raw_v = got[..., head_dim:]
        vals = raw_v.astype(jnp.float32) * slot_scale[:, :, 1, head][:, :, None, None]
        vals = vals.astype(jnp.bfloat16)
        if last and results:
            results.append(weigh(
                probs, vals.reshape(rows, cache_length, head_dim), fresh_values[..., cols],
                total, results[-1], head * request_group,
            ))
            continue
        values_all = jnp.concatenate(
            [vals.reshape(rows, cache_length, head_dim), fresh_values[..., cols]], axis=1
        )
        results.append(
            flash(
                query_head, keys_t, values_all, counts * span, request_group,
                cache_length, head * request_group, results[-1] if results else None, queries.shape[2],
                "both", top,
            )
        )
    return results[-1]


def flash_kernel(*refs, cache_length, chunk, heads, mode):
    bias_ref, q_ref, k_ref = refs[:3]
    v_ref = refs[3] if mode not in ("top", "prob") else None
    top_ref = refs[4] if mode == "mix" else None
    o_ref = refs[-1]
    pb_ref = refs[-2] if mode == "prob" else None
    tokens = q_ref.shape[0]
    lanes = 128
    new_mask = lax.broadcasted_iota(jnp.int32, (tokens, tokens), 1) <= lax.broadcasted_iota(
        jnp.int32, (tokens, tokens), 0
    )

    def fold(acc, s, op):
        for b in range(s.shape[1] // lanes):
            acc = op(acc, s[:, b * lanes:(b + 1) * lanes])
        return acc

    for head in range(heads):
        q = q_ref[:, head * lanes:(head + 1) * lanes]

        def scores(first, size):
            return lax.dot_general(
                q, k_ref[:, first:first + size], (((1,), (0,)), ((), ())),
                preferred_element_type=jnp.float32,
            )

        def masked(first, size):
            return scores(first, size) + bias_ref[:, first:first + size]

        fresh = jnp.where(new_mask, scores(cache_length, tokens), -1e30)
        if mode == "mix":
            top = top_ref[:, head * lanes:(head + 1) * lanes]
        else:
            top = fold(jnp.full((tokens, lanes), -1e30, jnp.float32), fresh, jnp.maximum)
            for first in range(0, cache_length, chunk):
                top = fold(top, masked(first, chunk), jnp.maximum)
            top = jnp.max(top, axis=1, keepdims=True)
        if mode == "top":
            o_ref[:, head * lanes:(head + 1) * lanes] = jnp.broadcast_to(top, (tokens, lanes))
            continue

        def mix(s, first, size):
            if mode == "mix":
                p = jnp.exp(s - jnp.tile(top, (1, size // lanes)))
            else:
                p = jnp.exp(s - top)
            return p, lax.dot_general(
                p.astype(jnp.bfloat16), v_ref[first:first + size, :], (((1,), (0,)), ((), ())),
                preferred_element_type=jnp.float32,
            )

        if mode == "prob":
            p = jnp.exp(fresh - top)
            pb_ref[head, :, cache_length:cache_length + tokens] = p.astype(pb_ref.dtype)
            total = fold(jnp.zeros((tokens, lanes), jnp.float32), p, jnp.add)
            for first in range(0, cache_length, chunk):
                p = jnp.exp(masked(first, chunk) - top)
                pb_ref[head, :, first:first + chunk] = p.astype(pb_ref.dtype)
                total = fold(total, p, jnp.add)
            total = jnp.sum(total, axis=1, keepdims=True)
            o_ref[:, head * lanes:(head + 1) * lanes] = jnp.broadcast_to(total, (tokens, lanes))
            continue

        p, acc = mix(fresh, cache_length, tokens)
        total = fold(jnp.zeros((tokens, lanes), jnp.float32), p, jnp.add)
        for first in range(0, cache_length, chunk):
            p, part = mix(masked(first, chunk), first, chunk)
            total = fold(total, p, jnp.add)
            acc = acc + part
        total = jnp.sum(total, axis=1, keepdims=True)
        o_ref[:, head * lanes:(head + 1) * lanes] = (acc / total).astype(o_ref.dtype)


def weigh_kernel(p_ref, v_ref, f_ref, t_ref, into_ref, o_ref):
    lanes = 128
    cache_length = v_ref.shape[0]
    for head in range(p_ref.shape[0]):
        acc = lax.dot_general(
            p_ref[head, :, :cache_length], v_ref[...], (((1,), (0,)), ((), ())),
            preferred_element_type=jnp.float32,
        ) + lax.dot_general(
            p_ref[head, :, cache_length:], f_ref[...], (((1,), (0,)), ((), ())),
            preferred_element_type=jnp.float32,
        )
        cols = slice(head * lanes, (head + 1) * lanes)
        o_ref[:, cols] = (acc / t_ref[:, cols]).astype(o_ref.dtype)


def weigh(probs, cached_values, new_values, total, into, offset):
    rows, q_heads, tokens, length = probs.shape
    cache_length, head_dim = cached_values.shape[1:]
    heads = HEADS
    per = q_heads // heads
    block = offset // heads
    return pl.pallas_call(
        weigh_kernel,
        grid=(rows, per),
        in_specs=[
            pl.BlockSpec((None, heads, tokens, length), lambda r, g: (r, g, 0, 0)),
            pl.BlockSpec((None, cache_length, head_dim), lambda r, g: (r, 0, 0)),
            pl.BlockSpec((None, tokens, head_dim), lambda r, g: (r, 0, 0)),
            pl.BlockSpec((None, tokens, head_dim * heads), lambda r, g: (r, 0, g)),
            pl.BlockSpec(memory_space=pl.ANY),
        ],
        out_specs=pl.BlockSpec((None, tokens, head_dim * heads), lambda r, g: (r, 0, block + g)),
        out_shape=jax.ShapeDtypeStruct(into.shape, jnp.bfloat16),
        input_output_aliases={4: 0},
    )(probs, cached_values, new_values, total, into)


CHUNK = 512
HEADS = 4


def flash(query_rot, keys_t, values_all, live, request_group, cache_length, offset, into, out_width,
          mode="both", top=None):
    rows, tokens, q_width = query_rot.shape
    head_dim, length = keys_t.shape[1:]
    kv_heads = 1
    chunk = CHUNK if cache_length % CHUNK == 0 else 128
    heads = HEADS
    bias = jnp.where(
        jnp.arange(cache_length, dtype=jnp.int32)[None, :] < live[:, None], 0.0, -1e30
    ).astype(jnp.float32)[:, None, :]
    kernel = functools.partial(
        flash_kernel, cache_length=cache_length, chunk=chunk, heads=heads, mode=mode
    )
    per = request_group // heads
    block = offset // heads
    in_specs = [
        pl.BlockSpec((None, 1, cache_length), lambda r, h, g: (r, 0, 0)),
        pl.BlockSpec((None, tokens, head_dim * heads), lambda r, h, g: (r, 0, h * per + g)),
        pl.BlockSpec((None, head_dim, length), lambda r, h, g: (r, h, 0)),
    ]
    operands = [bias, query_rot, keys_t]
    if mode not in ("top", "prob"):
        in_specs.append(pl.BlockSpec((None, length, head_dim), lambda r, h, g: (r, 0, h)))
        operands.append(values_all)
    if mode == "mix":
        in_specs.append(pl.BlockSpec((None, tokens, head_dim * heads), lambda r, h, g: (r, 0, h * per + g)))
        operands.append(top)
    aliases = {}
    if into is not None:
        in_specs.append(pl.BlockSpec(memory_space=pl.ANY))
        aliases = {len(operands): 0}
        operands.append(into)
    if mode == "prob":
        out_specs = [
            pl.BlockSpec((None, heads, tokens, length), lambda r, h, g: (r, h * per + g, 0, 0)),
            pl.BlockSpec((None, tokens, head_dim * heads), lambda r, h, g: (r, 0, h * per + g)),
        ]
        out_shape = [
            jax.ShapeDtypeStruct((rows, q_width // head_dim, tokens, length), jnp.bfloat16),
            jax.ShapeDtypeStruct((rows, tokens, q_width), jnp.float32),
        ]
    elif mode == "top":
        out_specs = pl.BlockSpec((None, tokens, head_dim * heads), lambda r, h, g: (r, 0, h * per + g))
        out_shape = jax.ShapeDtypeStruct((rows, tokens, q_width), jnp.float32)
    else:
        out_specs = pl.BlockSpec(
            (None, tokens, head_dim * heads), lambda r, h, g: (r, 0, block + h * per + g)
        )
        out_shape = jax.ShapeDtypeStruct((rows, tokens, out_width), jnp.bfloat16)
    passes = {"both": 3, "top": 1, "mix": 2, "prob": 2}[mode]
    return pl.pallas_call(
        kernel,
        grid=(rows, kv_heads, per),
        in_specs=in_specs,
        out_specs=out_specs,
        out_shape=out_shape,
        input_output_aliases=aliases,
        cost_estimate=pl.CostEstimate(
            flops=2 * passes * rows * tokens * q_width * length,
            transcendentals=rows * tokens * (q_width // head_dim) * length,
            bytes_accessed=2 * rows * (2 * tokens * q_width + 2 * length * head_dim),
        ),
    )(*operands)


def solution(mesh):
    return jax.shard_map(
        shards,
        mesh=mesh,
        in_specs=(
            P(("grp", "stretch"), None, "req"),
            P(("grp", "stretch"), None, "req"),
            P(("grp", "stretch"), None, "req"),
            P(("grp", "stretch"), None, "req"),
            P(("grp", "stretch"), None, "req"),
            P(("grp", "stretch"), None, "req"),
            P(("grp", "stretch"), None),
            P(("grp", "stretch")),
            P(("grp", "stretch"), None),
        ),
        out_specs=P(("grp", "stretch"), None, "req"),
        check_vma=False,
    )
```
